32 devices in a mesh: roll: 16 (over z, x, core), side: 2 (over y).
Axes of the slice: x: 2, y: 2, z: 4, core: 2. Of those that a mesh axis runs over, the one named last changes fastest.
Arguments:
- pressure: float32 [2048, 512], P('roll', 'side'), may hold values from -6 to 6
- source: float32 [2048, 512], P('roll', 'side'), may hold values from -6 to 6
- side_coupling: float32 [2048, 512], P('roll', 'side'), may hold values from 0.4 to 0.8
- block_inverse: float32 [2048, 256], P('roll', 'side'), may hold values from -1 to 1
- lower_coupling: float32 [16, 512], P('roll', 'side'), may hold values from 0.5 to 30
- cavity_mask: int32 [16, 512], P('roll', 'side'), may hold values 0 or 1
- rough_code: int32 [2048, 512], P('roll', 'side'), may hold values from 0 to 15
- film_offset: float32 [1], replicated, may hold values from 0.5 to 1.5
Outputs:
- new_pressure: float32 [2048, 512], P('roll', 'side')
- film: float32 [2048, 512], P('roll', 'side')
The draws below stay inside these ranges and needn't reach their ends.
All inputs are finite; a program needn't handle non-finite values. No bound on the sum of `cavity_mask` on one device may be relied on, other than what follows from the above.
Results may differ from the reference program's by a relative error of at most 0.00018.
Values sent between devices are 32-bit elements; how exact they have to be, the bound alone decides.
No kernel may reach another device: no remote copies, remote signals or barrier semaphores. Data moves between devices by JAX's collectives and lax.ppermute only.
A program may use at most 64 MiB of HBM per device.

```python
import math
import jax
import jax.numpy as jnp
from jax import lax

SECTION = 128
COLUMNS = 256
SWEEPS = 4
SECTIONS = 16
GRID_X = 2048
GRID_Y = 512
FFT_X = 4096
FFT_Y = 1024
N_ROLL = 16
N_SIDE = 2


def corner_table(key):
    return 0.05 * jax.random.uniform(jax.random.fold_in(key, 7), (N_ROLL, N_SIDE), jnp.float32, 0.8, 1.2)


def draw_block_inverse(key, part):
    mesh_dimensions = (GRID_X, SECTION * N_SIDE)
    row_index = jnp.arange(GRID_X, dtype=jnp.int32)[:, None]
    column_index = jnp.arange(SECTION * N_SIDE, dtype=jnp.int32)[None, :]
    inner_row = row_index % SECTION
    inner_col = column_index % SECTION
    spread = jax.random.truncated_normal(jax.random.fold_in(key, 11), -4.0, 4.0, mesh_dimensions, jnp.float32) * (0.3 / math.sqrt(SECTION))
    diagonal = jax.random.uniform(jax.random.fold_in(key, 12), mesh_dimensions, jnp.float32, 0.5, 1.0)
    values = jnp.where(inner_row == inner_col, diagonal, spread)
    values = jnp.where(inner_col == 0, 0.05 * values, values)
    values = jnp.where(inner_row == SECTION - 1, 0.05 * values, values)
    corners = corner_table(key)[row_index // SECTION, column_index // SECTION]
    return jnp.where((inner_row == SECTION - 1) & (inner_col == 0), corners, values)


def draw_lower_coupling(key, part):
    mesh_dimensions = (N_ROLL, GRID_Y)
    segment_index = jnp.arange(N_ROLL, dtype=jnp.int32)[:, None]
    column_index = jnp.arange(GRID_Y, dtype=jnp.int32)[None, :]
    slow_share = 0.5
    sluggish_marker = jax.random.uniform(jax.random.fold_in(key, 21), (1, GRID_Y), jnp.float32) < slow_share
    sluggish_speed = jnp.exp(jax.random.uniform(jax.random.fold_in(key, 22), mesh_dimensions, jnp.float32, math.log(0.15), math.log(0.6))) * (2.3 / N_ROLL)
    quick_speed = jax.random.uniform(jax.random.fold_in(key, 23), mesh_dimensions, jnp.float32, 1.0, 3.0)
    placement_slots = jax.random.randint(jax.random.fold_in(key, 24), (2, GRID_Y), 0, N_ROLL)
    surge_marker = (segment_index == placement_slots[0:1]) | (segment_index == placement_slots[1:2])
    surge_penalty = jax.random.uniform(jax.random.fold_in(key, 25), mesh_dimensions, jnp.float32, 0.5, 0.8)
    retain_fraction = jnp.where(sluggish_marker, jnp.exp(-sluggish_speed) * jnp.where(surge_marker, surge_penalty, 1.0), jnp.exp(-quick_speed))
    corners = corner_table(key)[segment_index, column_index // COLUMNS]
    return retain_fraction / corners


def draw_source(key, part):
    mesh_dimensions = (GRID_X, GRID_Y)
    return jax.random.truncated_normal(jax.random.fold_in(key, 31), -6.0, 6.0, mesh_dimensions, jnp.float32)


def touch_ends(values, key, least, high):
    longest = values.shape.index(max(values.shape))
    spots = []
    for shift in (0, 1):
        where = [jax.random.randint(jax.random.fold_in(key, axis), (), 0, length) for axis, length in enumerate(values.shape)]
        where[longest] = (where[longest] + shift) % values.shape[longest]
        spots.append(tuple(where))
    return values.at[spots[0]].set(least).at[spots[1]].set(high)


def level_of(stream_key, extent, pieces, least, top_value):
    level, own = 1.0, jax.random.fold_in(stream_key, 6)
    for axis_at, parts in pieces:
        draws = jnp.exp(jax.random.uniform(jax.random.fold_in(own, axis_at), (parts,), jnp.float32, least / len(pieces), top_value / len(pieces)))
        level = level * jnp.repeat(draws, extent[axis_at] // parts).reshape([-1 if axis == axis_at else 1 for axis in range(len(extent))])
    return level


def bell_draw(own_key, extent, width, bound, pieces=(), kind=jnp.bfloat16):
    values = width * jax.random.normal(own_key, extent, jnp.float32)
    if pieces:
        values = values * level_of(own_key, extent, pieces, -0.22, 0.18)
    return jnp.clip(values, -bound, bound).astype(kind)


def setup_inputs(seed: int = 0) -> dict:
    streams_of = jax.random.split(jax.random.key(seed), 9)
    pressure = bell_draw(streams_of[0], (GRID_X, GRID_Y), 1.0, 6.0, ((0, 16), (1, 2)), jnp.float32)
    source = draw_source(jax.random.fold_in(streams_of[8], 71), 0)
    side_coupling = jnp.clip(jnp.exp(math.log(0.8) - 0.6931472 * jax.random.uniform(streams_of[2], (GRID_X, GRID_Y), jnp.float32) ** level_of(streams_of[2], (GRID_X, GRID_Y), ((0, 16), (1, 2)), -0.2, 0.2)), 0.4, 0.8)
    block_inverse = draw_block_inverse(jax.random.fold_in(streams_of[8], 71), 0)
    lower_coupling = draw_lower_coupling(jax.random.fold_in(streams_of[8], 71), 0)
    cavity_mask = touch_ends((jax.random.randint(streams_of[5], (SECTIONS, GRID_Y), 0, 2) < 1).astype(jnp.int32), jax.random.fold_in(streams_of[5], 1), 0, 1)
    rough_code = touch_ends(jax.random.randint(streams_of[6], (GRID_X, GRID_Y), 0, 16), jax.random.fold_in(streams_of[6], 1), 0, 15).astype(jnp.int32)
    film_offset = jnp.clip(jax.random.uniform(streams_of[7], (1,), jnp.float32, 0.5, 1.5), 0.5, 1.5)
    return dict(pressure=pressure, source=source, side_coupling=side_coupling, block_inverse=block_inverse, lower_coupling=lower_coupling, cavity_mask=cavity_mask, rough_code=rough_code, film_offset=film_offset)


HIGHEST = lax.Precision.HIGHEST
ROUGH_STEP = 0.05

def relax_sweep(pressure_now, source, side_coupling, inverses, lower_blocks, mask_on):
    padded = jnp.pad(pressure_now, ((0, 0), (1, 1)))
    right_side = source + side_coupling * (padded[:, :-2] + padded[:, 2:])
    blocks = right_side.reshape(N_ROLL, SECTION, N_SIDE, COLUMNS)
    line_local = jnp.einsum('kism,kmsc->kisc', inverses, blocks, precision=HIGHEST)
    gain_rows = inverses[:, SECTION - 1, :, 0][:, :, None] * lower_blocks

    def advance(carry_in, inputs):
        outflow, gain_value = inputs
        return (outflow + gain_value * carry_in, carry_in)
    start_carry = jnp.zeros((N_SIDE, COLUMNS), jnp.float32)
    final_carry, carries = lax.scan(advance, start_carry, (line_local[:, SECTION - 1], gain_rows))
    solved = line_local + inverses[:, :, :, 0][..., None] * (lower_blocks * carries)[:, None]
    solved = jnp.where(mask_on, jnp.maximum(solved, 0.0), solved)
    return solved.reshape(GRID_X, GRID_Y)

def elastic_deflection(pressure_now):
    row_freq = jnp.arange(FFT_X, dtype=jnp.int32)
    col_freq = jnp.arange(FFT_Y // 2 + 1, dtype=jnp.int32)
    row_wave = jnp.minimum(row_freq, FFT_X - row_freq).astype(jnp.float32) / FFT_X
    col_wave = col_freq.astype(jnp.float32) / FFT_Y
    kernel_reach = min(FFT_X, FFT_Y) / 16.0
    radius = jnp.sqrt(row_wave[:, None] * row_wave[:, None] + col_wave[None, :] * col_wave[None, :])
    kernel = 0.4 * kernel_reach / (1.0 + kernel_reach * radius)
    spectrum = jnp.fft.rfft2(pressure_now, s=(FFT_X, FFT_Y))
    return jnp.fft.irfft2(spectrum * kernel, s=(FFT_X, FFT_Y))[:GRID_X, :GRID_Y]

def reference(pressure, source, side_coupling, block_inverse, lower_coupling, cavity_mask, rough_code, film_offset):
    inverses = block_inverse.reshape(N_ROLL, SECTION, N_SIDE, SECTION)
    lower_blocks = lower_coupling.reshape(N_ROLL, N_SIDE, COLUMNS)
    mask_on = (cavity_mask == 1).reshape(N_ROLL, 1, N_SIDE, COLUMNS)
    pressure_now = pressure
    for sweep_step in range(SWEEPS):
        pressure_now = relax_sweep(pressure_now, source, side_coupling, inverses, lower_blocks, mask_on)
    deflection = elastic_deflection(pressure_now)
    across = 4.0 * (jnp.arange(GRID_X).astype(jnp.float32) + 0.5) / GRID_X - 2.5
    transverse = 4.0 * (jnp.arange(GRID_Y).astype(jnp.float32) + 0.5) / GRID_Y - 2.0
    film_height = film_offset[0] + 0.5 * across[:, None] * across[:, None] + 0.5 * transverse[None, :] * transverse[None, :] + deflection - ROUGH_STEP * rough_code.astype(jnp.float32)
    return (pressure_now, film_height)
```

```python
import math

import jax
import jax.numpy as jnp
from jax import lax
from jax.sharding import PartitionSpec as P

SWEEPS = 4


HIGHEST = lax.Precision.HIGHEST
TWO_PI = 2.0 * math.pi
ROUGH_STEP = 0.05


def counting(length):
    return jnp.arange(length, dtype=jnp.int32)


def phase_pair(first_ints, second_ints, length, sign_value):
    angles = (first_ints * second_ints % length).astype(jnp.float32) * (TWO_PI / length)
    return (jnp.cos(angles), sign_value * jnp.sin(angles))


def mm(formula, left, right):
    return jnp.einsum(formula, left, right, precision=HIGHEST, preferred_element_type=jnp.float32)


def cmm(formula, left_re, left_im, right_re, right_im):
    real_part = mm(formula, left_re, right_re) - mm(formula, left_im, right_im)
    imag_part = mm(formula, left_re, right_im) + mm(formula, left_im, right_re)
    return (real_part, imag_part)


def halo_pack(cells, sl, block_inverse, lower_coupling, mask_f):
    width = sl.stop - sl.start
    top = jnp.concatenate(
        [cells[0][:, sl], cells[1][:, sl], cells[2][:, sl], block_inverse], axis=1
    )
    extra = jnp.concatenate([lower_coupling[:, sl], mask_f[:, sl]], axis=1)
    extra = jnp.pad(extra, ((0, 0), (0, top.shape[1] - 2 * width)))
    return jnp.concatenate([top, extra], axis=0)


def relax(pressure, source, side_coupling, block_inverse, lower_coupling, cavity_mask):
    row_count, col_count = pressure.shape
    roll_count = lax.axis_size("roll")
    side_count = lax.axis_size("side")
    roll_place = lax.axis_index("roll")
    halo = SWEEPS
    mask_f = (cavity_mask == 1).astype(jnp.float32)
    cells = (pressure, source, side_coupling)
    to_right = [(i, i + 1) for i in range(side_count - 1)]
    to_left = [(i + 1, i) for i in range(side_count - 1)]
    from_left = lax.ppermute(
        halo_pack(cells, slice(col_count - halo, col_count), block_inverse, lower_coupling, mask_f),
        "side",
        to_right,
    )
    from_right = lax.ppermute(
        halo_pack(cells, slice(0, halo), block_inverse, lower_coupling, mask_f), "side", to_left
    )

    def unpack(got):
        pieces = [got[:row_count, n * halo:(n + 1) * halo] for n in range(3)]
        inverse = got[:row_count, 3 * halo:]
        return pieces, inverse, got[row_count, 0:halo], got[row_count, halo:2 * halo]

    left_cells, left_inv, left_lc, left_mask = unpack(from_left)
    right_cells, right_inv, right_lc, right_mask = unpack(from_right)
    ext = [
        jnp.concatenate([left_cells[n], cells[n], right_cells[n]], axis=1) for n in range(3)
    ]
    pressure_now, source_ext, coupling_ext = ext
    lower_ext = jnp.concatenate([left_lc, lower_coupling[0], right_lc])
    mask_on = jnp.concatenate([left_mask, mask_f[0], right_mask]) > 0.5
    gain_ext = jnp.concatenate(
        [
            left_inv[row_count - 1, 0] * left_lc,
            block_inverse[row_count - 1, 0] * lower_coupling[0],
            right_inv[row_count - 1, 0] * right_lc,
        ]
    )
    first_ext = jnp.concatenate(
        [
            jnp.broadcast_to(left_inv[:, 0:1], (row_count, halo)),
            jnp.broadcast_to(block_inverse[:, 0:1], (row_count, col_count)),
            jnp.broadcast_to(right_inv[:, 0:1], (row_count, halo)),
        ],
        axis=1,
    )
    width = col_count + 2 * halo
    zero_col = jnp.zeros((row_count, 1), jnp.float32)
    gains = None
    for sweep_step in range(SWEEPS):
        left_of = jnp.concatenate([zero_col, pressure_now[:, :-1]], axis=1)
        right_of = jnp.concatenate([pressure_now[:, 1:], zero_col], axis=1)
        right_side = source_ext + coupling_ext * (left_of + right_of)
        line_local = jnp.concatenate(
            [
                mm("im,mc->ic", left_inv, right_side[:, :halo]),
                mm("im,mc->ic", block_inverse, right_side[:, halo:halo + col_count]),
                mm("im,mc->ic", right_inv, right_side[:, halo + col_count:]),
            ],
            axis=1,
        )
        outflow = line_local[row_count - 1]
        if gains is None:
            sent = jnp.broadcast_to(jnp.stack([outflow, gain_ext])[None], (roll_count, 2, width))
            got = lax.all_to_all(sent, "roll", 0, 0, tiled=True)
            outflows = got[:, 0]
            gains = got[:, 1]
        else:
            sent = jnp.broadcast_to(outflow[None], (roll_count, width))
            outflows = lax.all_to_all(sent, "roll", 0, 0, tiled=True)
        carry = jnp.zeros((width,), jnp.float32)
        for m in range(roll_count):
            carry = jnp.where(m < roll_place, outflows[m] + gains[m] * carry, carry)
        solved = line_local + first_ext * (lower_ext * carry)[None, :]
        pressure_now = jnp.where(mask_on[None, :], jnp.maximum(solved, 0.0), solved)
    return pressure_now[:, halo:halo + col_count]


def deflection_of(pressure_now):
    row_count, col_count = pressure_now.shape
    roll_count = lax.axis_size("roll")
    side_count = lax.axis_size("side")
    side_place = lax.axis_index("side")
    devices = roll_count * side_count
    fft_rows = 2 * row_count * roll_count
    fft_cols = 2 * col_count * side_count
    half_cols = fft_cols // 2
    slots = -(-(half_cols + 1) // devices)
    all_slots = devices * slots
    col_glob = side_place * col_count + counting(col_count)
    freq = counting(all_slots)
    col_cos, col_sin = phase_pair(col_glob[:, None], freq[None, :], fft_cols, -1.0)
    part_re = mm("jv,ij->vi", col_cos, pressure_now)
    part_im = mm("jv,ij->vi", col_sin, pressure_now)
    sent = jnp.stack([part_re, part_im]).reshape(2, devices, slots, row_count)
    sent = jnp.transpose(sent, (1, 0, 2, 3))
    got = lax.all_to_all(sent, ("roll", "side"), 0, 0, tiled=True)
    got = got.reshape(roll_count, side_count, 2, slots, row_count).sum(axis=1)
    x_re = jnp.transpose(got[:, 0], (1, 0, 2))
    x_im = jnp.transpose(got[:, 1], (1, 0, 2))
    first_len = fft_rows // row_count
    place_index = counting(roll_count)
    first_index = counting(first_len)
    inner_index = counting(row_count)
    f1_re, f1_im = phase_pair(first_index[:, None], place_index[None, :], first_len, -1.0)
    a_re, a_im = cmm("ua,vab->vub", f1_re, f1_im, x_re, x_im)
    tw_re, tw_im = phase_pair(first_index[:, None], inner_index[None, :], fft_rows, -1.0)
    a_re, a_im = (a_re * tw_re - a_im * tw_im, a_re * tw_im + a_im * tw_re)
    f2_re, f2_im = phase_pair(inner_index[:, None], inner_index[None, :], row_count, -1.0)
    s_re, s_im = cmm("vub,bw->vuw", a_re, a_im, f2_re, f2_im)
    my_device = lax.axis_index("roll") * side_count + side_place
    my_freq = my_device * slots + counting(slots)
    row_freq = first_index[:, None] + first_len * inner_index[None, :]
    row_wave = jnp.minimum(row_freq, fft_rows - row_freq).astype(jnp.float32) / fft_rows
    col_wave = jnp.minimum(my_freq, fft_cols - my_freq).astype(jnp.float32) / fft_cols
    kernel_reach = min(fft_rows, fft_cols) / 16.0
    radius = jnp.sqrt(
        row_wave[None] * row_wave[None] + col_wave[:, None, None] * col_wave[:, None, None]
    )
    weight = jnp.where(
        my_freq > half_cols, 0.0, jnp.where((my_freq == 0) | (my_freq == half_cols), 1.0, 2.0)
    )
    kernel = (0.4 * kernel_reach / (1.0 + kernel_reach * radius)) * (
        weight[:, None, None] / (float(fft_rows) * float(fft_cols))
    )
    s_re = s_re * kernel
    s_im = s_im * kernel
    b_re, b_im = cmm("vuw,bw->vub", s_re, s_im, f2_re, -f2_im)
    b_re, b_im = (b_re * tw_re + b_im * tw_im, b_im * tw_re - b_re * tw_im)
    o_re, o_im = cmm("ua,vub->vab", f1_re, -f1_im, b_re, b_im)
    back = jnp.stack([o_re, o_im], axis=0)
    back = jnp.transpose(back, (2, 0, 1, 3))
    back = jnp.broadcast_to(back[:, None], (roll_count, side_count, 2, slots, row_count))
    back = back.reshape(devices, 2, slots, row_count)
    home = lax.all_to_all(back, ("roll", "side"), 0, 0, tiled=True)
    home = jnp.transpose(home, (1, 0, 2, 3)).reshape(2, all_slots, row_count)
    return mm("vi,jv->ij", home[0], col_cos) + mm("vi,jv->ij", home[1], col_sin)


def per_device(
    pressure,
    source,
    side_coupling,
    block_inverse,
    lower_coupling,
    cavity_mask,
    rough_code,
    film_offset,
):
    row_count, col_count = pressure.shape
    roll_count = lax.axis_size("roll")
    side_count = lax.axis_size("side")
    roll_place = lax.axis_index("roll")
    side_place = lax.axis_index("side")
    pressure_now = relax(pressure, source, side_coupling, block_inverse, lower_coupling, cavity_mask)
    deflection = deflection_of(pressure_now)
    row_pos = (roll_place * row_count + counting(row_count)).astype(jnp.float32)
    col_pos = (side_place * col_count + counting(col_count)).astype(jnp.float32)
    across = 4.0 * (row_pos + 0.5) / (row_count * roll_count) - 2.5
    transverse = 4.0 * (col_pos + 0.5) / (col_count * side_count) - 2.0
    film_height = (
        film_offset[0]
        + 0.5 * across[:, None] * across[:, None]
        + 0.5 * transverse[None, :] * transverse[None, :]
        + deflection
        - ROUGH_STEP * rough_code.astype(jnp.float32)
    )
    return (pressure_now, film_height)


def solution(mesh):
    return jax.shard_map(
        per_device,
        mesh=mesh,
        in_specs=(
            P("roll", "side"),
            P("roll", "side"),
            P("roll", "side"),
            P("roll", "side"),
            P("roll", "side"),
            P("roll", "side"),
            P("roll", "side"),
            P(),
        ),
        out_specs=(P("roll", "side"), P("roll", "side")),
        check_vma=False,
    )
```

```python
import math

import jax
import jax.numpy as jnp
from jax import lax
from jax.sharding import PartitionSpec as P

SWEEPS = 4


HIGHEST = lax.Precision.HIGHEST
TWO_PI = 2.0 * math.pi
ROUGH_STEP = 0.05


def counting(length):
    return jnp.arange(length, dtype=jnp.int32)


def phase_pair(first_ints, second_ints, length, sign_value):
    angles = (first_ints * second_ints % length).astype(jnp.float32) * (TWO_PI / length)
    return (jnp.cos(angles), sign_value * jnp.sin(angles))


def mm(formula, left, right):
    return jnp.einsum(formula, left, right, precision=HIGHEST, preferred_element_type=jnp.float32)


def col_tables(col_count, side_place, fft_cols, all_slots):
    split = 16 if col_count % 16 == 0 else 1
    freq = counting(all_slots)
    high = side_place * col_count + split * counting(col_count // split)
    high_re, high_im = phase_pair(high[:, None], freq[None, :], fft_cols, -1.0)
    low_re, low_im = phase_pair(counting(split)[:, None], freq[None, :], fft_cols, -1.0)
    cos_t = high_re[:, None, :] * low_re[None] - high_im[:, None, :] * low_im[None]
    sin_t = high_re[:, None, :] * low_im[None] + high_im[:, None, :] * low_re[None]
    table = jnp.stack([cos_t.reshape(col_count, all_slots), sin_t.reshape(col_count, all_slots)])
    return jnp.transpose(table, (0, 2, 1))


def complex_block(f_re, f_im):
    return jnp.stack([jnp.stack([f_re, -f_im]), jnp.stack([f_im, f_re])])


def fft_tables(row_count, col_count):
    roll_count = lax.axis_size("roll")
    side_count = lax.axis_size("side")
    side_place = lax.axis_index("side")
    devices = roll_count * side_count
    fft_rows = 2 * row_count * roll_count
    fft_cols = 2 * col_count * side_count
    half_cols = fft_cols // 2
    slots = -(-(half_cols + 1) // devices)
    all_slots = devices * slots
    first_len = fft_rows // row_count
    place_index = counting(roll_count)
    first_index = counting(first_len)
    inner_index = counting(row_count)
    col_table = col_tables(col_count, side_place, fft_cols, all_slots)
    f1_re, f1_im = phase_pair(first_index[:, None], place_index[None, :], first_len, -1.0)
    g1 = jnp.transpose(complex_block(f1_re, f1_im), (2, 0, 1, 3))
    g1_back = jnp.transpose(complex_block(f1_re, -f1_im), (0, 3, 2, 1))
    tw_re, tw_im = phase_pair(first_index[:, None], inner_index[None, :], fft_rows, -1.0)
    f2_re, f2_im = phase_pair(inner_index[:, None], inner_index[None, :], row_count, -1.0)
    g2 = jnp.transpose(complex_block(f2_re, f2_im), (1, 2, 0, 3))
    g2_back = jnp.transpose(complex_block(f2_re, -f2_im), (1, 3, 0, 2))
    my_device = lax.axis_index("roll") * side_count + side_place
    my_freq = my_device * slots + counting(slots)
    row_freq = first_index[:, None] + first_len * inner_index[None, :]
    row_wave = jnp.minimum(row_freq, fft_rows - row_freq).astype(jnp.float32) / fft_rows
    col_wave = jnp.minimum(my_freq, fft_cols - my_freq).astype(jnp.float32) / fft_cols
    kernel_reach = min(fft_rows, fft_cols) / 16.0
    radius = jnp.sqrt(
        row_wave[None] * row_wave[None] + col_wave[:, None, None] * col_wave[:, None, None]
    )
    weight = jnp.where(
        my_freq > half_cols, 0.0, jnp.where((my_freq == 0) | (my_freq == half_cols), 1.0, 2.0)
    )
    kernel = (0.4 * kernel_reach / (1.0 + kernel_reach * radius)) * (
        weight[:, None, None] / (float(fft_rows) * float(fft_cols))
    )
    return dict(
        col_table=col_table, g1=g1, g1_back=g1_back, tw_re=tw_re, tw_im=tw_im,
        g2=g2, g2_back=g2_back, kernel=kernel[:, :, None, :],
    )


def halo_pack(cells, sl, block_inverse, lower_coupling, mask_f):
    width = sl.stop - sl.start
    top = jnp.concatenate(
        [cells[0][:, sl], cells[1][:, sl], cells[2][:, sl], block_inverse], axis=1
    )
    extra = jnp.concatenate([lower_coupling[:, sl], mask_f[:, sl]], axis=1)
    extra = jnp.pad(extra, ((0, 0), (0, top.shape[1] - 2 * width)))
    return jnp.concatenate([top, extra], axis=0)


def relax(pressure, source, side_coupling, block_inverse, lower_coupling, cavity_mask):
    row_count, col_count = pressure.shape
    roll_count = lax.axis_size("roll")
    side_count = lax.axis_size("side")
    roll_place = lax.axis_index("roll")
    halo = SWEEPS
    mask_f = (cavity_mask == 1).astype(jnp.float32)
    cells = (pressure, source, side_coupling)
    to_right = [(i, i + 1) for i in range(side_count - 1)]
    to_left = [(i + 1, i) for i in range(side_count - 1)]
    from_left = lax.ppermute(
        halo_pack(cells, slice(col_count - halo, col_count), block_inverse, lower_coupling, mask_f),
        "side",
        to_right,
    )
    from_right = lax.ppermute(
        halo_pack(cells, slice(0, halo), block_inverse, lower_coupling, mask_f), "side", to_left
    )
    tables = fft_tables(row_count, col_count)
    from_left, from_right, tables = lax.optimization_barrier((from_left, from_right, tables))

    def unpack(got):
        pieces = [got[:row_count, n * halo:(n + 1) * halo] for n in range(3)]
        inverse = got[:row_count, 3 * halo:]
        return pieces, inverse, got[row_count, 0:halo], got[row_count, halo:2 * halo]

    left_cells, left_inv, left_lc, left_mask = unpack(from_left)
    right_cells, right_inv, right_lc, right_mask = unpack(from_right)
    ext = [
        jnp.concatenate([left_cells[n], cells[n], right_cells[n]], axis=1) for n in range(3)
    ]
    pressure_now, source_ext, coupling_ext = ext
    lower_ext = jnp.concatenate([left_lc, lower_coupling[0], right_lc])
    mask_on = jnp.concatenate([left_mask, mask_f[0], right_mask]) > 0.5
    gain_ext = jnp.concatenate(
        [
            left_inv[row_count - 1, 0] * left_lc,
            block_inverse[row_count - 1, 0] * lower_coupling[0],
            right_inv[row_count - 1, 0] * right_lc,
        ]
    )
    first_ext = jnp.concatenate(
        [
            jnp.broadcast_to(left_inv[:, 0:1], (row_count, halo)),
            jnp.broadcast_to(block_inverse[:, 0:1], (row_count, col_count)),
            jnp.broadcast_to(right_inv[:, 0:1], (row_count, halo)),
        ],
        axis=1,
    )
    width = col_count + 2 * halo
    zero_col = jnp.zeros((row_count, 1), jnp.float32)
    inverses = (left_inv, block_inverse, right_inv)
    bounds = ((0, halo), (halo, halo + col_count), (halo + col_count, width))
    gains = None
    for sweep_step in range(SWEEPS):
        left_of = jnp.concatenate([zero_col, pressure_now[:, :-1]], axis=1)
        right_of = jnp.concatenate([pressure_now[:, 1:], zero_col], axis=1)
        right_side = source_ext + coupling_ext * (left_of + right_of)
        outflow = jnp.concatenate(
            [
                mm("m,mc->c", inv[row_count - 1], right_side[:, lo:hi])
                for inv, (lo, hi) in zip(inverses, bounds)
            ]
        )
        if gains is None:
            sent = jnp.broadcast_to(jnp.stack([outflow, gain_ext])[None], (roll_count, 2, width))
            got = lax.all_to_all(sent, "roll", 0, 0, tiled=True)
            outflows = got[:, 0]
            gains = got[:, 1]
        else:
            sent = jnp.broadcast_to(outflow[None], (roll_count, width))
            outflows = lax.all_to_all(sent, "roll", 0, 0, tiled=True)
        line_local = jnp.concatenate(
            [
                mm("im,mc->ic", inv, right_side[:, lo:hi])
                for inv, (lo, hi) in zip(inverses, bounds)
            ],
            axis=1,
        )
        carry = jnp.zeros((width,), jnp.float32)
        for m in range(roll_count):
            carry = jnp.where(m < roll_place, outflows[m] + gains[m] * carry, carry)
        solved = line_local + first_ext * (lower_ext * carry)[None, :]
        pressure_now = jnp.where(mask_on[None, :], jnp.maximum(solved, 0.0), solved)
    return pressure_now[:, halo:halo + col_count], tables


def deflection_of(pressure_now, tables):
    row_count, col_count = pressure_now.shape
    roll_count = lax.axis_size("roll")
    side_count = lax.axis_size("side")
    devices = roll_count * side_count
    col_table = tables["col_table"]
    all_slots = col_table.shape[1]
    slots = all_slots // devices
    part = mm("rvj,ij->rvi", col_table, pressure_now)
    sent = jnp.transpose(part.reshape(2, devices, slots, row_count), (1, 0, 2, 3))
    got = lax.all_to_all(sent, ("roll", "side"), 0, 0, tiled=True)
    got = got.reshape(roll_count, side_count, 2, slots, row_count).sum(axis=1)
    spread = mm("uRra,arvb->vuRb", tables["g1"], got)
    tw_re, tw_im = tables["tw_re"], tables["tw_im"]
    a_re, a_im = spread[:, :, 0], spread[:, :, 1]
    spread = jnp.stack([a_re * tw_re - a_im * tw_im, a_re * tw_im + a_im * tw_re], axis=2)
    wave = mm("vuRb,RbSw->vuSw", spread, tables["g2"]) * tables["kernel"]
    spread = mm("vuSw,SwRb->vuRb", wave, tables["g2_back"])
    b_re, b_im = spread[:, :, 0], spread[:, :, 1]
    spread = jnp.stack([b_re * tw_re + b_im * tw_im, b_im * tw_re - b_re * tw_im], axis=2)
    back = mm("RaUS,vUSb->aRvb", tables["g1_back"], spread)
    back = jnp.broadcast_to(back[:, None], (roll_count, side_count, 2, slots, row_count))
    back = back.reshape(devices, 2, slots, row_count)
    home = lax.all_to_all(back, ("roll", "side"), 0, 0, tiled=True)
    home = jnp.transpose(home, (1, 0, 2, 3)).reshape(2, all_slots, row_count)
    return mm("rvi,rvj->ij", home, col_table)


def per_device(
    pressure,
    source,
    side_coupling,
    block_inverse,
    lower_coupling,
    cavity_mask,
    rough_code,
    film_offset,
):
    row_count, col_count = pressure.shape
    roll_count = lax.axis_size("roll")
    side_count = lax.axis_size("side")
    roll_place = lax.axis_index("roll")
    side_place = lax.axis_index("side")
    pressure_now, tables = relax(
        pressure, source, side_coupling, block_inverse, lower_coupling, cavity_mask
    )
    deflection = deflection_of(pressure_now, tables)
    row_pos = (roll_place * row_count + counting(row_count)).astype(jnp.float32)
    col_pos = (side_place * col_count + counting(col_count)).astype(jnp.float32)
    across = 4.0 * (row_pos + 0.5) / (row_count * roll_count) - 2.5
    transverse = 4.0 * (col_pos + 0.5) / (col_count * side_count) - 2.0
    film_height = (
        film_offset[0]
        + 0.5 * across[:, None] * across[:, None]
        + 0.5 * transverse[None, :] * transverse[None, :]
        + deflection
        - ROUGH_STEP * rough_code.astype(jnp.float32)
    )
    return (pressure_now, film_height)


def solution(mesh):
    return jax.shard_map(
        per_device,
        mesh=mesh,
        in_specs=(
            P("roll", "side"),
            P("roll", "side"),
            P("roll", "side"),
            P("roll", "side"),
            P("roll", "side"),
            P("roll", "side"),
            P("roll", "side"),
            P(),
        ),
        out_specs=(P("roll", "side"), P("roll", "side")),
        check_vma=False,
    )
```

```python
import math

import jax
import jax.numpy as jnp
from jax import lax
from jax.sharding import PartitionSpec as P

SWEEPS = 4


HIGHEST = lax.Precision.HIGHEST
TWO_PI = 2.0 * math.pi
ROUGH_STEP = 0.05


def counting(length):
    return jnp.arange(length, dtype=jnp.int32)


def phase_pair(first_ints, second_ints, length, sign_value):
    angles = (first_ints * second_ints % length).astype(jnp.float32) * (TWO_PI / length)
    return (jnp.cos(angles), sign_value * jnp.sin(angles))


def mm(formula, left, right, precision=HIGHEST):
    return jnp.einsum(formula, left, right, precision=precision, preferred_element_type=jnp.float32)


def fm(formula, left, right):
    return mm(formula, left, right, lax.Precision.HIGH)


def col_tables(col_count, side_place, fft_cols, all_slots):
    split = 16 if col_count % 16 == 0 else 1
    freq = counting(all_slots)
    high = side_place * col_count + split * counting(col_count // split)
    high_re, high_im = phase_pair(high[:, None], freq[None, :], fft_cols, -1.0)
    low_re, low_im = phase_pair(counting(split)[:, None], freq[None, :], fft_cols, -1.0)
    cos_t = high_re[:, None, :] * low_re[None] - high_im[:, None, :] * low_im[None]
    sin_t = high_re[:, None, :] * low_im[None] + high_im[:, None, :] * low_re[None]
    table = jnp.stack([cos_t.reshape(col_count, all_slots), sin_t.reshape(col_count, all_slots)])
    return jnp.transpose(table, (0, 2, 1))


def complex_block(f_re, f_im):
    return jnp.stack([jnp.stack([f_re, -f_im]), jnp.stack([f_im, f_re])])


def fft_tables(row_count, col_count):
    roll_count = lax.axis_size("roll")
    side_count = lax.axis_size("side")
    side_place = lax.axis_index("side")
    devices = roll_count * side_count
    fft_rows = 2 * row_count * roll_count
    fft_cols = 2 * col_count * side_count
    half_cols = fft_cols // 2
    slots = -(-(half_cols + 1) // devices)
    all_slots = devices * slots
    first_len = fft_rows // row_count
    place_index = counting(roll_count)
    first_index = counting(first_len)
    inner_index = counting(row_count)
    col_table = col_tables(col_count, side_place, fft_cols, all_slots)
    f1_re, f1_im = phase_pair(first_index[:, None], place_index[None, :], first_len, -1.0)
    g1 = jnp.transpose(complex_block(f1_re, f1_im), (2, 0, 1, 3))
    g1_back = jnp.transpose(complex_block(f1_re, -f1_im), (0, 3, 2, 1))
    tw_re, tw_im = phase_pair(first_index[:, None], inner_index[None, :], fft_rows, -1.0)
    f2_re, f2_im = phase_pair(inner_index[:, None], inner_index[None, :], row_count, -1.0)
    g2 = jnp.transpose(complex_block(f2_re, f2_im), (1, 2, 0, 3))
    g2_back = jnp.transpose(complex_block(f2_re, -f2_im), (1, 3, 0, 2))
    my_device = lax.axis_index("roll") * side_count + side_place
    my_freq = my_device * slots + counting(slots)
    row_freq = first_index[:, None] + first_len * inner_index[None, :]
    row_wave = jnp.minimum(row_freq, fft_rows - row_freq).astype(jnp.float32) / fft_rows
    col_wave = jnp.minimum(my_freq, fft_cols - my_freq).astype(jnp.float32) / fft_cols
    kernel_reach = min(fft_rows, fft_cols) / 16.0
    radius = jnp.sqrt(
        row_wave[None] * row_wave[None] + col_wave[:, None, None] * col_wave[:, None, None]
    )
    weight = jnp.where(
        my_freq > half_cols, 0.0, jnp.where((my_freq == 0) | (my_freq == half_cols), 1.0, 2.0)
    )
    kernel = (0.4 * kernel_reach / (1.0 + kernel_reach * radius)) * (
        weight[:, None, None] / (float(fft_rows) * float(fft_cols))
    )
    return dict(
        col_table=col_table, g1=g1, g1_back=g1_back, tw_re=tw_re, tw_im=tw_im,
        g2=g2, g2_back=g2_back, kernel=kernel[:, :, None, :],
    )


def neighbour_cells(edges_left, edges_right):
    side_count = lax.axis_size("side")
    side_place = lax.axis_index("side")
    if side_count == 2:
        sent = jnp.where(side_place == 0, edges_right, edges_left)
        got = lax.ppermute(sent, "side", [(0, 1), (1, 0)])
        return jnp.where(side_place == 1, got, 0.0), jnp.where(side_place == 0, got, 0.0)
    to_right = [(i, i + 1) for i in range(side_count - 1)]
    to_left = [(i + 1, i) for i in range(side_count - 1)]
    return lax.ppermute(edges_right, "side", to_right), lax.ppermute(edges_left, "side", to_left)


def relax(pressure, source, side_coupling, block_inverse, lower_coupling, cavity_mask):
    row_count, col_count = pressure.shape
    roll_count = lax.axis_size("roll")
    roll_place = lax.axis_index("roll")
    halo = SWEEPS
    mask_f = (cavity_mask == 1).astype(jnp.float32)

    def edges(sl):
        wide = lambda row: jnp.broadcast_to(row[:, sl], (row_count, halo))
        return jnp.concatenate(
            [pressure[:, sl], source[:, sl], side_coupling[:, sl], block_inverse,
             wide(lower_coupling), wide(mask_f)],
            axis=1,
        )

    got_left, got_right = neighbour_cells(
        edges(slice(0, halo)), edges(slice(col_count - halo, col_count))
    )
    tables = fft_tables(row_count, col_count)
    got_left, got_right, tables = lax.optimization_barrier((got_left, got_right, tables))
    spans = [halo, halo, halo, row_count, halo, halo]
    cuts = [sum(spans[:n]) for n in range(7)]

    def unpack(got):
        return [got[:, cuts[n]:cuts[n + 1]] for n in range(6)]

    from_left, from_right = unpack(got_left), unpack(got_right)
    from_left[4], from_left[5] = from_left[4][0:1], from_left[5][0:1]
    from_right[4], from_right[5] = from_right[4][0:1], from_right[5][0:1]
    own = (pressure, source, side_coupling, block_inverse, lower_coupling, mask_f)
    ext = [jnp.concatenate([from_left[n], own[n], from_right[n]], axis=1) for n in range(6)]
    pressure_now, source_ext, coupling_ext, inverse_cat, lower_ext, mask_ext = ext
    lower_ext = lower_ext[0]
    mask_on = mask_ext[0] > 0.5
    left_inv, right_inv = from_left[3], from_right[3]
    width = col_count + 2 * halo
    gain_ext = jnp.concatenate(
        [
            left_inv[row_count - 1, 0] * from_left[4][0],
            block_inverse[row_count - 1, 0] * lower_coupling[0],
            right_inv[row_count - 1, 0] * from_right[4][0],
        ]
    )
    first_ext = jnp.concatenate(
        [
            jnp.broadcast_to(left_inv[:, 0:1], (row_count, halo)),
            jnp.broadcast_to(block_inverse[:, 0:1], (row_count, col_count)),
            jnp.broadcast_to(right_inv[:, 0:1], (row_count, halo)),
        ],
        axis=1,
    )
    column = counting(width)
    block_masks = [
        (column < halo)[None, :],
        ((column >= halo) & (column < halo + col_count))[None, :],
        (column >= halo + col_count)[None, :],
    ]
    zero_col = jnp.zeros((row_count, 1), jnp.float32)
    gains = None
    for sweep_step in range(SWEEPS):
        left_of = jnp.concatenate([zero_col, pressure_now[:, :-1]], axis=1)
        right_of = jnp.concatenate([pressure_now[:, 1:], zero_col], axis=1)
        right_side = source_ext + coupling_ext * (left_of + right_of)
        stacked = jnp.concatenate([jnp.where(m, right_side, 0.0) for m in block_masks], axis=0)
        outflow = mm("m,mc->c", inverse_cat[row_count - 1], stacked)
        if gains is None:
            sent = jnp.broadcast_to(jnp.stack([outflow, gain_ext])[None], (roll_count, 2, width))
            got = lax.all_to_all(sent, "roll", 0, 0, tiled=True)
            outflows = got[:, 0]
            gains = got[:, 1]
        else:
            sent = jnp.broadcast_to(outflow[None], (roll_count, width))
            outflows = lax.all_to_all(sent, "roll", 0, 0, tiled=True)
        line_local = mm("im,mc->ic", inverse_cat, stacked)
        carry = jnp.zeros((width,), jnp.float32)
        for m in range(roll_count):
            carry = jnp.where(m < roll_place, outflows[m] + gains[m] * carry, carry)
        solved = line_local + first_ext * (lower_ext * carry)[None, :]
        pressure_now = jnp.where(mask_on[None, :], jnp.maximum(solved, 0.0), solved)
    return pressure_now[:, halo:halo + col_count], tables


def deflection_of(pressure_now, tables):
    row_count, col_count = pressure_now.shape
    roll_count = lax.axis_size("roll")
    side_count = lax.axis_size("side")
    devices = roll_count * side_count
    col_table = tables["col_table"]
    all_slots = col_table.shape[1]
    slots = all_slots // devices
    part = fm("rvj,ij->rvi", col_table, pressure_now)
    sent = jnp.transpose(part.reshape(2, devices, slots, row_count), (1, 0, 2, 3))
    got = lax.all_to_all(sent, ("roll", "side"), 0, 0, tiled=True)
    got = got.reshape(roll_count, side_count, 2, slots, row_count).sum(axis=1)
    spread = fm("uRra,arvb->vuRb", tables["g1"], got)
    tw_re, tw_im = tables["tw_re"], tables["tw_im"]
    a_re, a_im = spread[:, :, 0], spread[:, :, 1]
    spread = jnp.stack([a_re * tw_re - a_im * tw_im, a_re * tw_im + a_im * tw_re], axis=2)
    wave = fm("vuRb,RbSw->vuSw", spread, tables["g2"]) * tables["kernel"]
    spread = fm("vuSw,SwRb->vuRb", wave, tables["g2_back"])
    b_re, b_im = spread[:, :, 0], spread[:, :, 1]
    spread = jnp.stack([b_re * tw_re + b_im * tw_im, b_im * tw_re - b_re * tw_im], axis=2)
    back = fm("RaUS,vUSb->aRvb", tables["g1_back"], spread)
    back = jnp.broadcast_to(back[:, None], (roll_count, side_count, 2, slots, row_count))
    back = back.reshape(devices, 2, slots, row_count)
    home = lax.all_to_all(back, ("roll", "side"), 0, 0, tiled=True)
    home = jnp.transpose(home, (1, 0, 2, 3)).reshape(2, all_slots, row_count)
    return fm("rvi,rvj->ij", home, col_table)


def per_device(
    pressure,
    source,
    side_coupling,
    block_inverse,
    lower_coupling,
    cavity_mask,
    rough_code,
    film_offset,
):
    row_count, col_count = pressure.shape
    roll_count = lax.axis_size("roll")
    side_count = lax.axis_size("side")
    roll_place = lax.axis_index("roll")
    side_place = lax.axis_index("side")
    pressure_now, tables = relax(
        pressure, source, side_coupling, block_inverse, lower_coupling, cavity_mask
    )
    deflection = deflection_of(pressure_now, tables)
    row_pos = (roll_place * row_count + counting(row_count)).astype(jnp.float32)
    col_pos = (side_place * col_count + counting(col_count)).astype(jnp.float32)
    across = 4.0 * (row_pos + 0.5) / (row_count * roll_count) - 2.5
    transverse = 4.0 * (col_pos + 0.5) / (col_count * side_count) - 2.0
    film_height = (
        film_offset[0]
        + 0.5 * across[:, None] * across[:, None]
        + 0.5 * transverse[None, :] * transverse[None, :]
        + deflection
        - ROUGH_STEP * rough_code.astype(jnp.float32)
    )
    return (pressure_now, film_height)


def solution(mesh):
    return jax.shard_map(
        per_device,
        mesh=mesh,
        in_specs=(
            P("roll", "side"),
            P("roll", "side"),
            P("roll", "side"),
            P("roll", "side"),
            P("roll", "side"),
            P("roll", "side"),
            P("roll", "side"),
            P(),
        ),
        out_specs=(P("roll", "side"), P("roll", "side")),
        check_vma=False,
    )
```

```python
import math

import jax
import jax.numpy as jnp
from jax import lax
from jax.sharding import PartitionSpec as P

SWEEPS = 4


HIGHEST = lax.Precision.HIGHEST
TWO_PI = 2.0 * math.pi
ROUGH_STEP = 0.05


def counting(length):
    return jnp.arange(length, dtype=jnp.int32)


def phase_pair(first_ints, second_ints, length, sign_value):
    angles = (first_ints * second_ints % length).astype(jnp.float32) * (TWO_PI / length)
    return (jnp.cos(angles), sign_value * jnp.sin(angles))


def mm(formula, left, right, precision=HIGHEST):
    return jnp.einsum(formula, left, right, precision=precision, preferred_element_type=jnp.float32)


def fm(formula, left, right):
    return mm(formula, left, right, lax.Precision.HIGH)


def col_tables(col_count, side_place, fft_cols, all_slots):
    split = 16 if col_count % 16 == 0 else 1
    freq = counting(all_slots)
    high = side_place * col_count + split * counting(col_count // split)
    high_re, high_im = phase_pair(high[:, None], freq[None, :], fft_cols, -1.0)
    low_re, low_im = phase_pair(counting(split)[:, None], freq[None, :], fft_cols, -1.0)
    cos_t = high_re[:, None, :] * low_re[None] - high_im[:, None, :] * low_im[None]
    sin_t = high_re[:, None, :] * low_im[None] + high_im[:, None, :] * low_re[None]
    table = jnp.stack([cos_t.reshape(col_count, all_slots), sin_t.reshape(col_count, all_slots)])
    return jnp.transpose(table, (0, 2, 1))


def complex_block(f_re, f_im):
    return jnp.stack([jnp.stack([f_re, -f_im]), jnp.stack([f_im, f_re])])


def fft_tables(row_count, col_count):
    roll_count = lax.axis_size("roll")
    side_count = lax.axis_size("side")
    side_place = lax.axis_index("side")
    devices = roll_count * side_count
    fft_rows = 2 * row_count * roll_count
    fft_cols = 2 * col_count * side_count
    half_cols = fft_cols // 2
    slots = -(-(half_cols + 1) // devices)
    all_slots = devices * slots
    first_len = fft_rows // row_count
    place_index = counting(roll_count)
    first_index = counting(first_len)
    inner_index = counting(row_count)
    col_table = col_tables(col_count, side_place, fft_cols, all_slots)
    f1_re, f1_im = phase_pair(first_index[:, None], place_index[None, :], first_len, -1.0)
    g1 = jnp.transpose(complex_block(f1_re, f1_im), (2, 0, 1, 3))
    g1_back = jnp.transpose(complex_block(f1_re, -f1_im), (0, 3, 2, 1))
    g1_back = jnp.broadcast_to(g1_back[:, :, None], (2, roll_count, side_count, first_len, 2))
    tw_re, tw_im = phase_pair(first_index[:, None], inner_index[None, :], fft_rows, -1.0)
    f2_re, f2_im = phase_pair(inner_index[:, None], inner_index[None, :], row_count, -1.0)
    g2 = jnp.transpose(complex_block(f2_re, f2_im), (1, 2, 0, 3))
    g2_back = jnp.transpose(complex_block(f2_re, -f2_im), (1, 3, 0, 2))
    my_device = lax.axis_index("roll") * side_count + side_place
    my_freq = my_device * slots + counting(slots)
    row_freq = first_index[:, None] + first_len * inner_index[None, :]
    row_wave = jnp.minimum(row_freq, fft_rows - row_freq).astype(jnp.float32) / fft_rows
    col_wave = jnp.minimum(my_freq, fft_cols - my_freq).astype(jnp.float32) / fft_cols
    kernel_reach = min(fft_rows, fft_cols) / 16.0
    radius = jnp.sqrt(
        row_wave[None] * row_wave[None] + col_wave[:, None, None] * col_wave[:, None, None]
    )
    weight = jnp.where(
        my_freq > half_cols, 0.0, jnp.where((my_freq == 0) | (my_freq == half_cols), 1.0, 2.0)
    )
    kernel = (0.4 * kernel_reach / (1.0 + kernel_reach * radius)) * (
        weight[:, None, None] / (float(fft_rows) * float(fft_cols))
    )
    return dict(
        col_table=col_table, g1=g1, g1_back=g1_back, tw_re=tw_re, tw_im=tw_im,
        g2=g2, g2_back=g2_back, kernel=kernel[:, :, None, :],
    )


def neighbour_cells(edges_left, edges_right):
    side_count = lax.axis_size("side")
    side_place = lax.axis_index("side")
    if side_count == 2:
        sent = jnp.where(side_place == 0, edges_right, edges_left)
        got = lax.ppermute(sent, "side", [(0, 1), (1, 0)])
        return jnp.where(side_place == 1, got, 0.0), jnp.where(side_place == 0, got, 0.0)
    to_right = [(i, i + 1) for i in range(side_count - 1)]
    to_left = [(i + 1, i) for i in range(side_count - 1)]
    return lax.ppermute(edges_right, "side", to_right), lax.ppermute(edges_left, "side", to_left)


def relax(pressure, source, side_coupling, block_inverse, lower_coupling, cavity_mask):
    row_count, col_count = pressure.shape
    roll_count = lax.axis_size("roll")
    roll_place = lax.axis_index("roll")
    halo = SWEEPS
    mask_f = (cavity_mask == 1).astype(jnp.float32)

    def edges(sl):
        wide = lambda row: jnp.broadcast_to(row[:, sl], (row_count, halo))
        return jnp.concatenate(
            [pressure[:, sl], source[:, sl], side_coupling[:, sl], block_inverse,
             wide(lower_coupling), wide(mask_f)],
            axis=1,
        )

    got_left, got_right = neighbour_cells(
        edges(slice(0, halo)), edges(slice(col_count - halo, col_count))
    )
    tables = fft_tables(row_count, col_count)
    got_left, got_right, tables = lax.optimization_barrier((got_left, got_right, tables))
    spans = [halo, halo, halo, row_count, halo, halo]
    cuts = [sum(spans[:n]) for n in range(7)]

    def unpack(got):
        return [got[:, cuts[n]:cuts[n + 1]] for n in range(6)]

    from_left, from_right = unpack(got_left), unpack(got_right)
    from_left[4], from_left[5] = from_left[4][0:1], from_left[5][0:1]
    from_right[4], from_right[5] = from_right[4][0:1], from_right[5][0:1]
    own = (pressure, source, side_coupling, block_inverse, lower_coupling, mask_f)
    ext = [jnp.concatenate([from_left[n], own[n], from_right[n]], axis=1) for n in range(6)]
    pressure_now, source_ext, coupling_ext, inverse_cat, lower_ext, mask_ext = ext
    lower_ext = lower_ext[0]
    mask_on = mask_ext[0] > 0.5
    left_inv, right_inv = from_left[3], from_right[3]
    width = col_count + 2 * halo
    gain_ext = jnp.concatenate(
        [
            left_inv[row_count - 1, 0] * from_left[4][0],
            block_inverse[row_count - 1, 0] * lower_coupling[0],
            right_inv[row_count - 1, 0] * from_right[4][0],
        ]
    )
    first_ext = jnp.concatenate(
        [
            jnp.broadcast_to(left_inv[:, 0:1], (row_count, halo)),
            jnp.broadcast_to(block_inverse[:, 0:1], (row_count, col_count)),
            jnp.broadcast_to(right_inv[:, 0:1], (row_count, halo)),
        ],
        axis=1,
    )
    column = counting(width)
    block_masks = [
        (column < halo)[None, :],
        ((column >= halo) & (column < halo + col_count))[None, :],
        (column >= halo + col_count)[None, :],
    ]
    zero_col = jnp.zeros((row_count, 1), jnp.float32)
    last_rows = jnp.broadcast_to(inverse_cat[row_count - 1][None], (roll_count, 3 * row_count))
    gains = None
    for sweep_step in range(SWEEPS):
        left_of = jnp.concatenate([zero_col, pressure_now[:, :-1]], axis=1)
        right_of = jnp.concatenate([pressure_now[:, 1:], zero_col], axis=1)
        right_side = source_ext + coupling_ext * (left_of + right_of)
        stacked = jnp.concatenate([jnp.where(m, right_side, 0.0) for m in block_masks], axis=0)
        sent = mm("km,mc->kc", last_rows, stacked)
        if gains is None:
            sent = jnp.stack([sent, jnp.broadcast_to(gain_ext[None], sent.shape)], axis=1)
            got = lax.all_to_all(sent, "roll", 0, 0, tiled=True)
            outflows = got[:, 0]
            gains = got[:, 1]
        else:
            outflows = lax.all_to_all(sent, "roll", 0, 0, tiled=True)
        line_local = mm("im,mc->ic", inverse_cat, stacked)
        carry = jnp.zeros((width,), jnp.float32)
        for m in range(roll_count):
            carry = jnp.where(m < roll_place, outflows[m] + gains[m] * carry, carry)
        solved = line_local + first_ext * (lower_ext * carry)[None, :]
        pressure_now = jnp.where(mask_on[None, :], jnp.maximum(solved, 0.0), solved)
    return pressure_now[:, halo:halo + col_count], tables


def deflection_of(pressure_now, tables):
    row_count, col_count = pressure_now.shape
    roll_count = lax.axis_size("roll")
    side_count = lax.axis_size("side")
    devices = roll_count * side_count
    col_table = tables["col_table"]
    all_slots = col_table.shape[1]
    slots = all_slots // devices
    part = fm("rvj,ij->rvi", col_table, pressure_now)
    sent = jnp.transpose(part.reshape(2, devices, slots, row_count), (1, 0, 2, 3))
    got = lax.all_to_all(sent, ("roll", "side"), 0, 0, tiled=True)
    got = got.reshape(roll_count, side_count, 2, slots, row_count).sum(axis=1)
    spread = fm("uRra,arvb->vuRb", tables["g1"], got)
    tw_re, tw_im = tables["tw_re"], tables["tw_im"]
    a_re, a_im = spread[:, :, 0], spread[:, :, 1]
    spread = jnp.stack([a_re * tw_re - a_im * tw_im, a_re * tw_im + a_im * tw_re], axis=2)
    wave = fm("vuRb,RbSw->vuSw", spread, tables["g2"]) * tables["kernel"]
    spread = fm("vuSw,SwRb->vuRb", wave, tables["g2_back"])
    b_re, b_im = spread[:, :, 0], spread[:, :, 1]
    spread = jnp.stack([b_re * tw_re + b_im * tw_im, b_im * tw_re - b_re * tw_im], axis=2)
    back = fm("RasUS,vUSb->asRvb", tables["g1_back"], spread)
    back = back.reshape(devices, 2, slots, row_count)
    home = lax.all_to_all(back, ("roll", "side"), 0, 0, tiled=True)
    home = jnp.transpose(home, (1, 0, 2, 3)).reshape(2, all_slots, row_count)
    return fm("rvi,rvj->ij", home, col_table)


def per_device(
    pressure,
    source,
    side_coupling,
    block_inverse,
    lower_coupling,
    cavity_mask,
    rough_code,
    film_offset,
):
    row_count, col_count = pressure.shape
    roll_count = lax.axis_size("roll")
    side_count = lax.axis_size("side")
    roll_place = lax.axis_index("roll")
    side_place = lax.axis_index("side")
    pressure_now, tables = relax(
        pressure, source, side_coupling, block_inverse, lower_coupling, cavity_mask
    )
    deflection = deflection_of(pressure_now, tables)
    row_pos = (roll_place * row_count + counting(row_count)).astype(jnp.float32)
    col_pos = (side_place * col_count + counting(col_count)).astype(jnp.float32)
    across = 4.0 * (row_pos + 0.5) / (row_count * roll_count) - 2.5
    transverse = 4.0 * (col_pos + 0.5) / (col_count * side_count) - 2.0
    film_height = (
        film_offset[0]
        + 0.5 * across[:, None] * across[:, None]
        + 0.5 * transverse[None, :] * transverse[None, :]
        + deflection
        - ROUGH_STEP * rough_code.astype(jnp.float32)
    )
    return (pressure_now, film_height)


def solution(mesh):
    return jax.shard_map(
        per_device,
        mesh=mesh,
        in_specs=(
            P("roll", "side"),
            P("roll", "side"),
            P("roll", "side"),
            P("roll", "side"),
            P("roll", "side"),
            P("roll", "side"),
            P("roll", "side"),
            P(),
        ),
        out_specs=(P("roll", "side"), P("roll", "side")),
        check_vma=False,
    )
```

```python
import math

import jax
import jax.numpy as jnp
from jax import lax
from jax.sharding import PartitionSpec as P

SWEEPS = 4


HIGHEST = lax.Precision.HIGHEST
TWO_PI = 2.0 * math.pi
ROUGH_STEP = 0.05


def counting(length):
    return jnp.arange(length, dtype=jnp.int32)


def phase_pair(first_ints, second_ints, length, sign_value):
    angles = (first_ints * second_ints % length).astype(jnp.float32) * (TWO_PI / length)
    return (jnp.cos(angles), sign_value * jnp.sin(angles))


def mm(formula, left, right, precision=HIGHEST):
    return jnp.einsum(formula, left, right, precision=precision, preferred_element_type=jnp.float32)


def fm(formula, left, right):
    return mm(formula, left, right, lax.Precision.HIGH)


def col_tables(col_count, side_place, fft_cols, all_slots):
    split = 16 if col_count % 16 == 0 else 1
    freq = counting(all_slots)
    high = side_place * col_count + split * counting(col_count // split)
    high_re, high_im = phase_pair(high[:, None], freq[None, :], fft_cols, -1.0)
    low_re, low_im = phase_pair(counting(split)[:, None], freq[None, :], fft_cols, -1.0)
    cos_t = high_re[:, None, :] * low_re[None] - high_im[:, None, :] * low_im[None]
    sin_t = high_re[:, None, :] * low_im[None] + high_im[:, None, :] * low_re[None]
    table = jnp.stack([cos_t.reshape(col_count, all_slots), sin_t.reshape(col_count, all_slots)])
    return jnp.transpose(table, (0, 2, 1))


def complex_block(f_re, f_im):
    return jnp.stack([jnp.stack([f_re, -f_im]), jnp.stack([f_im, f_re])])


def fft_tables(row_count, col_count):
    roll_count = lax.axis_size("roll")
    side_count = lax.axis_size("side")
    side_place = lax.axis_index("side")
    devices = roll_count * side_count
    fft_rows = 2 * row_count * roll_count
    fft_cols = 2 * col_count * side_count
    half_cols = fft_cols // 2
    slots = -(-(half_cols + 1) // devices)
    all_slots = devices * slots
    first_len = fft_rows // row_count
    place_index = counting(roll_count)
    first_index = counting(first_len)
    inner_index = counting(row_count)
    col_table = col_tables(col_count, side_place, fft_cols, all_slots)
    f1_re, f1_im = phase_pair(first_index[:, None], place_index[None, :], first_len, -1.0)
    g1 = jnp.transpose(complex_block(f1_re, f1_im), (2, 0, 1, 3))
    g1_back = jnp.transpose(complex_block(f1_re, -f1_im), (0, 3, 2, 1))
    tw_re, tw_im = phase_pair(first_index[:, None], inner_index[None, :], fft_rows, -1.0)
    f2_re, f2_im = phase_pair(inner_index[:, None], inner_index[None, :], row_count, -1.0)
    g2 = jnp.transpose(complex_block(f2_re, f2_im), (1, 2, 0, 3))
    g2_back = jnp.transpose(complex_block(f2_re, -f2_im), (1, 3, 0, 2))
    my_device = lax.axis_index("roll") * side_count + side_place
    my_freq = my_device * slots + counting(slots)
    row_freq = first_index[:, None] + first_len * inner_index[None, :]
    row_wave = jnp.minimum(row_freq, fft_rows - row_freq).astype(jnp.float32) / fft_rows
    col_wave = jnp.minimum(my_freq, fft_cols - my_freq).astype(jnp.float32) / fft_cols
    kernel_reach = min(fft_rows, fft_cols) / 16.0
    radius = jnp.sqrt(
        row_wave[None] * row_wave[None] + col_wave[:, None, None] * col_wave[:, None, None]
    )
    weight = jnp.where(
        my_freq > half_cols, 0.0, jnp.where((my_freq == 0) | (my_freq == half_cols), 1.0, 2.0)
    )
    kernel = (0.4 * kernel_reach / (1.0 + kernel_reach * radius)) * (
        weight[:, None, None] / (float(fft_rows) * float(fft_cols))
    )
    return dict(
        col_table=col_table, g1=g1, g1_back=g1_back, tw_re=tw_re, tw_im=tw_im,
        g2=g2, g2_back=g2_back, kernel=kernel[:, :, None, :],
    )


def neighbour_cells(edges_left, edges_right):
    side_count = lax.axis_size("side")
    side_place = lax.axis_index("side")
    if side_count == 2:
        sent = jnp.where(side_place == 0, edges_right, edges_left)
        got = lax.ppermute(sent, "side", [(0, 1), (1, 0)])
        return jnp.where(side_place == 1, got, 0.0), jnp.where(side_place == 0, got, 0.0)
    to_right = [(i, i + 1) for i in range(side_count - 1)]
    to_left = [(i + 1, i) for i in range(side_count - 1)]
    return lax.ppermute(edges_right, "side", to_right), lax.ppermute(edges_left, "side", to_left)


def relax(pressure, source, side_coupling, block_inverse, lower_coupling, cavity_mask):
    row_count, col_count = pressure.shape
    roll_count = lax.axis_size("roll")
    roll_place = lax.axis_index("roll")
    halo = SWEEPS
    mask_f = (cavity_mask == 1).astype(jnp.float32)

    def edges(sl):
        wide = lambda row: jnp.broadcast_to(row[:, sl], (row_count, halo))
        return jnp.concatenate(
            [pressure[:, sl], source[:, sl], side_coupling[:, sl], block_inverse,
             wide(lower_coupling), wide(mask_f)],
            axis=1,
        )

    got_left, got_right = neighbour_cells(
        edges(slice(0, halo)), edges(slice(col_count - halo, col_count))
    )
    side_count = lax.axis_size("side")
    side_place = lax.axis_index("side")
    own_gain = block_inverse[row_count - 1, 0] * lower_coupling[0]
    all_gains = lax.all_to_all(
        jnp.broadcast_to(own_gain[None], (roll_count * side_count, col_count)),
        ("roll", "side"), 0, 0, tiled=True,
    ).reshape(roll_count, side_count, col_count)
    all_gains = jnp.pad(all_gains, ((0, 0), (1, 1), (0, 0)))

    def gains_of(place):
        return lax.dynamic_slice_in_dim(all_gains, place, 1, axis=1)[:, 0]

    gains = jnp.concatenate(
        [gains_of(side_place)[:, col_count - halo:], gains_of(side_place + 1),
         gains_of(side_place + 2)[:, :halo]],
        axis=1,
    )
    tables = fft_tables(row_count, col_count)
    got_left, got_right, tables = lax.optimization_barrier((got_left, got_right, tables))
    spans = [halo, halo, halo, row_count, halo, halo]
    cuts = [sum(spans[:n]) for n in range(7)]

    def unpack(got):
        return [got[:, cuts[n]:cuts[n + 1]] for n in range(6)]

    from_left, from_right = unpack(got_left), unpack(got_right)
    from_left[4], from_left[5] = from_left[4][0:1], from_left[5][0:1]
    from_right[4], from_right[5] = from_right[4][0:1], from_right[5][0:1]
    own = (pressure, source, side_coupling, block_inverse, lower_coupling, mask_f)
    ext = [jnp.concatenate([from_left[n], own[n], from_right[n]], axis=1) for n in range(6)]
    pressure_now, source_ext, coupling_ext, inverse_cat, lower_ext, mask_ext = ext
    lower_ext = lower_ext[0]
    mask_on = mask_ext[0] > 0.5
    left_inv, right_inv = from_left[3], from_right[3]
    width = col_count + 2 * halo
    first_ext = jnp.concatenate(
        [
            jnp.broadcast_to(left_inv[:, 0:1], (row_count, halo)),
            jnp.broadcast_to(block_inverse[:, 0:1], (row_count, col_count)),
            jnp.broadcast_to(right_inv[:, 0:1], (row_count, halo)),
        ],
        axis=1,
    )
    column = counting(width)
    block_masks = [
        (column < halo)[None, :],
        ((column >= halo) & (column < halo + col_count))[None, :],
        (column >= halo + col_count)[None, :],
    ]
    zero_col = jnp.zeros((row_count, 1), jnp.float32)
    for sweep_step in range(SWEEPS):
        left_of = jnp.concatenate([zero_col, pressure_now[:, :-1]], axis=1)
        right_of = jnp.concatenate([pressure_now[:, 1:], zero_col], axis=1)
        right_side = source_ext + coupling_ext * (left_of + right_of)
        stacked = jnp.concatenate([jnp.where(m, right_side, 0.0) for m in block_masks], axis=0)
        outflow = mm("m,mc->c", inverse_cat[row_count - 1], stacked)
        sent = jnp.broadcast_to(outflow[None], (roll_count, width))
        outflows = lax.all_to_all(sent, "roll", 0, 0, tiled=True)
        line_local = mm("im,mc->ic", inverse_cat, stacked)
        carry = jnp.zeros((width,), jnp.float32)
        for m in range(roll_count):
            carry = jnp.where(m < roll_place, outflows[m] + gains[m] * carry, carry)
        solved = line_local + first_ext * (lower_ext * carry)[None, :]
        pressure_now = jnp.where(mask_on[None, :], jnp.maximum(solved, 0.0), solved)
    return pressure_now[:, halo:halo + col_count], tables


def deflection_of(pressure_now, tables):
    row_count, col_count = pressure_now.shape
    roll_count = lax.axis_size("roll")
    side_count = lax.axis_size("side")
    devices = roll_count * side_count
    col_table = tables["col_table"]
    all_slots = col_table.shape[1]
    slots = all_slots // devices
    part = fm("rvj,ij->rvi", col_table, pressure_now)
    sent = jnp.transpose(part.reshape(2, devices, slots, row_count), (1, 0, 2, 3))
    got = lax.all_to_all(sent, ("roll", "side"), 0, 0, tiled=True)
    got = got.reshape(roll_count, side_count, 2, slots, row_count).sum(axis=1)
    spread = fm("uRra,arvb->vuRb", tables["g1"], got)
    tw_re, tw_im = tables["tw_re"], tables["tw_im"]
    a_re, a_im = spread[:, :, 0], spread[:, :, 1]
    spread = jnp.stack([a_re * tw_re - a_im * tw_im, a_re * tw_im + a_im * tw_re], axis=2)
    wave = fm("vuRb,RbSw->vuSw", spread, tables["g2"]) * tables["kernel"]
    spread = fm("vuSw,SwRb->vuRb", wave, tables["g2_back"])
    b_re, b_im = spread[:, :, 0], spread[:, :, 1]
    spread = jnp.stack([b_re * tw_re + b_im * tw_im, b_im * tw_re - b_re * tw_im], axis=2)
    back = fm("RaUS,vUSb->aRvb", tables["g1_back"], spread)
    back = jnp.broadcast_to(back[:, None], (roll_count, side_count, 2, slots, row_count))
    back = back.reshape(devices, 2, slots, row_count)
    home = lax.all_to_all(back, ("roll", "side"), 0, 0, tiled=True)
    home = jnp.transpose(home, (1, 0, 2, 3)).reshape(2, all_slots, row_count)
    return fm("rvi,rvj->ij", home, col_table)


def per_device(
    pressure,
    source,
    side_coupling,
    block_inverse,
    lower_coupling,
    cavity_mask,
    rough_code,
    film_offset,
):
    row_count, col_count = pressure.shape
    roll_count = lax.axis_size("roll")
    side_count = lax.axis_size("side")
    roll_place = lax.axis_index("roll")
    side_place = lax.axis_index("side")
    pressure_now, tables = relax(
        pressure, source, side_coupling, block_inverse, lower_coupling, cavity_mask
    )
    deflection = deflection_of(pressure_now, tables)
    row_pos = (roll_place * row_count + counting(row_count)).astype(jnp.float32)
    col_pos = (side_place * col_count + counting(col_count)).astype(jnp.float32)
    across = 4.0 * (row_pos + 0.5) / (row_count * roll_count) - 2.5
    transverse = 4.0 * (col_pos + 0.5) / (col_count * side_count) - 2.0
    film_height = (
        film_offset[0]
        + 0.5 * across[:, None] * across[:, None]
        + 0.5 * transverse[None, :] * transverse[None, :]
        + deflection
        - ROUGH_STEP * rough_code.astype(jnp.float32)
    )
    return (pressure_now, film_height)


def solution(mesh):
    return jax.shard_map(
        per_device,
        mesh=mesh,
        in_specs=(
            P("roll", "side"),
            P("roll", "side"),
            P("roll", "side"),
            P("roll", "side"),
            P("roll", "side"),
            P("roll", "side"),
            P("roll", "side"),
            P(),
        ),
        out_specs=(P("roll", "side"), P("roll", "side")),
        check_vma=False,
    )
```

```python
import math

import jax
import jax.numpy as jnp
from jax import lax
from jax.sharding import PartitionSpec as P

SWEEPS = 4


HIGHEST = lax.Precision.HIGHEST
TWO_PI = 2.0 * math.pi
ROUGH_STEP = 0.05


def counting(length):
    return jnp.arange(length, dtype=jnp.int32)


def phase_pair(first_ints, second_ints, length, sign_value):
    angles = (first_ints * second_ints % length).astype(jnp.float32) * (TWO_PI / length)
    return (jnp.cos(angles), sign_value * jnp.sin(angles))


def mm(formula, left, right, precision=HIGHEST):
    return jnp.einsum(formula, left, right, precision=precision, preferred_element_type=jnp.float32)


def fm(formula, left, right):
    return mm(formula, left, right, lax.Precision.HIGH)


def col_tables(col_count, side_place, fft_cols, all_slots):
    split = 16 if col_count % 16 == 0 else 1
    freq = counting(all_slots)
    high = side_place * col_count + split * counting(col_count // split)
    high_re, high_im = phase_pair(high[:, None], freq[None, :], fft_cols, -1.0)
    low_re, low_im = phase_pair(counting(split)[:, None], freq[None, :], fft_cols, -1.0)
    cos_t = high_re[:, None, :] * low_re[None] - high_im[:, None, :] * low_im[None]
    sin_t = high_re[:, None, :] * low_im[None] + high_im[:, None, :] * low_re[None]
    table = jnp.stack([cos_t.reshape(col_count, all_slots), sin_t.reshape(col_count, all_slots)])
    return jnp.transpose(table, (0, 2, 1))


def complex_block(f_re, f_im):
    return jnp.stack([jnp.stack([f_re, -f_im]), jnp.stack([f_im, f_re])])


def fft_tables(row_count, col_count):
    roll_count = lax.axis_size("roll")
    side_count = lax.axis_size("side")
    side_place = lax.axis_index("side")
    devices = roll_count * side_count
    fft_rows = 2 * row_count * roll_count
    fft_cols = 2 * col_count * side_count
    half_cols = fft_cols // 2
    slots = -(-(half_cols + 1) // devices)
    all_slots = devices * slots
    first_len = fft_rows // row_count
    place_index = counting(roll_count)
    first_index = counting(first_len)
    inner_index = counting(row_count)
    col_table = col_tables(col_count, side_place, fft_cols, all_slots)
    f1_re, f1_im = phase_pair(first_index[:, None], place_index[None, :], first_len, -1.0)
    g1 = jnp.transpose(complex_block(f1_re, f1_im), (2, 0, 1, 3))
    g1_back = jnp.transpose(complex_block(f1_re, -f1_im), (0, 3, 2, 1))
    tw_re, tw_im = phase_pair(first_index[:, None], inner_index[None, :], fft_rows, -1.0)
    f2_re, f2_im = phase_pair(inner_index[:, None], inner_index[None, :], row_count, -1.0)
    g2 = jnp.transpose(complex_block(f2_re, f2_im), (1, 2, 0, 3))
    g2_back = jnp.transpose(complex_block(f2_re, -f2_im), (1, 3, 0, 2))
    my_device = lax.axis_index("roll") * side_count + side_place
    my_freq = my_device * slots + counting(slots)
    row_freq = first_index[:, None] + first_len * inner_index[None, :]
    row_wave = jnp.minimum(row_freq, fft_rows - row_freq).astype(jnp.float32) / fft_rows
    col_wave = jnp.minimum(my_freq, fft_cols - my_freq).astype(jnp.float32) / fft_cols
    kernel_reach = min(fft_rows, fft_cols) / 16.0
    radius = jnp.sqrt(
        row_wave[None] * row_wave[None] + col_wave[:, None, None] * col_wave[:, None, None]
    )
    weight = jnp.where(
        my_freq > half_cols, 0.0, jnp.where((my_freq == 0) | (my_freq == half_cols), 1.0, 2.0)
    )
    kernel = (0.4 * kernel_reach / (1.0 + kernel_reach * radius)) * (
        weight[:, None, None] / (float(fft_rows) * float(fft_cols))
    )
    return dict(
        col_table=col_table, g1=g1, g1_back=g1_back, tw_re=tw_re, tw_im=tw_im,
        g2=g2, g2_back=g2_back, kernel=kernel[:, :, None, :],
    )


def relax(pressure, source, side_coupling, block_inverse, lower_coupling, cavity_mask):
    row_count, col_count = pressure.shape
    roll_count = lax.axis_size("roll")
    side_count = lax.axis_size("side")
    roll_place = lax.axis_index("roll")
    side_place = lax.axis_index("side")
    devices = roll_count * side_count
    last = row_count - 1
    mask_on = (cavity_mask[0] == 1)[None, :]
    lower = lower_coupling[0]
    first = block_inverse[:, 0:1]
    edge_coupling = jnp.stack([side_coupling[:, 0], side_coupling[:, col_count - 1]])
    edge_weight = block_inverse[last][None, :] * edge_coupling
    edge_inverse = block_inverse[None, :, :] * edge_coupling[:, None, :]
    gain = block_inverse[last, 0] * lower
    zero_col = jnp.zeros((row_count, 1), jnp.float32)
    pressure_now = pressure
    for sweep_step in range(SWEEPS):
        left_of = jnp.concatenate([zero_col, pressure_now[:, :-1]], axis=1)
        right_of = jnp.concatenate([pressure_now[:, 1:], zero_col], axis=1)
        right_side = source + side_coupling * (left_of + right_of)
        outflow = mm("m,mc->c", block_inverse[last], right_side)
        edges = jnp.stack([pressure_now[:, 0], pressure_now[:, col_count - 1]]).reshape(-1)
        parts = [outflow, edges]
        if sweep_step == 0:
            parts += [edge_weight.reshape(-1), gain]
        chunk = jnp.concatenate(parts)
        got = lax.all_to_all(
            jnp.broadcast_to(chunk[None], (devices, chunk.shape[0])), ("roll", "side"), 0, 0,
            tiled=True,
        ).reshape(roll_count, side_count, chunk.shape[0])
        if sweep_step == 0:
            tables = fft_tables(row_count, col_count)
            got, tables = lax.optimization_barrier((got, tables))
            tail = got[:, :, col_count + 2 * row_count:]
            weights = jnp.pad(tail[:, :, :2 * row_count], ((0, 0), (1, 1), (0, 0)))
            gains = jnp.pad(tail[:, :, 2 * row_count:], ((0, 0), (1, 1), (0, 0)))
            my_weights = lax.dynamic_index_in_dim(weights, side_place + 1, 1, False)
            my_weights = my_weights.reshape(roll_count, 2, row_count)
            my_gains = lax.dynamic_index_in_dim(gains, side_place + 1, 1, False)
        padded = jnp.pad(got[:, :, :col_count + 2 * row_count], ((0, 0), (1, 1), (0, 0)))
        mine = lax.dynamic_index_in_dim(padded, side_place + 1, 1, False)
        from_left = lax.dynamic_index_in_dim(padded, side_place, 1, False)
        from_right = lax.dynamic_index_in_dim(padded, side_place + 2, 1, False)
        near_left = from_left[:, col_count + row_count:]
        near_right = from_right[:, col_count:col_count + row_count]
        outflows = mine[:, :col_count]
        fix_first = jnp.sum(my_weights[:, 0] * near_left, axis=1)
        fix_last = jnp.sum(my_weights[:, 1] * near_right, axis=1)
        outflows = jnp.concatenate(
            [
                outflows[:, 0:1] + fix_first[:, None],
                outflows[:, 1:col_count - 1],
                outflows[:, col_count - 1:] + fix_last[:, None],
            ],
            axis=1,
        )
        carry = jnp.zeros((col_count,), jnp.float32)
        for m in range(roll_count):
            carry = jnp.where(m < roll_place, outflows[m] + my_gains[m] * carry, carry)
        line_local = mm("im,mc->ic", block_inverse, right_side)
        own_left = lax.dynamic_index_in_dim(near_left, roll_place, 0, False)
        own_right = lax.dynamic_index_in_dim(near_right, roll_place, 0, False)
        edge_fix = mm("eim,em->ie", edge_inverse, jnp.stack([own_left, own_right]))
        line_local = jnp.concatenate(
            [
                line_local[:, 0:1] + edge_fix[:, 0:1],
                line_local[:, 1:col_count - 1],
                line_local[:, col_count - 1:] + edge_fix[:, 1:2],
            ],
            axis=1,
        )
        solved = line_local + first * (lower * carry)[None, :]
        pressure_now = jnp.where(mask_on, jnp.maximum(solved, 0.0), solved)
    return pressure_now, tables


def deflection_of(pressure_now, tables):
    row_count, col_count = pressure_now.shape
    roll_count = lax.axis_size("roll")
    side_count = lax.axis_size("side")
    devices = roll_count * side_count
    col_table = tables["col_table"]
    all_slots = col_table.shape[1]
    slots = all_slots // devices
    part = fm("rvj,ij->rvi", col_table, pressure_now)
    sent = jnp.transpose(part.reshape(2, devices, slots, row_count), (1, 0, 2, 3))
    got = lax.all_to_all(sent, ("roll", "side"), 0, 0, tiled=True)
    got = got.reshape(roll_count, side_count, 2, slots, row_count).sum(axis=1)
    spread = fm("uRra,arvb->vuRb", tables["g1"], got)
    tw_re, tw_im = tables["tw_re"], tables["tw_im"]
    a_re, a_im = spread[:, :, 0], spread[:, :, 1]
    spread = jnp.stack([a_re * tw_re - a_im * tw_im, a_re * tw_im + a_im * tw_re], axis=2)
    wave = fm("vuRb,RbSw->vuSw", spread, tables["g2"]) * tables["kernel"]
    spread = fm("vuSw,SwRb->vuRb", wave, tables["g2_back"])
    b_re, b_im = spread[:, :, 0], spread[:, :, 1]
    spread = jnp.stack([b_re * tw_re + b_im * tw_im, b_im * tw_re - b_re * tw_im], axis=2)
    back = fm("RaUS,vUSb->aRvb", tables["g1_back"], spread)
    back = jnp.broadcast_to(back[:, None], (roll_count, side_count, 2, slots, row_count))
    back = back.reshape(devices, 2, slots, row_count)
    home = lax.all_to_all(back, ("roll", "side"), 0, 0, tiled=True)
    home = jnp.transpose(home, (1, 0, 2, 3)).reshape(2, all_slots, row_count)
    return fm("rvi,rvj->ij", home, col_table)


def per_device(
    pressure,
    source,
    side_coupling,
    block_inverse,
    lower_coupling,
    cavity_mask,
    rough_code,
    film_offset,
):
    row_count, col_count = pressure.shape
    roll_count = lax.axis_size("roll")
    side_count = lax.axis_size("side")
    roll_place = lax.axis_index("roll")
    side_place = lax.axis_index("side")
    pressure_now, tables = relax(
        pressure, source, side_coupling, block_inverse, lower_coupling, cavity_mask
    )
    deflection = deflection_of(pressure_now, tables)
    row_pos = (roll_place * row_count + counting(row_count)).astype(jnp.float32)
    col_pos = (side_place * col_count + counting(col_count)).astype(jnp.float32)
    across = 4.0 * (row_pos + 0.5) / (row_count * roll_count) - 2.5
    transverse = 4.0 * (col_pos + 0.5) / (col_count * side_count) - 2.0
    film_height = (
        film_offset[0]
        + 0.5 * across[:, None] * across[:, None]
        + 0.5 * transverse[None, :] * transverse[None, :]
        + deflection
        - ROUGH_STEP * rough_code.astype(jnp.float32)
    )
    return (pressure_now, film_height)


def solution(mesh):
    return jax.shard_map(
        per_device,
        mesh=mesh,
        in_specs=(
            P("roll", "side"),
            P("roll", "side"),
            P("roll", "side"),
            P("roll", "side"),
            P("roll", "side"),
            P("roll", "side"),
            P("roll", "side"),
            P(),
        ),
        out_specs=(P("roll", "side"), P("roll", "side")),
        check_vma=False,
    )
```

```python
import math

import jax
import jax.numpy as jnp
from jax import lax
from jax.sharding import PartitionSpec as P

SWEEPS = 4


HIGHEST = lax.Precision.HIGHEST
TWO_PI = 2.0 * math.pi
ROUGH_STEP = 0.05


def counting(length):
    return jnp.arange(length, dtype=jnp.int32)


def phase_pair(first_ints, second_ints, length, sign_value):
    angles = (first_ints * second_ints % length).astype(jnp.float32) * (TWO_PI / length)
    return (jnp.cos(angles), sign_value * jnp.sin(angles))


def mm(formula, left, right, precision=HIGHEST):
    return jnp.einsum(formula, left, right, precision=precision, preferred_element_type=jnp.float32)


def fm(formula, left, right):
    return mm(formula, left, right, lax.Precision.HIGH)


def col_tables(col_count, side_place, fft_cols, all_slots):
    split = 16 if col_count % 16 == 0 else 1
    freq = counting(all_slots)
    high = side_place * col_count + split * counting(col_count // split)
    high_re, high_im = phase_pair(high[:, None], freq[None, :], fft_cols, -1.0)
    low_re, low_im = phase_pair(counting(split)[:, None], freq[None, :], fft_cols, -1.0)
    cos_t = high_re[:, None, :] * low_re[None] - high_im[:, None, :] * low_im[None]
    sin_t = high_re[:, None, :] * low_im[None] + high_im[:, None, :] * low_re[None]
    table = jnp.stack([cos_t.reshape(col_count, all_slots), sin_t.reshape(col_count, all_slots)])
    return jnp.transpose(table, (0, 2, 1))


def complex_block(f_re, f_im):
    return jnp.stack([jnp.stack([f_re, -f_im]), jnp.stack([f_im, f_re])])


def fft_tables(row_count, col_count):
    roll_count = lax.axis_size("roll")
    side_count = lax.axis_size("side")
    side_place = lax.axis_index("side")
    devices = roll_count * side_count
    fft_rows = 2 * row_count * roll_count
    fft_cols = 2 * col_count * side_count
    half_cols = fft_cols // 2
    slots = -(-(half_cols + 1) // devices)
    all_slots = devices * slots
    first_len = fft_rows // row_count
    place_index = counting(roll_count)
    first_index = counting(first_len)
    inner_index = counting(row_count)
    col_table = col_tables(col_count, side_place, fft_cols, all_slots)
    f1_re, f1_im = phase_pair(first_index[:, None], place_index[None, :], first_len, -1.0)
    g1 = jnp.transpose(complex_block(f1_re, f1_im), (2, 0, 1, 3))
    g1_back = jnp.transpose(complex_block(f1_re, -f1_im), (0, 3, 2, 1))
    tw_re, tw_im = phase_pair(first_index[:, None], inner_index[None, :], fft_rows, -1.0)
    f2_re, f2_im = phase_pair(inner_index[:, None], inner_index[None, :], row_count, -1.0)
    g2 = jnp.transpose(complex_block(f2_re, f2_im), (1, 2, 0, 3))
    g2_back = jnp.transpose(complex_block(f2_re, -f2_im), (1, 3, 0, 2))
    my_device = lax.axis_index("roll") * side_count + side_place
    my_freq = my_device * slots + counting(slots)
    row_freq = first_index[:, None] + first_len * inner_index[None, :]
    row_wave = jnp.minimum(row_freq, fft_rows - row_freq).astype(jnp.float32) / fft_rows
    col_wave = jnp.minimum(my_freq, fft_cols - my_freq).astype(jnp.float32) / fft_cols
    kernel_reach = min(fft_rows, fft_cols) / 16.0
    radius = jnp.sqrt(
        row_wave[None] * row_wave[None] + col_wave[:, None, None] * col_wave[:, None, None]
    )
    weight = jnp.where(
        my_freq > half_cols, 0.0, jnp.where((my_freq == 0) | (my_freq == half_cols), 1.0, 2.0)
    )
    kernel = (0.4 * kernel_reach / (1.0 + kernel_reach * radius)) * (
        weight[:, None, None] / (float(fft_rows) * float(fft_cols))
    )
    return dict(
        col_table=col_table, g1=g1, g1_back=g1_back, tw_re=tw_re, tw_im=tw_im,
        g2=g2, g2_back=g2_back, kernel=kernel[:, :, None, :],
    )


def relax(pressure, source, side_coupling, block_inverse, lower_coupling, cavity_mask):
    row_count, col_count = pressure.shape
    roll_count = lax.axis_size("roll")
    side_count = lax.axis_size("side")
    roll_place = lax.axis_index("roll")
    side_place = lax.axis_index("side")
    devices = roll_count * side_count
    last = row_count - 1
    mask_on = (cavity_mask[0] == 1)[None, :]
    lower = lower_coupling[0]
    first = block_inverse[:, 0:1]
    edge_coupling = jnp.stack([side_coupling[:, 0], side_coupling[:, col_count - 1]])
    last_row = block_inverse[last]
    edge_weight = last_row[None, :] * edge_coupling
    edge_inverse = block_inverse[None, :, :] * edge_coupling[:, None, :]
    gain = last_row[0] * lower
    pressure_now = pressure
    for sweep_step in range(SWEEPS):
        padded = jnp.pad(pressure_now, ((0, 0), (1, 1)))
        right_side = source + side_coupling * (padded[:, :-2] + padded[:, 2:])
        outflow = mm("m,mc->c", last_row, right_side)
        edges = jnp.stack([pressure_now[:, 0], pressure_now[:, col_count - 1]]).reshape(-1)
        parts = [outflow, edges]
        if sweep_step == 0:
            parts += [edge_weight.reshape(-1), gain]
        chunk = jnp.concatenate(parts)
        got = lax.all_to_all(
            jnp.broadcast_to(chunk[None], (devices, chunk.shape[0])), ("roll", "side"), 0, 0,
            tiled=True,
        ).reshape(roll_count, side_count, chunk.shape[0])
        if sweep_step == 0:
            tables = fft_tables(row_count, col_count)
            got, tables = lax.optimization_barrier((got, tables))
            tail = got[:, :, col_count + 2 * row_count:]
            weights = jnp.pad(tail[:, :, :2 * row_count], ((0, 0), (1, 1), (0, 0)))
            gains = jnp.pad(tail[:, :, 2 * row_count:], ((0, 0), (1, 1), (0, 0)))
            my_weights = lax.dynamic_index_in_dim(weights, side_place + 1, 1, False)
            my_weights = my_weights.reshape(roll_count, 2, row_count)
            my_gains = lax.dynamic_index_in_dim(gains, side_place + 1, 1, False)
        padded = jnp.pad(got[:, :, :col_count + 2 * row_count], ((0, 0), (1, 1), (0, 0)))
        mine = lax.dynamic_index_in_dim(padded, side_place + 1, 1, False)
        from_left = lax.dynamic_index_in_dim(padded, side_place, 1, False)
        from_right = lax.dynamic_index_in_dim(padded, side_place + 2, 1, False)
        near_left = from_left[:, col_count + row_count:]
        near_right = from_right[:, col_count:col_count + row_count]
        outflows = mine[:, :col_count]
        fix_first = jnp.sum(my_weights[:, 0] * near_left, axis=1)
        fix_last = jnp.sum(my_weights[:, 1] * near_right, axis=1)
        outflows = jnp.concatenate(
            [
                outflows[:, 0:1] + fix_first[:, None],
                outflows[:, 1:col_count - 1],
                outflows[:, col_count - 1:] + fix_last[:, None],
            ],
            axis=1,
        )
        carry = jnp.zeros((col_count,), jnp.float32)
        for m in range(roll_count):
            carry = jnp.where(m < roll_place, outflows[m] + my_gains[m] * carry, carry)
        line_local = mm("im,mc->ic", block_inverse, right_side)
        own_left = lax.dynamic_index_in_dim(near_left, roll_place, 0, False)
        own_right = lax.dynamic_index_in_dim(near_right, roll_place, 0, False)
        edge_fix = mm("eim,em->ie", edge_inverse, jnp.stack([own_left, own_right]))
        line_local = jnp.concatenate(
            [
                line_local[:, 0:1] + edge_fix[:, 0:1],
                line_local[:, 1:col_count - 1],
                line_local[:, col_count - 1:] + edge_fix[:, 1:2],
            ],
            axis=1,
        )
        solved = line_local + first * (lower * carry)[None, :]
        pressure_now = jnp.where(mask_on, jnp.maximum(solved, 0.0), solved)
    return pressure_now, tables


def deflection_of(pressure_now, tables):
    row_count, col_count = pressure_now.shape
    roll_count = lax.axis_size("roll")
    side_count = lax.axis_size("side")
    devices = roll_count * side_count
    col_table = tables["col_table"]
    all_slots = col_table.shape[1]
    slots = all_slots // devices
    part = fm("rvj,ij->rvi", col_table, pressure_now)
    sent = jnp.transpose(part.reshape(2, devices, slots, row_count), (1, 0, 2, 3))
    got = lax.all_to_all(sent, ("roll", "side"), 0, 0, tiled=True)
    got = got.reshape(roll_count, side_count, 2, slots, row_count).sum(axis=1)
    spread = fm("uRra,arvb->vuRb", tables["g1"], got)
    tw_re, tw_im = tables["tw_re"], tables["tw_im"]
    a_re, a_im = spread[:, :, 0], spread[:, :, 1]
    spread = jnp.stack([a_re * tw_re - a_im * tw_im, a_re * tw_im + a_im * tw_re], axis=2)
    wave = fm("vuRb,RbSw->vuSw", spread, tables["g2"]) * tables["kernel"]
    spread = fm("vuSw,SwRb->vuRb", wave, tables["g2_back"])
    b_re, b_im = spread[:, :, 0], spread[:, :, 1]
    spread = jnp.stack([b_re * tw_re + b_im * tw_im, b_im * tw_re - b_re * tw_im], axis=2)
    back = fm("RaUS,vUSb->aRvb", tables["g1_back"], spread)
    back = jnp.broadcast_to(back[:, None], (roll_count, side_count, 2, slots, row_count))
    back = back.reshape(devices, 2, slots, row_count)
    home = lax.all_to_all(back, ("roll", "side"), 0, 0, tiled=True)
    home = jnp.transpose(home, (1, 0, 2, 3)).reshape(2, all_slots, row_count)
    return fm("rvi,rvj->ij", home, col_table)


def per_device(
    pressure,
    source,
    side_coupling,
    block_inverse,
    lower_coupling,
    cavity_mask,
    rough_code,
    film_offset,
):
    row_count, col_count = pressure.shape
    roll_count = lax.axis_size("roll")
    side_count = lax.axis_size("side")
    roll_place = lax.axis_index("roll")
    side_place = lax.axis_index("side")
    pressure_now, tables = relax(
        pressure, source, side_coupling, block_inverse, lower_coupling, cavity_mask
    )
    deflection = deflection_of(pressure_now, tables)
    row_pos = (roll_place * row_count + counting(row_count)).astype(jnp.float32)
    col_pos = (side_place * col_count + counting(col_count)).astype(jnp.float32)
    across = 4.0 * (row_pos + 0.5) / (row_count * roll_count) - 2.5
    transverse = 4.0 * (col_pos + 0.5) / (col_count * side_count) - 2.0
    film_height = (
        film_offset[0]
        + 0.5 * across[:, None] * across[:, None]
        + 0.5 * transverse[None, :] * transverse[None, :]
        + deflection
        - ROUGH_STEP * rough_code.astype(jnp.float32)
    )
    return (pressure_now, film_height)


def solution(mesh):
    return jax.shard_map(
        per_device,
        mesh=mesh,
        in_specs=(
            P("roll", "side"),
            P("roll", "side"),
            P("roll", "side"),
            P("roll", "side"),
            P("roll", "side"),
            P("roll", "side"),
            P("roll", "side"),
            P(),
        ),
        out_specs=(P("roll", "side"), P("roll", "side")),
        check_vma=False,
    )
```

```python
import math

import jax
import jax.numpy as jnp
from jax import lax
from jax.experimental import pallas as pl
from jax.experimental.pallas import tpu as pltpu
from jax.sharding import PartitionSpec as P

SWEEPS = 4
INTERPRET = False


HIGHEST = lax.Precision.HIGHEST
TWO_PI = 2.0 * math.pi
ROUGH_STEP = 0.05


def counting(length):
    return jnp.arange(length, dtype=jnp.int32)


def phase_pair(first_ints, second_ints, length, sign_value):
    angles = (first_ints * second_ints % length).astype(jnp.float32) * (TWO_PI / length)
    return (jnp.cos(angles), sign_value * jnp.sin(angles))


def mm(formula, left, right, precision=HIGHEST):
    return jnp.einsum(formula, left, right, precision=precision, preferred_element_type=jnp.float32)


def fm(formula, left, right):
    return mm(formula, left, right, lax.Precision.HIGH)


def col_tables(col_count, side_place, fft_cols, all_slots):
    split = 16 if col_count % 16 == 0 else 1
    freq = counting(all_slots)
    high = side_place * col_count + split * counting(col_count // split)
    high_re, high_im = phase_pair(high[:, None], freq[None, :], fft_cols, -1.0)
    low_re, low_im = phase_pair(counting(split)[:, None], freq[None, :], fft_cols, -1.0)
    cos_t = high_re[:, None, :] * low_re[None] - high_im[:, None, :] * low_im[None]
    sin_t = high_re[:, None, :] * low_im[None] + high_im[:, None, :] * low_re[None]
    table = jnp.stack([cos_t.reshape(col_count, all_slots), sin_t.reshape(col_count, all_slots)])
    return jnp.transpose(table, (0, 2, 1))


def complex_block(f_re, f_im):
    return jnp.stack([jnp.stack([f_re, -f_im]), jnp.stack([f_im, f_re])])


def fft_tables(row_count, col_count):
    roll_count = lax.axis_size("roll")
    side_count = lax.axis_size("side")
    side_place = lax.axis_index("side")
    devices = roll_count * side_count
    fft_rows = 2 * row_count * roll_count
    fft_cols = 2 * col_count * side_count
    half_cols = fft_cols // 2
    slots = -(-(half_cols + 1) // devices)
    all_slots = devices * slots
    first_len = fft_rows // row_count
    place_index = counting(roll_count)
    first_index = counting(first_len)
    inner_index = counting(row_count)
    col_table = col_tables(col_count, side_place, fft_cols, all_slots)
    f1_re, f1_im = phase_pair(first_index[:, None], place_index[None, :], first_len, -1.0)
    g1 = jnp.transpose(complex_block(f1_re, f1_im), (2, 0, 1, 3))
    g1_back = jnp.transpose(complex_block(f1_re, -f1_im), (0, 3, 2, 1))
    tw_re, tw_im = phase_pair(first_index[:, None], inner_index[None, :], fft_rows, -1.0)
    f2_re, f2_im = phase_pair(inner_index[:, None], inner_index[None, :], row_count, -1.0)
    g2 = jnp.transpose(complex_block(f2_re, f2_im), (1, 2, 0, 3))
    g2_back = jnp.transpose(complex_block(f2_re, -f2_im), (1, 3, 0, 2))
    my_device = lax.axis_index("roll") * side_count + side_place
    my_freq = my_device * slots + counting(slots)
    row_freq = first_index[:, None] + first_len * inner_index[None, :]
    row_wave = jnp.minimum(row_freq, fft_rows - row_freq).astype(jnp.float32) / fft_rows
    col_wave = jnp.minimum(my_freq, fft_cols - my_freq).astype(jnp.float32) / fft_cols
    kernel_reach = min(fft_rows, fft_cols) / 16.0
    radius = jnp.sqrt(
        row_wave[None] * row_wave[None] + col_wave[:, None, None] * col_wave[:, None, None]
    )
    weight = jnp.where(
        my_freq > half_cols, 0.0, jnp.where((my_freq == 0) | (my_freq == half_cols), 1.0, 2.0)
    )
    kernel = (0.4 * kernel_reach / (1.0 + kernel_reach * radius)) * (
        weight[:, None, None] / (float(fft_rows) * float(fft_cols))
    )
    return dict(
        col_table=col_table, g1=g1, g1_back=g1_back, tw_re=tw_re, tw_im=tw_im,
        g2=g2, g2_back=g2_back, kernel=kernel[:, :, None, :],
    )


def kdot(left, right, contract):
    return lax.dot_general(
        left, right, ((contract[0], contract[1]), ((), ())), precision=HIGHEST,
        preferred_element_type=jnp.float32,
    )


def make_tail(roll_count, side_count, chunk_len, row_count, col_count, more):
    devices = roll_count * side_count

    def tail(place_ref, got_ref, weights_ref, gains_ref, local_ref, inverse_ref, first_ref,
             lower_ref, mask_ref, source_ref, coupling_ref, *out_refs):
        roll_place = place_ref[0]
        side_place = place_ref[1]
        mine = jnp.zeros((roll_count, col_count + 2 * row_count), jnp.float32)
        left = mine
        right = mine
        for s in range(side_count):
            piece = got_ref[:, s * chunk_len:s * chunk_len + col_count + 2 * row_count]
            mine = mine + jnp.where(side_place == s, piece, 0.0)
            left = left + jnp.where(side_place - 1 == s, piece, 0.0)
            right = right + jnp.where(side_place + 1 == s, piece, 0.0)
        near_left = left[:, col_count + row_count:]
        near_right = right[:, col_count:col_count + row_count]
        col = lax.broadcasted_iota(jnp.int32, (1, col_count), 1)
        fix_first = jnp.sum(weights_ref[0] * near_left, axis=1, keepdims=True)
        fix_last = jnp.sum(weights_ref[1] * near_right, axis=1, keepdims=True)
        outflows = mine[:, :col_count]
        outflows = jnp.where(col == 0, outflows + fix_first, outflows)
        outflows = jnp.where(col == col_count - 1, outflows + fix_last, outflows)
        gains = gains_ref[...]
        carry = jnp.zeros((1, col_count), jnp.float32)
        for m in range(roll_count):
            carry = jnp.where(m < roll_place, outflows[m:m + 1] + gains[m:m + 1] * carry, carry)
        rows = lax.broadcasted_iota(jnp.int32, (roll_count, 1), 0)
        own_left = jnp.sum(jnp.where(rows == roll_place, near_left, 0.0), axis=0, keepdims=True)
        own_right = jnp.sum(jnp.where(rows == roll_place, near_right, 0.0), axis=0, keepdims=True)
        fix0 = kdot(inverse_ref[0], own_left, ((1,), (1,)))
        fix1 = kdot(inverse_ref[1], own_right, ((1,), (1,)))
        line = local_ref[...]
        line = jnp.where(col == 0, line + fix0, line)
        line = jnp.where(col == col_count - 1, line + fix1, line)
        solved = line + first_ref[...] * (lower_ref[...] * carry)
        field = jnp.where(mask_ref[...] > 0.5, jnp.maximum(solved, 0.0), solved)
        out_refs[0][...] = field
        if more:
            spot = col.astype(jnp.float32)
            one = pltpu.roll(field, 1, 1)
            other = pltpu.roll(field, col_count - 1, 1)
            one_ok = jnp.abs(pltpu.roll(spot, 1, 1) - spot) == 1.0
            other_ok = jnp.abs(pltpu.roll(spot, col_count - 1, 1) - spot) == 1.0
            both = jnp.where(one_ok, one, 0.0) + jnp.where(other_ok, other, 0.0)
            right_side = source_ref[...] + coupling_ref[...] * both
            out_refs[1][...] = right_side
            outflow = kdot(inverse_ref[2][0:1], right_side, ((1,), (0,)))
            pick = lax.broadcasted_iota(jnp.int32, (2, col_count), 1)
            which = lax.broadcasted_iota(jnp.int32, (2, col_count), 0)
            sel = jnp.where(pick == which * (col_count - 1), 1.0, 0.0)
            edges = kdot(sel, field, ((1,), (1,)))
            chunk = jnp.concatenate([outflow, edges[0:1], edges[1:2]], axis=1)
            out_refs[2][...] = jnp.broadcast_to(chunk, (devices, chunk.shape[1]))

    shapes = [jax.ShapeDtypeStruct((row_count, col_count), jnp.float32)]
    if more:
        shapes += [
            jax.ShapeDtypeStruct((row_count, col_count), jnp.float32),
            jax.ShapeDtypeStruct((devices, col_count + 2 * row_count), jnp.float32),
        ]
    vmem = pl.BlockSpec(memory_space=pltpu.VMEM)
    return pl.pallas_call(
        tail,
        out_shape=tuple(shapes),
        in_specs=[pl.BlockSpec(memory_space=pltpu.SMEM)] + [vmem] * 10,
        out_specs=tuple([vmem] * len(shapes)),
        interpret=INTERPRET,
    )


def relax(pressure, source, side_coupling, block_inverse, lower_coupling, cavity_mask):
    row_count, col_count = pressure.shape
    roll_count = lax.axis_size("roll")
    side_count = lax.axis_size("side")
    roll_place = lax.axis_index("roll")
    side_place = lax.axis_index("side")
    devices = roll_count * side_count
    last = row_count - 1
    mask_f = (cavity_mask == 1).astype(jnp.float32)
    first = block_inverse[:, 0:1]
    edge_coupling = jnp.stack([side_coupling[:, 0], side_coupling[:, col_count - 1]])
    last_row = block_inverse[last]
    edge_weight = last_row[None, :] * edge_coupling
    edge_inverse = block_inverse[None, :, :] * edge_coupling[:, None, :]
    extra = jnp.zeros((1, row_count, row_count), jnp.float32).at[0, 0].set(last_row)
    inverse_slabs = jnp.concatenate([edge_inverse, extra], axis=0)
    gain = last_row[0] * lower_coupling[0]
    places = jnp.stack([roll_place, side_place]).astype(jnp.int32)
    padded = jnp.pad(pressure, ((0, 0), (1, 1)))
    right_side = source + side_coupling * (padded[:, :-2] + padded[:, 2:])
    outflow = mm("m,mc->c", last_row, right_side)
    edges = jnp.stack([pressure[:, 0], pressure[:, col_count - 1]]).reshape(-1)
    chunk = jnp.concatenate([outflow, edges, edge_weight.reshape(-1), gain])
    sent = jnp.broadcast_to(chunk[None], (devices, chunk.shape[0]))
    for sweep_step in range(SWEEPS):
        got = lax.all_to_all(sent, ("roll", "side"), 0, 0, tiled=True)
        chunk_len = got.shape[1]
        got = got.reshape(roll_count, side_count * chunk_len)
        if sweep_step == 0:
            tables = fft_tables(row_count, col_count)
            got, tables = lax.optimization_barrier((got, tables))
            tail = got.reshape(roll_count, side_count, chunk_len)[:, :, col_count + 2 * row_count:]
            tail = jnp.pad(tail, ((0, 0), (1, 1), (0, 0)))
            tail = lax.dynamic_index_in_dim(tail, side_place + 1, 1, False)
            my_weights = jnp.transpose(
                tail[:, :2 * row_count].reshape(roll_count, 2, row_count), (1, 0, 2)
            )
            my_gains = tail[:, 2 * row_count:]
        line_local = mm("im,mc->ic", block_inverse, right_side)
        more = sweep_step < SWEEPS - 1
        outs = make_tail(roll_count, side_count, chunk_len, row_count, col_count, more)(
            places, got, my_weights, my_gains, line_local, inverse_slabs, first,
            lower_coupling, mask_f, source, side_coupling,
        )
        pressure_now = outs[0]
        if more:
            right_side, sent = outs[1], outs[2]
    return pressure_now, tables


def deflection_of(pressure_now, tables):
    row_count, col_count = pressure_now.shape
    roll_count = lax.axis_size("roll")
    side_count = lax.axis_size("side")
    devices = roll_count * side_count
    col_table = tables["col_table"]
    all_slots = col_table.shape[1]
    slots = all_slots // devices
    part = fm("rvj,ij->rvi", col_table, pressure_now)
    sent = jnp.transpose(part.reshape(2, devices, slots, row_count), (1, 0, 2, 3))
    got = lax.all_to_all(sent, ("roll", "side"), 0, 0, tiled=True)
    got = got.reshape(roll_count, side_count, 2, slots, row_count).sum(axis=1)
    spread = fm("uRra,arvb->vuRb", tables["g1"], got)
    tw_re, tw_im = tables["tw_re"], tables["tw_im"]
    a_re, a_im = spread[:, :, 0], spread[:, :, 1]
    spread = jnp.stack([a_re * tw_re - a_im * tw_im, a_re * tw_im + a_im * tw_re], axis=2)
    wave = fm("vuRb,RbSw->vuSw", spread, tables["g2"]) * tables["kernel"]
    spread = fm("vuSw,SwRb->vuRb", wave, tables["g2_back"])
    b_re, b_im = spread[:, :, 0], spread[:, :, 1]
    spread = jnp.stack([b_re * tw_re + b_im * tw_im, b_im * tw_re - b_re * tw_im], axis=2)
    back = fm("RaUS,vUSb->aRvb", tables["g1_back"], spread)
    back = jnp.broadcast_to(back[:, None], (roll_count, side_count, 2, slots, row_count))
    back = back.reshape(devices, 2, slots, row_count)
    home = lax.all_to_all(back, ("roll", "side"), 0, 0, tiled=True)
    home = jnp.transpose(home, (1, 0, 2, 3)).reshape(2, all_slots, row_count)
    return fm("rvi,rvj->ij", home, col_table)


def per_device(
    pressure,
    source,
    side_coupling,
    block_inverse,
    lower_coupling,
    cavity_mask,
    rough_code,
    film_offset,
):
    row_count, col_count = pressure.shape
    roll_count = lax.axis_size("roll")
    side_count = lax.axis_size("side")
    roll_place = lax.axis_index("roll")
    side_place = lax.axis_index("side")
    pressure_now, tables = relax(
        pressure, source, side_coupling, block_inverse, lower_coupling, cavity_mask
    )
    deflection = deflection_of(pressure_now, tables)
    row_pos = (roll_place * row_count + counting(row_count)).astype(jnp.float32)
    col_pos = (side_place * col_count + counting(col_count)).astype(jnp.float32)
    across = 4.0 * (row_pos + 0.5) / (row_count * roll_count) - 2.5
    transverse = 4.0 * (col_pos + 0.5) / (col_count * side_count) - 2.0
    film_height = (
        film_offset[0]
        + 0.5 * across[:, None] * across[:, None]
        + 0.5 * transverse[None, :] * transverse[None, :]
        + deflection
        - ROUGH_STEP * rough_code.astype(jnp.float32)
    )
    return (pressure_now, film_height)


def solution(mesh):
    return jax.shard_map(
        per_device,
        mesh=mesh,
        in_specs=(
            P("roll", "side"),
            P("roll", "side"),
            P("roll", "side"),
            P("roll", "side"),
            P("roll", "side"),
            P("roll", "side"),
            P("roll", "side"),
            P(),
        ),
        out_specs=(P("roll", "side"), P("roll", "side")),
        check_vma=False,
    )
```

```python
import math

import jax
import jax.numpy as jnp
from jax import lax
from jax.sharding import PartitionSpec as P

SWEEPS = 4


HIGHEST = lax.Precision.HIGHEST
TWO_PI = 2.0 * math.pi
ROUGH_STEP = 0.05


def counting(length):
    return jnp.arange(length, dtype=jnp.int32)


def phase_pair(first_ints, second_ints, length, sign_value):
    angles = (first_ints * second_ints % length).astype(jnp.float32) * (TWO_PI / length)
    return (jnp.cos(angles), sign_value * jnp.sin(angles))


def mm(formula, left, right, precision=HIGHEST):
    return jnp.einsum(formula, left, right, precision=precision, preferred_element_type=jnp.float32)


def fm(formula, left, right):
    return mm(formula, left, right, lax.Precision.HIGH)


def col_tables(col_count, side_place, fft_cols, all_slots):
    split = 16 if col_count % 16 == 0 else 1
    freq = counting(all_slots)
    high = side_place * col_count + split * counting(col_count // split)
    high_re, high_im = phase_pair(high[:, None], freq[None, :], fft_cols, -1.0)
    low_re, low_im = phase_pair(counting(split)[:, None], freq[None, :], fft_cols, -1.0)
    cos_t = high_re[:, None, :] * low_re[None] - high_im[:, None, :] * low_im[None]
    sin_t = high_re[:, None, :] * low_im[None] + high_im[:, None, :] * low_re[None]
    table = jnp.stack([cos_t.reshape(col_count, all_slots), sin_t.reshape(col_count, all_slots)])
    return jnp.transpose(table, (0, 2, 1))


def complex_block(f_re, f_im):
    return jnp.stack([jnp.stack([f_re, -f_im]), jnp.stack([f_im, f_re])])


def fft_tables(row_count, col_count):
    roll_count = lax.axis_size("roll")
    side_count = lax.axis_size("side")
    side_place = lax.axis_index("side")
    devices = roll_count * side_count
    fft_rows = 2 * row_count * roll_count
    fft_cols = 2 * col_count * side_count
    half_cols = fft_cols // 2
    slots = -(-(half_cols + 1) // devices)
    all_slots = devices * slots
    first_len = fft_rows // row_count
    place_index = counting(roll_count)
    first_index = counting(first_len)
    inner_index = counting(row_count)
    col_table = col_tables(col_count, side_place, fft_cols, all_slots)
    f1_re, f1_im = phase_pair(first_index[:, None], place_index[None, :], first_len, -1.0)
    g1 = jnp.transpose(complex_block(f1_re, f1_im), (2, 0, 1, 3))
    g1_back = jnp.transpose(complex_block(f1_re, -f1_im), (0, 3, 2, 1))
    tw_re, tw_im = phase_pair(first_index[:, None], inner_index[None, :], fft_rows, -1.0)
    f2_re, f2_im = phase_pair(inner_index[:, None], inner_index[None, :], row_count, -1.0)
    g2 = jnp.transpose(complex_block(f2_re, f2_im), (1, 2, 0, 3))
    g2_back = jnp.transpose(complex_block(f2_re, -f2_im), (1, 3, 0, 2))
    my_device = lax.axis_index("roll") * side_count + side_place
    my_freq = my_device * slots + counting(slots)
    row_freq = first_index[:, None] + first_len * inner_index[None, :]
    row_wave = jnp.minimum(row_freq, fft_rows - row_freq).astype(jnp.float32) / fft_rows
    col_wave = jnp.minimum(my_freq, fft_cols - my_freq).astype(jnp.float32) / fft_cols
    kernel_reach = min(fft_rows, fft_cols) / 16.0
    radius = jnp.sqrt(
        row_wave[None] * row_wave[None] + col_wave[:, None, None] * col_wave[:, None, None]
    )
    weight = jnp.where(
        my_freq > half_cols, 0.0, jnp.where((my_freq == 0) | (my_freq == half_cols), 1.0, 2.0)
    )
    kernel = (0.4 * kernel_reach / (1.0 + kernel_reach * radius)) * (
        weight[:, None, None] / (float(fft_rows) * float(fft_cols))
    )
    return dict(
        col_table=col_table, g1=g1, g1_back=g1_back, tw_re=tw_re, tw_im=tw_im,
        g2=g2, g2_back=g2_back, kernel=kernel[:, :, None, :],
    )


def relax(pressure, source, side_coupling, block_inverse, lower_coupling, cavity_mask):
    row_count, col_count = pressure.shape
    roll_count = lax.axis_size("roll")
    side_count = lax.axis_size("side")
    roll_place = lax.axis_index("roll")
    side_place = lax.axis_index("side")
    devices = roll_count * side_count
    last = row_count - 1
    mask_on = (cavity_mask[0] == 1)[None, :]
    lower = lower_coupling[0]
    first = block_inverse[:, 0:1]
    edge_coupling = jnp.stack([side_coupling[:, 0], side_coupling[:, col_count - 1]])
    edge_weight = block_inverse[last][None, :] * edge_coupling
    edge_inverse = block_inverse[None, :, :] * edge_coupling[:, None, :]
    gain = block_inverse[last, 0] * lower
    zero_col = jnp.zeros((row_count, 1), jnp.float32)
    pressure_now = pressure
    for sweep_step in range(SWEEPS):
        left_of = jnp.concatenate([zero_col, pressure_now[:, :-1]], axis=1)
        right_of = jnp.concatenate([pressure_now[:, 1:], zero_col], axis=1)
        right_side = source + side_coupling * (left_of + right_of)
        outflow = mm("m,mc->c", block_inverse[last], right_side)
        edges = jnp.stack([pressure_now[:, 0], pressure_now[:, col_count - 1]]).reshape(-1)
        parts = [outflow, edges]
        if sweep_step == 0:
            parts += [edge_weight.reshape(-1), gain]
        chunk = jnp.concatenate(parts)
        got = lax.all_to_all(
            jnp.broadcast_to(chunk[None], (devices, chunk.shape[0])), ("roll", "side"), 0, 0,
            tiled=True,
        ).reshape(roll_count, side_count, chunk.shape[0])
        if sweep_step == 0:
            tables = fft_tables(row_count, col_count)
            got, tables = lax.optimization_barrier((got, tables))
            tail = got[:, :, col_count + 2 * row_count:]
            weights = jnp.pad(tail[:, :, :2 * row_count], ((0, 0), (1, 1), (0, 0)))
            gains = jnp.pad(tail[:, :, 2 * row_count:], ((0, 0), (1, 1), (0, 0)))
            my_weights = lax.dynamic_index_in_dim(weights, side_place + 1, 1, False)
            my_weights = my_weights.reshape(roll_count, 2, row_count)
            my_gains = lax.dynamic_index_in_dim(gains, side_place + 1, 1, False)
        padded = jnp.pad(got[:, :, :col_count + 2 * row_count], ((0, 0), (1, 1), (0, 0)))
        mine = lax.dynamic_index_in_dim(padded, side_place + 1, 1, False)
        from_left = lax.dynamic_index_in_dim(padded, side_place, 1, False)
        from_right = lax.dynamic_index_in_dim(padded, side_place + 2, 1, False)
        near_left = from_left[:, col_count + row_count:]
        near_right = from_right[:, col_count:col_count + row_count]
        outflows = mine[:, :col_count]
        fix_first = jnp.sum(my_weights[:, 0] * near_left, axis=1)
        fix_last = jnp.sum(my_weights[:, 1] * near_right, axis=1)
        outflows = jnp.concatenate(
            [
                outflows[:, 0:1] + fix_first[:, None],
                outflows[:, 1:col_count - 1],
                outflows[:, col_count - 1:] + fix_last[:, None],
            ],
            axis=1,
        )
        carry = jnp.zeros((col_count,), jnp.float32)
        for m in range(roll_count):
            carry = jnp.where(m < roll_place, outflows[m] + my_gains[m] * carry, carry)
        line_local = mm("im,mc->ic", block_inverse, right_side)
        own_left = lax.dynamic_index_in_dim(near_left, roll_place, 0, False)
        own_right = lax.dynamic_index_in_dim(near_right, roll_place, 0, False)
        edge_fix = mm("eim,em->ie", edge_inverse, jnp.stack([own_left, own_right]))
        line_local = jnp.concatenate(
            [
                line_local[:, 0:1] + edge_fix[:, 0:1],
                line_local[:, 1:col_count - 1],
                line_local[:, col_count - 1:] + edge_fix[:, 1:2],
            ],
            axis=1,
        )
        solved = line_local + first * (lower * carry)[None, :]
        pressure_now = jnp.where(mask_on, jnp.maximum(solved, 0.0), solved)
    return pressure_now, tables


def deflection_of(pressure_now, tables):
    row_count, col_count = pressure_now.shape
    roll_count = lax.axis_size("roll")
    side_count = lax.axis_size("side")
    devices = roll_count * side_count
    col_table = tables["col_table"]
    all_slots = col_table.shape[1]
    slots = all_slots // devices
    part = fm("rvj,ij->rvi", col_table, pressure_now)
    sent = jnp.transpose(part.reshape(2, devices, slots, row_count), (1, 0, 2, 3))
    sent = sent.reshape(devices, 2 * slots * row_count)
    got = lax.all_to_all(sent, ("roll", "side"), 0, 0, tiled=True)
    got = got.reshape(roll_count, side_count, 2, slots, row_count).sum(axis=1)
    spread = fm("uRra,arvb->vuRb", tables["g1"], got)
    tw_re, tw_im = tables["tw_re"], tables["tw_im"]
    a_re, a_im = spread[:, :, 0], spread[:, :, 1]
    spread = jnp.stack([a_re * tw_re - a_im * tw_im, a_re * tw_im + a_im * tw_re], axis=2)
    wave = fm("vuRb,RbSw->vuSw", spread, tables["g2"]) * tables["kernel"]
    spread = fm("vuSw,SwRb->vuRb", wave, tables["g2_back"])
    b_re, b_im = spread[:, :, 0], spread[:, :, 1]
    spread = jnp.stack([b_re * tw_re + b_im * tw_im, b_im * tw_re - b_re * tw_im], axis=2)
    back = fm("RaUS,vUSb->aRvb", tables["g1_back"], spread)
    back = jnp.broadcast_to(back[:, None], (roll_count, side_count, 2, slots, row_count))
    back = back.reshape(devices, 2 * slots * row_count)
    home = lax.all_to_all(back, ("roll", "side"), 0, 0, tiled=True)
    home = home.reshape(devices, 2, slots, row_count)
    home = jnp.transpose(home, (1, 0, 2, 3)).reshape(2, all_slots, row_count)
    return fm("rvi,rvj->ij", home, col_table)


def per_device(
    pressure,
    source,
    side_coupling,
    block_inverse,
    lower_coupling,
    cavity_mask,
    rough_code,
    film_offset,
):
    row_count, col_count = pressure.shape
    roll_count = lax.axis_size("roll")
    side_count = lax.axis_size("side")
    roll_place = lax.axis_index("roll")
    side_place = lax.axis_index("side")
    pressure_now, tables = relax(
        pressure, source, side_coupling, block_inverse, lower_coupling, cavity_mask
    )
    deflection = deflection_of(pressure_now, tables)
    row_pos = (roll_place * row_count + counting(row_count)).astype(jnp.float32)
    col_pos = (side_place * col_count + counting(col_count)).astype(jnp.float32)
    across = 4.0 * (row_pos + 0.5) / (row_count * roll_count) - 2.5
    transverse = 4.0 * (col_pos + 0.5) / (col_count * side_count) - 2.0
    film_height = (
        film_offset[0]
        + 0.5 * across[:, None] * across[:, None]
        + 0.5 * transverse[None, :] * transverse[None, :]
        + deflection
        - ROUGH_STEP * rough_code.astype(jnp.float32)
    )
    return (pressure_now, film_height)


def solution(mesh):
    return jax.shard_map(
        per_device,
        mesh=mesh,
        in_specs=(
            P("roll", "side"),
            P("roll", "side"),
            P("roll", "side"),
            P("roll", "side"),
            P("roll", "side"),
            P("roll", "side"),
            P("roll", "side"),
            P(),
        ),
        out_specs=(P("roll", "side"), P("roll", "side")),
        check_vma=False,
    )
```

```python
import math

import jax
import jax.numpy as jnp
from jax import lax
from jax.sharding import PartitionSpec as P

SWEEPS = 4


HIGHEST = lax.Precision.HIGHEST
TWO_PI = 2.0 * math.pi
ROUGH_STEP = 0.05


def counting(length):
    return jnp.arange(length, dtype=jnp.int32)


def phase_pair(first_ints, second_ints, length, sign_value):
    angles = (first_ints * second_ints % length).astype(jnp.float32) * (TWO_PI / length)
    return (jnp.cos(angles), sign_value * jnp.sin(angles))


def mm(formula, left, right, precision=HIGHEST):
    return jnp.einsum(formula, left, right, precision=precision, preferred_element_type=jnp.float32)


def fm(formula, left, right):
    return mm(formula, left, right, lax.Precision.HIGH)


def col_tables(col_count, side_place, fft_cols, all_slots):
    split = 16 if col_count % 16 == 0 else 1
    freq = counting(all_slots)
    high = side_place * col_count + split * counting(col_count // split)
    high_re, high_im = phase_pair(high[:, None], freq[None, :], fft_cols, -1.0)
    low_re, low_im = phase_pair(counting(split)[:, None], freq[None, :], fft_cols, -1.0)
    cos_t = high_re[:, None, :] * low_re[None] - high_im[:, None, :] * low_im[None]
    sin_t = high_re[:, None, :] * low_im[None] + high_im[:, None, :] * low_re[None]
    table = jnp.stack([cos_t.reshape(col_count, all_slots), sin_t.reshape(col_count, all_slots)])
    return jnp.transpose(table, (0, 2, 1))


def complex_block(f_re, f_im):
    return jnp.stack([jnp.stack([f_re, -f_im]), jnp.stack([f_im, f_re])])


def fft_tables(row_count, col_count):
    roll_count = lax.axis_size("roll")
    side_count = lax.axis_size("side")
    side_place = lax.axis_index("side")
    devices = roll_count * side_count
    fft_rows = 2 * row_count * roll_count
    fft_cols = 2 * col_count * side_count
    half_cols = fft_cols // 2
    slots = -(-(half_cols + 1) // devices)
    all_slots = devices * slots
    first_len = fft_rows // row_count
    place_index = counting(roll_count)
    first_index = counting(first_len)
    inner_index = counting(row_count)
    col_table = col_tables(col_count, side_place, fft_cols, all_slots)
    f1_re, f1_im = phase_pair(first_index[:, None], place_index[None, :], first_len, -1.0)
    g1 = jnp.transpose(complex_block(f1_re, f1_im), (2, 0, 1, 3))
    g1_back = jnp.transpose(complex_block(f1_re, -f1_im), (0, 3, 2, 1))
    tw_re, tw_im = phase_pair(first_index[:, None], inner_index[None, :], fft_rows, -1.0)
    f2_re, f2_im = phase_pair(inner_index[:, None], inner_index[None, :], row_count, -1.0)
    g2 = jnp.transpose(complex_block(f2_re, f2_im), (1, 2, 0, 3))
    g2_back = jnp.transpose(complex_block(f2_re, -f2_im), (1, 3, 0, 2))
    my_device = lax.axis_index("roll") * side_count + side_place
    my_freq = my_device * slots + counting(slots)
    row_freq = first_index[:, None] + first_len * inner_index[None, :]
    row_wave = jnp.minimum(row_freq, fft_rows - row_freq).astype(jnp.float32) / fft_rows
    col_wave = jnp.minimum(my_freq, fft_cols - my_freq).astype(jnp.float32) / fft_cols
    kernel_reach = min(fft_rows, fft_cols) / 16.0
    radius = jnp.sqrt(
        row_wave[None] * row_wave[None] + col_wave[:, None, None] * col_wave[:, None, None]
    )
    weight = jnp.where(
        my_freq > half_cols, 0.0, jnp.where((my_freq == 0) | (my_freq == half_cols), 1.0, 2.0)
    )
    kernel = (0.4 * kernel_reach / (1.0 + kernel_reach * radius)) * (
        weight[:, None, None] / (float(fft_rows) * float(fft_cols))
    )
    return dict(
        col_table=col_table, g1=g1, g1_back=g1_back, tw_re=tw_re, tw_im=tw_im,
        g2=g2, g2_back=g2_back, kernel=kernel[:, :, None, :],
    )


def relax(pressure, source, side_coupling, block_inverse, lower_coupling, cavity_mask):
    row_count, col_count = pressure.shape
    roll_count = lax.axis_size("roll")
    side_count = lax.axis_size("side")
    roll_place = lax.axis_index("roll")
    side_place = lax.axis_index("side")
    devices = roll_count * side_count
    last = row_count - 1
    mask_on = (cavity_mask[0] == 1)[None, :]
    lower = lower_coupling[0]
    first = block_inverse[:, 0:1]
    edge_coupling = jnp.stack([side_coupling[:, 0], side_coupling[:, col_count - 1]])
    edge_weight = block_inverse[last][None, :] * edge_coupling
    edge_inverse = block_inverse[None, :, :] * edge_coupling[:, None, :]
    gain = block_inverse[last, 0] * lower
    zero_col = jnp.zeros((row_count, 1), jnp.float32)
    pressure_now = pressure
    for sweep_step in range(SWEEPS):
        left_of = jnp.concatenate([zero_col, pressure_now[:, :-1]], axis=1)
        right_of = jnp.concatenate([pressure_now[:, 1:], zero_col], axis=1)
        right_side = source + side_coupling * (left_of + right_of)
        outflow = mm("m,mc->c", block_inverse[last], right_side)
        edges = jnp.stack([pressure_now[:, 0], pressure_now[:, col_count - 1]]).reshape(-1)
        parts = [outflow, edges]
        if sweep_step == 0:
            parts += [edge_weight.reshape(-1), gain]
        chunk = jnp.concatenate(parts)
        got = lax.all_to_all(
            jnp.broadcast_to(chunk[None], (devices, chunk.shape[0])), ("roll", "side"), 0, 0,
            tiled=True,
        ).reshape(roll_count, side_count, chunk.shape[0])
        if sweep_step == 0:
            tables = fft_tables(row_count, col_count)
            got, tables = lax.optimization_barrier((got, tables))
            tail = got[:, :, col_count + 2 * row_count:]
            weights = jnp.pad(tail[:, :, :2 * row_count], ((0, 0), (1, 1), (0, 0)))
            gains = jnp.pad(tail[:, :, 2 * row_count:], ((0, 0), (1, 1), (0, 0)))
            my_weights = lax.dynamic_index_in_dim(weights, side_place + 1, 1, False)
            my_weights = my_weights.reshape(roll_count, 2, row_count)
            my_gains = lax.dynamic_index_in_dim(gains, side_place + 1, 1, False)
        head = got[:, :, :col_count + 2 * row_count]
        mine = sum(jnp.where(side_place == n, head[:, n], 0.0) for n in range(side_count))
        from_left = sum(jnp.where(side_place - 1 == n, head[:, n], 0.0) for n in range(side_count))
        from_right = sum(jnp.where(side_place + 1 == n, head[:, n], 0.0) for n in range(side_count))
        near_left = from_left[:, col_count + row_count:]
        near_right = from_right[:, col_count:col_count + row_count]
        outflows = mine[:, :col_count]
        fix_first = jnp.sum(my_weights[:, 0] * near_left, axis=1)
        fix_last = jnp.sum(my_weights[:, 1] * near_right, axis=1)
        outflows = jnp.concatenate(
            [
                outflows[:, 0:1] + fix_first[:, None],
                outflows[:, 1:col_count - 1],
                outflows[:, col_count - 1:] + fix_last[:, None],
            ],
            axis=1,
        )
        carry = jnp.zeros((col_count,), jnp.float32)
        for m in range(roll_count):
            carry = jnp.where(m < roll_place, outflows[m] + my_gains[m] * carry, carry)
        line_local = mm("im,mc->ic", block_inverse, right_side)
        own_left = lax.dynamic_index_in_dim(near_left, roll_place, 0, False)
        own_right = lax.dynamic_index_in_dim(near_right, roll_place, 0, False)
        edge_fix = mm("eim,em->ie", edge_inverse, jnp.stack([own_left, own_right]))
        line_local = jnp.concatenate(
            [
                line_local[:, 0:1] + edge_fix[:, 0:1],
                line_local[:, 1:col_count - 1],
                line_local[:, col_count - 1:] + edge_fix[:, 1:2],
            ],
            axis=1,
        )
        solved = line_local + first * (lower * carry)[None, :]
        pressure_now = jnp.where(mask_on, jnp.maximum(solved, 0.0), solved)
    return pressure_now, tables


def deflection_of(pressure_now, tables):
    row_count, col_count = pressure_now.shape
    roll_count = lax.axis_size("roll")
    side_count = lax.axis_size("side")
    devices = roll_count * side_count
    col_table = tables["col_table"]
    all_slots = col_table.shape[1]
    slots = all_slots // devices
    part = fm("rvj,ij->rvi", col_table, pressure_now)
    sent = jnp.transpose(part.reshape(2, devices, slots, row_count), (1, 0, 2, 3))
    got = lax.all_to_all(sent, ("roll", "side"), 0, 0, tiled=True)
    got = got.reshape(roll_count, side_count, 2, slots, row_count).sum(axis=1)
    spread = fm("uRra,arvb->vuRb", tables["g1"], got)
    tw_re, tw_im = tables["tw_re"], tables["tw_im"]
    a_re, a_im = spread[:, :, 0], spread[:, :, 1]
    spread = jnp.stack([a_re * tw_re - a_im * tw_im, a_re * tw_im + a_im * tw_re], axis=2)
    wave = fm("vuRb,RbSw->vuSw", spread, tables["g2"]) * tables["kernel"]
    spread = fm("vuSw,SwRb->vuRb", wave, tables["g2_back"])
    b_re, b_im = spread[:, :, 0], spread[:, :, 1]
    spread = jnp.stack([b_re * tw_re + b_im * tw_im, b_im * tw_re - b_re * tw_im], axis=2)
    back = fm("RaUS,vUSb->aRvb", tables["g1_back"], spread)
    back = jnp.broadcast_to(back[:, None], (roll_count, side_count, 2, slots, row_count))
    back = back.reshape(devices, 2, slots, row_count)
    home = lax.all_to_all(back, ("roll", "side"), 0, 0, tiled=True)
    home = jnp.transpose(home, (1, 0, 2, 3)).reshape(2, all_slots, row_count)
    return fm("rvi,rvj->ij", home, col_table)


def per_device(
    pressure,
    source,
    side_coupling,
    block_inverse,
    lower_coupling,
    cavity_mask,
    rough_code,
    film_offset,
):
    row_count, col_count = pressure.shape
    roll_count = lax.axis_size("roll")
    side_count = lax.axis_size("side")
    roll_place = lax.axis_index("roll")
    side_place = lax.axis_index("side")
    pressure_now, tables = relax(
        pressure, source, side_coupling, block_inverse, lower_coupling, cavity_mask
    )
    deflection = deflection_of(pressure_now, tables)
    row_pos = (roll_place * row_count + counting(row_count)).astype(jnp.float32)
    col_pos = (side_place * col_count + counting(col_count)).astype(jnp.float32)
    across = 4.0 * (row_pos + 0.5) / (row_count * roll_count) - 2.5
    transverse = 4.0 * (col_pos + 0.5) / (col_count * side_count) - 2.0
    film_height = (
        film_offset[0]
        + 0.5 * across[:, None] * across[:, None]
        + 0.5 * transverse[None, :] * transverse[None, :]
        + deflection
        - ROUGH_STEP * rough_code.astype(jnp.float32)
    )
    return (pressure_now, film_height)


def solution(mesh):
    return jax.shard_map(
        per_device,
        mesh=mesh,
        in_specs=(
            P("roll", "side"),
            P("roll", "side"),
            P("roll", "side"),
            P("roll", "side"),
            P("roll", "side"),
            P("roll", "side"),
            P("roll", "side"),
            P(),
        ),
        out_specs=(P("roll", "side"), P("roll", "side")),
        check_vma=False,
    )
```

```python
import math

import jax
import jax.numpy as jnp
from jax import lax
from jax.sharding import PartitionSpec as P

SWEEPS = 4


HIGHEST = lax.Precision.HIGHEST
TWO_PI = 2.0 * math.pi
ROUGH_STEP = 0.05


def counting(length):
    return jnp.arange(length, dtype=jnp.int32)


def phase_pair(first_ints, second_ints, length, sign_value):
    angles = (first_ints * second_ints % length).astype(jnp.float32) * (TWO_PI / length)
    return (jnp.cos(angles), sign_value * jnp.sin(angles))


def mm(formula, left, right, precision=HIGHEST):
    return jnp.einsum(formula, left, right, precision=precision, preferred_element_type=jnp.float32)


def fm(formula, left, right):
    return mm(formula, left, right, lax.Precision.HIGH)


def col_tables(col_count, side_place, fft_cols, all_slots):
    split = 16 if col_count % 16 == 0 else 1
    freq = counting(all_slots)
    high = side_place * col_count + split * counting(col_count // split)
    high_re, high_im = phase_pair(high[:, None], freq[None, :], fft_cols, -1.0)
    low_re, low_im = phase_pair(counting(split)[:, None], freq[None, :], fft_cols, -1.0)
    cos_t = high_re[:, None, :] * low_re[None] - high_im[:, None, :] * low_im[None]
    sin_t = high_re[:, None, :] * low_im[None] + high_im[:, None, :] * low_re[None]
    table = jnp.stack([cos_t.reshape(col_count, all_slots), sin_t.reshape(col_count, all_slots)])
    return jnp.transpose(table, (0, 2, 1))


def complex_block(f_re, f_im):
    return jnp.stack([jnp.stack([f_re, -f_im]), jnp.stack([f_im, f_re])])


def fft_tables(row_count, col_count):
    roll_count = lax.axis_size("roll")
    side_count = lax.axis_size("side")
    side_place = lax.axis_index("side")
    devices = roll_count * side_count
    fft_rows = 2 * row_count * roll_count
    fft_cols = 2 * col_count * side_count
    half_cols = fft_cols // 2
    slots = -(-(half_cols + 1) // devices)
    all_slots = devices * slots
    first_len = fft_rows // row_count
    place_index = counting(roll_count)
    first_index = counting(first_len)
    inner_index = counting(row_count)
    col_table = col_tables(col_count, side_place, fft_cols, all_slots)
    f1_re, f1_im = phase_pair(first_index[:, None], place_index[None, :], first_len, -1.0)
    g1 = jnp.transpose(complex_block(f1_re, f1_im), (2, 0, 1, 3))
    g1_back = jnp.transpose(complex_block(f1_re, -f1_im), (0, 3, 2, 1))
    tw_re, tw_im = phase_pair(first_index[:, None], inner_index[None, :], fft_rows, -1.0)
    f2_re, f2_im = phase_pair(inner_index[:, None], inner_index[None, :], row_count, -1.0)
    g2 = jnp.transpose(complex_block(f2_re, f2_im), (1, 2, 0, 3))
    g2_back = jnp.transpose(complex_block(f2_re, -f2_im), (1, 3, 0, 2))
    my_device = lax.axis_index("roll") * side_count + side_place
    my_freq = my_device * slots + counting(slots)
    row_freq = first_index[:, None] + first_len * inner_index[None, :]
    row_wave = jnp.minimum(row_freq, fft_rows - row_freq).astype(jnp.float32) / fft_rows
    col_wave = jnp.minimum(my_freq, fft_cols - my_freq).astype(jnp.float32) / fft_cols
    kernel_reach = min(fft_rows, fft_cols) / 16.0
    radius = jnp.sqrt(
        row_wave[None] * row_wave[None] + col_wave[:, None, None] * col_wave[:, None, None]
    )
    weight = jnp.where(
        my_freq > half_cols, 0.0, jnp.where((my_freq == 0) | (my_freq == half_cols), 1.0, 2.0)
    )
    kernel = (0.4 * kernel_reach / (1.0 + kernel_reach * radius)) * (
        weight[:, None, None] / (float(fft_rows) * float(fft_cols))
    )
    return dict(
        col_table=col_table, g1=g1, g1_back=g1_back, tw_re=tw_re, tw_im=tw_im,
        g2=g2, g2_back=g2_back, kernel=kernel[:, :, None, :],
    )


def relax(pressure, source, side_coupling, block_inverse, lower_coupling, cavity_mask):
    row_count, col_count = pressure.shape
    roll_count = lax.axis_size("roll")
    side_count = lax.axis_size("side")
    roll_place = lax.axis_index("roll")
    side_place = lax.axis_index("side")
    devices = roll_count * side_count
    last = row_count - 1
    mask_on = (cavity_mask[0] == 1)[None, :]
    lower = lower_coupling[0]
    first = block_inverse[:, 0:1]
    edge_coupling = jnp.stack([side_coupling[:, 0], side_coupling[:, col_count - 1]])
    edge_weight = block_inverse[last][None, :] * edge_coupling
    edge_inverse = block_inverse[None, :, :] * edge_coupling[:, None, :]
    gain = block_inverse[last, 0] * lower
    zero_col = jnp.zeros((row_count, 1), jnp.float32)
    pressure_now = pressure
    for sweep_step in range(SWEEPS):
        left_of = jnp.concatenate([zero_col, pressure_now[:, :-1]], axis=1)
        right_of = jnp.concatenate([pressure_now[:, 1:], zero_col], axis=1)
        right_side = source + side_coupling * (left_of + right_of)
        outflow = mm("m,mc->c", block_inverse[last], right_side)
        edges = jnp.stack([pressure_now[:, 0], pressure_now[:, col_count - 1]]).reshape(-1)
        parts = [outflow, edges]
        if sweep_step == 0:
            parts += [edge_weight.reshape(-1), gain]
        sent = jnp.concatenate(
            [jnp.broadcast_to(piece[None], (devices, piece.shape[0])) for piece in parts], axis=1
        )
        got = lax.all_to_all(sent, ("roll", "side"), 0, 0, tiled=True)
        got = got.reshape(roll_count, side_count, sent.shape[1])
        if sweep_step == 0:
            tables = fft_tables(row_count, col_count)
            got, tables = lax.optimization_barrier((got, tables))
            tail = got[:, :, col_count + 2 * row_count:]
            weights = jnp.pad(tail[:, :, :2 * row_count], ((0, 0), (1, 1), (0, 0)))
            gains = jnp.pad(tail[:, :, 2 * row_count:], ((0, 0), (1, 1), (0, 0)))
            my_weights = lax.dynamic_index_in_dim(weights, side_place + 1, 1, False)
            my_weights = my_weights.reshape(roll_count, 2, row_count)
            my_gains = lax.dynamic_index_in_dim(gains, side_place + 1, 1, False)
        head = got[:, :, :col_count + 2 * row_count]
        mine = sum(jnp.where(side_place == n, head[:, n], 0.0) for n in range(side_count))
        from_left = sum(jnp.where(side_place - 1 == n, head[:, n], 0.0) for n in range(side_count))
        from_right = sum(jnp.where(side_place + 1 == n, head[:, n], 0.0) for n in range(side_count))
        near_left = from_left[:, col_count + row_count:]
        near_right = from_right[:, col_count:col_count + row_count]
        outflows = mine[:, :col_count]
        fix_first = jnp.sum(my_weights[:, 0] * near_left, axis=1)
        fix_last = jnp.sum(my_weights[:, 1] * near_right, axis=1)
        outflows = jnp.concatenate(
            [
                outflows[:, 0:1] + fix_first[:, None],
                outflows[:, 1:col_count - 1],
                outflows[:, col_count - 1:] + fix_last[:, None],
            ],
            axis=1,
        )
        carry = jnp.zeros((col_count,), jnp.float32)
        for m in range(roll_count):
            carry = jnp.where(m < roll_place, outflows[m] + my_gains[m] * carry, carry)
        line_local = mm("im,mc->ic", block_inverse, right_side)
        own_left = lax.dynamic_index_in_dim(near_left, roll_place, 0, False)
        own_right = lax.dynamic_index_in_dim(near_right, roll_place, 0, False)
        edge_fix = mm("eim,em->ie", edge_inverse, jnp.stack([own_left, own_right]))
        line_local = jnp.concatenate(
            [
                line_local[:, 0:1] + edge_fix[:, 0:1],
                line_local[:, 1:col_count - 1],
                line_local[:, col_count - 1:] + edge_fix[:, 1:2],
            ],
            axis=1,
        )
        solved = line_local + first * (lower * carry)[None, :]
        pressure_now = jnp.where(mask_on, jnp.maximum(solved, 0.0), solved)
    return pressure_now, tables


def deflection_of(pressure_now, tables):
    row_count, col_count = pressure_now.shape
    roll_count = lax.axis_size("roll")
    side_count = lax.axis_size("side")
    devices = roll_count * side_count
    col_table = tables["col_table"]
    all_slots = col_table.shape[1]
    slots = all_slots // devices
    part = fm("rvj,ij->rvi", col_table, pressure_now)
    sent = jnp.transpose(part.reshape(2, devices, slots, row_count), (1, 0, 2, 3))
    got = lax.all_to_all(sent, ("roll", "side"), 0, 0, tiled=True)
    got = got.reshape(roll_count, side_count, 2, slots, row_count).sum(axis=1)
    spread = fm("uRra,arvb->vuRb", tables["g1"], got)
    tw_re, tw_im = tables["tw_re"], tables["tw_im"]
    a_re, a_im = spread[:, :, 0], spread[:, :, 1]
    spread = jnp.stack([a_re * tw_re - a_im * tw_im, a_re * tw_im + a_im * tw_re], axis=2)
    wave = fm("vuRb,RbSw->vuSw", spread, tables["g2"]) * tables["kernel"]
    spread = fm("vuSw,SwRb->vuRb", wave, tables["g2_back"])
    b_re, b_im = spread[:, :, 0], spread[:, :, 1]
    spread = jnp.stack([b_re * tw_re + b_im * tw_im, b_im * tw_re - b_re * tw_im], axis=2)
    back = fm("RaUS,vUSb->aRvb", tables["g1_back"], spread)
    back = jnp.broadcast_to(back[:, None], (roll_count, side_count, 2, slots, row_count))
    back = back.reshape(devices, 2, slots, row_count)
    home = lax.all_to_all(back, ("roll", "side"), 0, 0, tiled=True)
    home = jnp.transpose(home, (1, 0, 2, 3)).reshape(2, all_slots, row_count)
    return fm("rvi,rvj->ij", home, col_table)


def per_device(
    pressure,
    source,
    side_coupling,
    block_inverse,
    lower_coupling,
    cavity_mask,
    rough_code,
    film_offset,
):
    row_count, col_count = pressure.shape
    roll_count = lax.axis_size("roll")
    side_count = lax.axis_size("side")
    roll_place = lax.axis_index("roll")
    side_place = lax.axis_index("side")
    pressure_now, tables = relax(
        pressure, source, side_coupling, block_inverse, lower_coupling, cavity_mask
    )
    deflection = deflection_of(pressure_now, tables)
    row_pos = (roll_place * row_count + counting(row_count)).astype(jnp.float32)
    col_pos = (side_place * col_count + counting(col_count)).astype(jnp.float32)
    across = 4.0 * (row_pos + 0.5) / (row_count * roll_count) - 2.5
    transverse = 4.0 * (col_pos + 0.5) / (col_count * side_count) - 2.0
    film_height = (
        film_offset[0]
        + 0.5 * across[:, None] * across[:, None]
        + 0.5 * transverse[None, :] * transverse[None, :]
        + deflection
        - ROUGH_STEP * rough_code.astype(jnp.float32)
    )
    return (pressure_now, film_height)


def solution(mesh):
    return jax.shard_map(
        per_device,
        mesh=mesh,
        in_specs=(
            P("roll", "side"),
            P("roll", "side"),
            P("roll", "side"),
            P("roll", "side"),
            P("roll", "side"),
            P("roll", "side"),
            P("roll", "side"),
            P(),
        ),
        out_specs=(P("roll", "side"), P("roll", "side")),
        check_vma=False,
    )
```

```python
import math

import jax
import jax.numpy as jnp
from jax import lax
from jax.sharding import PartitionSpec as P

SWEEPS = 4


HIGHEST = lax.Precision.HIGHEST
TWO_PI = 2.0 * math.pi
ROUGH_STEP = 0.05


def counting(length):
    return jnp.arange(length, dtype=jnp.int32)


def phase_pair(first_ints, second_ints, length, sign_value):
    angles = (first_ints * second_ints % length).astype(jnp.float32) * (TWO_PI / length)
    return (jnp.cos(angles), sign_value * jnp.sin(angles))


def mm(formula, left, right, precision=HIGHEST):
    return jnp.einsum(formula, left, right, precision=precision, preferred_element_type=jnp.float32)


def fm(formula, left, right):
    return mm(formula, left, right, lax.Precision.HIGH)


def col_tables(col_count, side_place, fft_cols, all_slots):
    split = 16 if col_count % 16 == 0 else 1
    freq = counting(all_slots)
    high = side_place * col_count + split * counting(col_count // split)
    high_re, high_im = phase_pair(high[:, None], freq[None, :], fft_cols, -1.0)
    low_re, low_im = phase_pair(counting(split)[:, None], freq[None, :], fft_cols, -1.0)
    cos_t = high_re[:, None, :] * low_re[None] - high_im[:, None, :] * low_im[None]
    sin_t = high_re[:, None, :] * low_im[None] + high_im[:, None, :] * low_re[None]
    table = jnp.stack([cos_t.reshape(col_count, all_slots), sin_t.reshape(col_count, all_slots)])
    return jnp.transpose(table, (0, 2, 1))


def complex_block(f_re, f_im):
    return jnp.stack([jnp.stack([f_re, -f_im]), jnp.stack([f_im, f_re])])


def fft_tables(row_count, col_count):
    roll_count = lax.axis_size("roll")
    side_count = lax.axis_size("side")
    side_place = lax.axis_index("side")
    devices = roll_count * side_count
    fft_rows = 2 * row_count * roll_count
    fft_cols = 2 * col_count * side_count
    half_cols = fft_cols // 2
    slots = -(-(half_cols + 1) // devices)
    all_slots = devices * slots
    first_len = fft_rows // row_count
    place_index = counting(roll_count)
    first_index = counting(first_len)
    inner_index = counting(row_count)
    col_table = col_tables(col_count, side_place, fft_cols, all_slots)
    f1_re, f1_im = phase_pair(first_index[:, None], place_index[None, :], first_len, -1.0)
    g1 = jnp.transpose(complex_block(f1_re, f1_im), (2, 0, 1, 3))
    g1_back = jnp.transpose(complex_block(f1_re, -f1_im), (0, 3, 2, 1))
    tw_re, tw_im = phase_pair(first_index[:, None], inner_index[None, :], fft_rows, -1.0)
    f2_re, f2_im = phase_pair(inner_index[:, None], inner_index[None, :], row_count, -1.0)
    g2 = jnp.transpose(complex_block(f2_re, f2_im), (1, 2, 0, 3))
    g2_back = jnp.transpose(complex_block(f2_re, -f2_im), (1, 3, 0, 2))
    my_device = lax.axis_index("roll") * side_count + side_place
    my_freq = my_device * slots + counting(slots)
    row_freq = first_index[:, None] + first_len * inner_index[None, :]
    row_wave = jnp.minimum(row_freq, fft_rows - row_freq).astype(jnp.float32) / fft_rows
    col_wave = jnp.minimum(my_freq, fft_cols - my_freq).astype(jnp.float32) / fft_cols
    kernel_reach = min(fft_rows, fft_cols) / 16.0
    radius = jnp.sqrt(
        row_wave[None] * row_wave[None] + col_wave[:, None, None] * col_wave[:, None, None]
    )
    weight = jnp.where(
        my_freq > half_cols, 0.0, jnp.where((my_freq == 0) | (my_freq == half_cols), 1.0, 2.0)
    )
    kernel = (0.4 * kernel_reach / (1.0 + kernel_reach * radius)) * (
        weight[:, None, None] / (float(fft_rows) * float(fft_cols))
    )
    return dict(
        col_table=col_table, g1=g1, g1_back=g1_back, tw_re=tw_re, tw_im=tw_im,
        g2=g2, g2_back=g2_back, kernel=kernel[:, :, None, :],
    )


def relax(pressure, source, side_coupling, block_inverse, lower_coupling, cavity_mask):
    row_count, col_count = pressure.shape
    roll_count = lax.axis_size("roll")
    side_count = lax.axis_size("side")
    roll_place = lax.axis_index("roll")
    side_place = lax.axis_index("side")
    devices = roll_count * side_count
    last = row_count - 1
    mask_on = (cavity_mask[0] == 1)[None, :]
    lower = lower_coupling[0]
    first = block_inverse[:, 0:1]
    edge_coupling = jnp.stack([side_coupling[:, 0], side_coupling[:, col_count - 1]])
    last_row = lax.optimization_barrier(block_inverse[last])
    edge_weight = last_row[None, :] * edge_coupling
    edge_inverse = block_inverse[None, :, :] * edge_coupling[:, None, :]
    gain = last_row[0] * lower
    zero_col = jnp.zeros((row_count, 1), jnp.float32)
    pressure_now = pressure
    for sweep_step in range(SWEEPS):
        left_of = jnp.concatenate([zero_col, pressure_now[:, :-1]], axis=1)
        right_of = jnp.concatenate([pressure_now[:, 1:], zero_col], axis=1)
        right_side = source + side_coupling * (left_of + right_of)
        outflow = mm("m,mc->c", last_row, right_side)
        edges = jnp.stack([pressure_now[:, 0], pressure_now[:, col_count - 1]]).reshape(-1)
        parts = [outflow, edges]
        if sweep_step == 0:
            parts += [edge_weight.reshape(-1), gain]
        sent = jnp.concatenate(
            [jnp.broadcast_to(piece[None], (devices, piece.shape[0])) for piece in parts], axis=1
        )
        got = lax.all_to_all(sent, ("roll", "side"), 0, 0, tiled=True)
        got = got.reshape(roll_count, side_count, sent.shape[1])
        if sweep_step == 0:
            tables = fft_tables(row_count, col_count)
            got, tables = lax.optimization_barrier((got, tables))
            tail = got[:, :, col_count + 2 * row_count:]
            weights = jnp.pad(tail[:, :, :2 * row_count], ((0, 0), (1, 1), (0, 0)))
            gains = jnp.pad(tail[:, :, 2 * row_count:], ((0, 0), (1, 1), (0, 0)))
            my_weights = lax.dynamic_index_in_dim(weights, side_place + 1, 1, False)
            my_weights = my_weights.reshape(roll_count, 2, row_count)
            my_gains = lax.dynamic_index_in_dim(gains, side_place + 1, 1, False)
        head = got[:, :, :col_count + 2 * row_count]
        mine = sum(jnp.where(side_place == n, head[:, n], 0.0) for n in range(side_count))
        from_left = sum(jnp.where(side_place - 1 == n, head[:, n], 0.0) for n in range(side_count))
        from_right = sum(jnp.where(side_place + 1 == n, head[:, n], 0.0) for n in range(side_count))
        near_left = from_left[:, col_count + row_count:]
        near_right = from_right[:, col_count:col_count + row_count]
        outflows = mine[:, :col_count]
        fix_first = jnp.sum(my_weights[:, 0] * near_left, axis=1)
        fix_last = jnp.sum(my_weights[:, 1] * near_right, axis=1)
        outflows = jnp.concatenate(
            [
                outflows[:, 0:1] + fix_first[:, None],
                outflows[:, 1:col_count - 1],
                outflows[:, col_count - 1:] + fix_last[:, None],
            ],
            axis=1,
        )
        carry = jnp.zeros((col_count,), jnp.float32)
        for m in range(roll_count):
            carry = jnp.where(m < roll_place, outflows[m] + my_gains[m] * carry, carry)
        line_local = mm("im,mc->ic", block_inverse, right_side)
        own_left = lax.dynamic_index_in_dim(near_left, roll_place, 0, False)
        own_right = lax.dynamic_index_in_dim(near_right, roll_place, 0, False)
        edge_fix = mm("eim,em->ie", edge_inverse, jnp.stack([own_left, own_right]))
        line_local = jnp.concatenate(
            [
                line_local[:, 0:1] + edge_fix[:, 0:1],
                line_local[:, 1:col_count - 1],
                line_local[:, col_count - 1:] + edge_fix[:, 1:2],
            ],
            axis=1,
        )
        solved = line_local + first * (lower * carry)[None, :]
        pressure_now = jnp.where(mask_on, jnp.maximum(solved, 0.0), solved)
    return pressure_now, tables


def deflection_of(pressure_now, tables):
    row_count, col_count = pressure_now.shape
    roll_count = lax.axis_size("roll")
    side_count = lax.axis_size("side")
    devices = roll_count * side_count
    col_table = tables["col_table"]
    all_slots = col_table.shape[1]
    slots = all_slots // devices
    part = fm("rvj,ij->rvi", col_table, pressure_now)
    sent = jnp.transpose(part.reshape(2, devices, slots, row_count), (1, 0, 2, 3))
    got = lax.all_to_all(sent, ("roll", "side"), 0, 0, tiled=True)
    got = got.reshape(roll_count, side_count, 2, slots, row_count).sum(axis=1)
    spread = fm("uRra,arvb->vuRb", tables["g1"], got)
    tw_re, tw_im = tables["tw_re"], tables["tw_im"]
    a_re, a_im = spread[:, :, 0], spread[:, :, 1]
    spread = jnp.stack([a_re * tw_re - a_im * tw_im, a_re * tw_im + a_im * tw_re], axis=2)
    wave = fm("vuRb,RbSw->vuSw", spread, tables["g2"]) * tables["kernel"]
    spread = fm("vuSw,SwRb->vuRb", wave, tables["g2_back"])
    b_re, b_im = spread[:, :, 0], spread[:, :, 1]
    spread = jnp.stack([b_re * tw_re + b_im * tw_im, b_im * tw_re - b_re * tw_im], axis=2)
    back = fm("RaUS,vUSb->aRvb", tables["g1_back"], spread)
    back = jnp.broadcast_to(back[:, None], (roll_count, side_count, 2, slots, row_count))
    back = back.reshape(devices, 2, slots, row_count)
    home = lax.all_to_all(back, ("roll", "side"), 0, 0, tiled=True)
    home = jnp.transpose(home, (1, 0, 2, 3)).reshape(2, all_slots, row_count)
    return fm("rvi,rvj->ij", home, col_table)


def per_device(
    pressure,
    source,
    side_coupling,
    block_inverse,
    lower_coupling,
    cavity_mask,
    rough_code,
    film_offset,
):
    row_count, col_count = pressure.shape
    roll_count = lax.axis_size("roll")
    side_count = lax.axis_size("side")
    roll_place = lax.axis_index("roll")
    side_place = lax.axis_index("side")
    pressure_now, tables = relax(
        pressure, source, side_coupling, block_inverse, lower_coupling, cavity_mask
    )
    deflection = deflection_of(pressure_now, tables)
    row_pos = (roll_place * row_count + counting(row_count)).astype(jnp.float32)
    col_pos = (side_place * col_count + counting(col_count)).astype(jnp.float32)
    across = 4.0 * (row_pos + 0.5) / (row_count * roll_count) - 2.5
    transverse = 4.0 * (col_pos + 0.5) / (col_count * side_count) - 2.0
    film_height = (
        film_offset[0]
        + 0.5 * across[:, None] * across[:, None]
        + 0.5 * transverse[None, :] * transverse[None, :]
        + deflection
        - ROUGH_STEP * rough_code.astype(jnp.float32)
    )
    return (pressure_now, film_height)


def solution(mesh):
    return jax.shard_map(
        per_device,
        mesh=mesh,
        in_specs=(
            P("roll", "side"),
            P("roll", "side"),
            P("roll", "side"),
            P("roll", "side"),
            P("roll", "side"),
            P("roll", "side"),
            P("roll", "side"),
            P(),
        ),
        out_specs=(P("roll", "side"), P("roll", "side")),
        check_vma=False,
    )
```

```python
import math

import jax
import jax.numpy as jnp
from jax import lax
from jax.sharding import PartitionSpec as P

SWEEPS = 4


HIGHEST = lax.Precision.HIGHEST
TWO_PI = 2.0 * math.pi
ROUGH_STEP = 0.05


def counting(length):
    return jnp.arange(length, dtype=jnp.int32)


def phase_pair(first_ints, second_ints, length, sign_value):
    angles = (first_ints * second_ints % length).astype(jnp.float32) * (TWO_PI / length)
    return (jnp.cos(angles), sign_value * jnp.sin(angles))


def mm(formula, left, right, precision=HIGHEST):
    return jnp.einsum(formula, left, right, precision=precision, preferred_element_type=jnp.float32)


def fm(formula, left, right):
    return mm(formula, left, right, lax.Precision.HIGH)


def col_tables(col_count, side_place, fft_cols, all_slots):
    split = 16 if col_count % 16 == 0 else 1
    freq = counting(all_slots)
    high = side_place * col_count + split * counting(col_count // split)
    high_re, high_im = phase_pair(high[:, None], freq[None, :], fft_cols, -1.0)
    low_re, low_im = phase_pair(counting(split)[:, None], freq[None, :], fft_cols, -1.0)
    cos_t = high_re[:, None, :] * low_re[None] - high_im[:, None, :] * low_im[None]
    sin_t = high_re[:, None, :] * low_im[None] + high_im[:, None, :] * low_re[None]
    table = jnp.stack([cos_t.reshape(col_count, all_slots), sin_t.reshape(col_count, all_slots)])
    return jnp.transpose(table, (0, 2, 1))


def complex_block(f_re, f_im):
    return jnp.stack([jnp.stack([f_re, -f_im]), jnp.stack([f_im, f_re])])


def fft_tables(row_count, col_count):
    roll_count = lax.axis_size("roll")
    side_count = lax.axis_size("side")
    side_place = lax.axis_index("side")
    devices = roll_count * side_count
    fft_rows = 2 * row_count * roll_count
    fft_cols = 2 * col_count * side_count
    half_cols = fft_cols // 2
    slots = -(-(half_cols + 1) // devices)
    all_slots = devices * slots
    first_len = fft_rows // row_count
    place_index = counting(roll_count)
    first_index = counting(first_len)
    inner_index = counting(row_count)
    col_table = col_tables(col_count, side_place, fft_cols, all_slots)
    f1_re, f1_im = phase_pair(first_index[:, None], place_index[None, :], first_len, -1.0)
    g1 = jnp.transpose(complex_block(f1_re, f1_im), (2, 0, 1, 3))
    g1_back = jnp.transpose(complex_block(f1_re, -f1_im), (0, 3, 2, 1))
    tw_re, tw_im = phase_pair(first_index[:, None], inner_index[None, :], fft_rows, -1.0)
    f2_re, f2_im = phase_pair(inner_index[:, None], inner_index[None, :], row_count, -1.0)
    g2 = jnp.transpose(complex_block(f2_re, f2_im), (1, 2, 0, 3))
    g2_back = jnp.transpose(complex_block(f2_re, -f2_im), (1, 3, 0, 2))
    my_device = lax.axis_index("roll") * side_count + side_place
    my_freq = my_device * slots + counting(slots)
    row_freq = first_index[:, None] + first_len * inner_index[None, :]
    row_wave = jnp.minimum(row_freq, fft_rows - row_freq).astype(jnp.float32) / fft_rows
    col_wave = jnp.minimum(my_freq, fft_cols - my_freq).astype(jnp.float32) / fft_cols
    kernel_reach = min(fft_rows, fft_cols) / 16.0
    radius = jnp.sqrt(
        row_wave[None] * row_wave[None] + col_wave[:, None, None] * col_wave[:, None, None]
    )
    weight = jnp.where(
        my_freq > half_cols, 0.0, jnp.where((my_freq == 0) | (my_freq == half_cols), 1.0, 2.0)
    )
    kernel = (0.4 * kernel_reach / (1.0 + kernel_reach * radius)) * (
        weight[:, None, None] / (float(fft_rows) * float(fft_cols))
    )
    return dict(
        col_table=col_table, g1=g1, g1_back=g1_back, tw_re=tw_re, tw_im=tw_im,
        g2=g2, g2_back=g2_back, kernel=kernel[:, :, None, :],
    )


def relax(pressure, source, side_coupling, block_inverse, lower_coupling, cavity_mask):
    row_count, col_count = pressure.shape
    roll_count = lax.axis_size("roll")
    side_count = lax.axis_size("side")
    roll_place = lax.axis_index("roll")
    side_place = lax.axis_index("side")
    devices = roll_count * side_count
    last = row_count - 1
    mask_on = (cavity_mask[0] == 1)[None, :]
    lower = lower_coupling[0]
    first = block_inverse[:, 0:1]
    first_edges = jnp.stack(
        [pressure[:, 0], pressure[:, col_count - 1], side_coupling[:, 0],
         side_coupling[:, col_count - 1]]
    )
    edge_coupling = first_edges[2:]
    last_row = lax.optimization_barrier(block_inverse[last])
    edge_weight = last_row[None, :] * edge_coupling
    edge_inverse = block_inverse[None, :, :] * edge_coupling[:, None, :]
    gain = last_row[0] * lower
    pressure_now = pressure
    for sweep_step in range(SWEEPS):
        padded = jnp.pad(pressure_now, ((0, 0), (1, 1)))
        right_side = source + side_coupling * (padded[:, :-2] + padded[:, 2:])
        outflow = mm("m,mc->c", last_row, right_side)
        if sweep_step == 0:
            edges = first_edges[:2].reshape(-1)
        else:
            edges = jnp.stack([pressure_now[:, 0], pressure_now[:, col_count - 1]]).reshape(-1)
        parts = [outflow, edges]
        if sweep_step == 0:
            parts += [edge_weight.reshape(-1), gain]
        sent = jnp.concatenate(
            [jnp.broadcast_to(piece[None], (devices, piece.shape[0])) for piece in parts], axis=1
        )
        got = lax.all_to_all(sent, ("roll", "side"), 0, 0, tiled=True)
        got = got.reshape(roll_count, side_count, sent.shape[1])
        if sweep_step == 0:
            tables = fft_tables(row_count, col_count)
            got, tables = lax.optimization_barrier((got, tables))
            tail = got[:, :, col_count + 2 * row_count:]
            weights = jnp.pad(tail[:, :, :2 * row_count], ((0, 0), (1, 1), (0, 0)))
            gains = jnp.pad(tail[:, :, 2 * row_count:], ((0, 0), (1, 1), (0, 0)))
            my_weights = lax.dynamic_index_in_dim(weights, side_place + 1, 1, False)
            my_weights = my_weights.reshape(roll_count, 2, row_count)
            my_gains = lax.dynamic_index_in_dim(gains, side_place + 1, 1, False)
        head = got[:, :, :col_count + 2 * row_count]
        mine = sum(jnp.where(side_place == n, head[:, n], 0.0) for n in range(side_count))
        from_left = sum(jnp.where(side_place - 1 == n, head[:, n], 0.0) for n in range(side_count))
        from_right = sum(jnp.where(side_place + 1 == n, head[:, n], 0.0) for n in range(side_count))
        near_left = from_left[:, col_count + row_count:]
        near_right = from_right[:, col_count:col_count + row_count]
        outflows = mine[:, :col_count]
        fix_first = jnp.sum(my_weights[:, 0] * near_left, axis=1)
        fix_last = jnp.sum(my_weights[:, 1] * near_right, axis=1)
        outflows = jnp.concatenate(
            [
                outflows[:, 0:1] + fix_first[:, None],
                outflows[:, 1:col_count - 1],
                outflows[:, col_count - 1:] + fix_last[:, None],
            ],
            axis=1,
        )
        carry = jnp.zeros((col_count,), jnp.float32)
        for m in range(roll_count):
            carry = jnp.where(m < roll_place, outflows[m] + my_gains[m] * carry, carry)
        line_local = mm("im,mc->ic", block_inverse, right_side)
        own_left = lax.dynamic_index_in_dim(near_left, roll_place, 0, False)
        own_right = lax.dynamic_index_in_dim(near_right, roll_place, 0, False)
        edge_fix = mm("eim,em->ie", edge_inverse, jnp.stack([own_left, own_right]))
        line_local = jnp.concatenate(
            [
                line_local[:, 0:1] + edge_fix[:, 0:1],
                line_local[:, 1:col_count - 1],
                line_local[:, col_count - 1:] + edge_fix[:, 1:2],
            ],
            axis=1,
        )
        solved = line_local + first * (lower * carry)[None, :]
        pressure_now = jnp.where(mask_on, jnp.maximum(solved, 0.0), solved)
    return pressure_now, tables


def deflection_of(pressure_now, tables):
    row_count, col_count = pressure_now.shape
    roll_count = lax.axis_size("roll")
    side_count = lax.axis_size("side")
    devices = roll_count * side_count
    col_table = tables["col_table"]
    all_slots = col_table.shape[1]
    slots = all_slots // devices
    part = fm("rvj,ij->rvi", col_table, pressure_now)
    sent = jnp.transpose(part.reshape(2, devices, slots, row_count), (1, 0, 2, 3))
    got = lax.all_to_all(sent, ("roll", "side"), 0, 0, tiled=True)
    got = got.reshape(roll_count, side_count, 2, slots, row_count).sum(axis=1)
    spread = fm("uRra,arvb->vuRb", tables["g1"], got)
    tw_re, tw_im = tables["tw_re"], tables["tw_im"]
    a_re, a_im = spread[:, :, 0], spread[:, :, 1]
    spread = jnp.stack([a_re * tw_re - a_im * tw_im, a_re * tw_im + a_im * tw_re], axis=2)
    wave = fm("vuRb,RbSw->vuSw", spread, tables["g2"]) * tables["kernel"]
    spread = fm("vuSw,SwRb->vuRb", wave, tables["g2_back"])
    b_re, b_im = spread[:, :, 0], spread[:, :, 1]
    spread = jnp.stack([b_re * tw_re + b_im * tw_im, b_im * tw_re - b_re * tw_im], axis=2)
    back = fm("RaUS,vUSb->aRvb", tables["g1_back"], spread)
    back = jnp.broadcast_to(back[:, None], (roll_count, side_count, 2, slots, row_count))
    back = back.reshape(devices, 2, slots, row_count)
    home = lax.all_to_all(back, ("roll", "side"), 0, 0, tiled=True)
    home = jnp.transpose(home, (1, 0, 2, 3)).reshape(2, all_slots, row_count)
    return fm("rvi,rvj->ij", home, col_table)


def per_device(
    pressure,
    source,
    side_coupling,
    block_inverse,
    lower_coupling,
    cavity_mask,
    rough_code,
    film_offset,
):
    row_count, col_count = pressure.shape
    roll_count = lax.axis_size("roll")
    side_count = lax.axis_size("side")
    roll_place = lax.axis_index("roll")
    side_place = lax.axis_index("side")
    pressure_now, tables = relax(
        pressure, source, side_coupling, block_inverse, lower_coupling, cavity_mask
    )
    deflection = deflection_of(pressure_now, tables)
    row_pos = (roll_place * row_count + counting(row_count)).astype(jnp.float32)
    col_pos = (side_place * col_count + counting(col_count)).astype(jnp.float32)
    across = 4.0 * (row_pos + 0.5) / (row_count * roll_count) - 2.5
    transverse = 4.0 * (col_pos + 0.5) / (col_count * side_count) - 2.0
    film_height = (
        film_offset[0]
        + 0.5 * across[:, None] * across[:, None]
        + 0.5 * transverse[None, :] * transverse[None, :]
        + deflection
        - ROUGH_STEP * rough_code.astype(jnp.float32)
    )
    return (pressure_now, film_height)


def solution(mesh):
    return jax.shard_map(
        per_device,
        mesh=mesh,
        in_specs=(
            P("roll", "side"),
            P("roll", "side"),
            P("roll", "side"),
            P("roll", "side"),
            P("roll", "side"),
            P("roll", "side"),
            P("roll", "side"),
            P(),
        ),
        out_specs=(P("roll", "side"), P("roll", "side")),
        check_vma=False,
    )
```

```python
import math

import jax
import jax.numpy as jnp
from jax import lax
from jax.sharding import PartitionSpec as P

SWEEPS = 4


HIGHEST = lax.Precision.HIGHEST
TWO_PI = 2.0 * math.pi
ROUGH_STEP = 0.05


def counting(length):
    return jnp.arange(length, dtype=jnp.int32)


def phase_pair(first_ints, second_ints, length, sign_value):
    angles = (first_ints * second_ints % length).astype(jnp.float32) * (TWO_PI / length)
    return (jnp.cos(angles), sign_value * jnp.sin(angles))


def mm(formula, left, right, precision=HIGHEST):
    return jnp.einsum(formula, left, right, precision=precision, preferred_element_type=jnp.float32)


def fm(formula, left, right):
    return mm(formula, left, right, lax.Precision.HIGH)


def col_tables(col_count, side_place, fft_cols, all_slots):
    split = 16 if col_count % 16 == 0 else 1
    freq = counting(all_slots)
    high = side_place * col_count + split * counting(col_count // split)
    high_re, high_im = phase_pair(high[:, None], freq[None, :], fft_cols, -1.0)
    low_re, low_im = phase_pair(counting(split)[:, None], freq[None, :], fft_cols, -1.0)
    cos_t = high_re[:, None, :] * low_re[None] - high_im[:, None, :] * low_im[None]
    sin_t = high_re[:, None, :] * low_im[None] + high_im[:, None, :] * low_re[None]
    table = jnp.stack([cos_t.reshape(col_count, all_slots), sin_t.reshape(col_count, all_slots)])
    return jnp.transpose(table, (0, 2, 1))


def complex_block(f_re, f_im):
    return jnp.stack([jnp.stack([f_re, -f_im]), jnp.stack([f_im, f_re])])


def fft_tables(row_count, col_count):
    roll_count = lax.axis_size("roll")
    side_count = lax.axis_size("side")
    side_place = lax.axis_index("side")
    devices = roll_count * side_count
    fft_rows = 2 * row_count * roll_count
    fft_cols = 2 * col_count * side_count
    half_cols = fft_cols // 2
    slots = -(-(half_cols + 1) // devices)
    all_slots = devices * slots
    first_len = fft_rows // row_count
    place_index = counting(roll_count)
    first_index = counting(first_len)
    inner_index = counting(row_count)
    col_table = col_tables(col_count, side_place, fft_cols, all_slots)
    f1_re, f1_im = phase_pair(first_index[:, None], place_index[None, :], first_len, -1.0)
    g1 = jnp.transpose(complex_block(f1_re, f1_im), (2, 0, 1, 3))
    g1_back = jnp.transpose(complex_block(f1_re, -f1_im), (0, 3, 2, 1))
    tw_re, tw_im = phase_pair(first_index[:, None], inner_index[None, :], fft_rows, -1.0)
    f2_re, f2_im = phase_pair(inner_index[:, None], inner_index[None, :], row_count, -1.0)
    g2 = jnp.transpose(complex_block(f2_re, f2_im), (1, 2, 0, 3))
    g2_back = jnp.transpose(complex_block(f2_re, -f2_im), (1, 3, 0, 2))
    my_device = lax.axis_index("roll") * side_count + side_place
    my_freq = my_device * slots + counting(slots)
    row_freq = first_index[:, None] + first_len * inner_index[None, :]
    row_wave = jnp.minimum(row_freq, fft_rows - row_freq).astype(jnp.float32) / fft_rows
    col_wave = jnp.minimum(my_freq, fft_cols - my_freq).astype(jnp.float32) / fft_cols
    kernel_reach = min(fft_rows, fft_cols) / 16.0
    radius = jnp.sqrt(
        row_wave[None] * row_wave[None] + col_wave[:, None, None] * col_wave[:, None, None]
    )
    weight = jnp.where(
        my_freq > half_cols, 0.0, jnp.where((my_freq == 0) | (my_freq == half_cols), 1.0, 2.0)
    )
    kernel = (0.4 * kernel_reach / (1.0 + kernel_reach * radius)) * (
        weight[:, None, None] / (float(fft_rows) * float(fft_cols))
    )
    return dict(
        col_table=col_table, g1=g1, g1_back=g1_back, tw_re=tw_re, tw_im=tw_im,
        g2=g2, g2_back=g2_back, kernel=kernel[:, :, None, :],
    )


def relax(pressure, source, side_coupling, block_inverse, lower_coupling, cavity_mask):
    row_count, col_count = pressure.shape
    roll_count = lax.axis_size("roll")
    side_count = lax.axis_size("side")
    roll_place = lax.axis_index("roll")
    side_place = lax.axis_index("side")
    devices = roll_count * side_count
    last = row_count - 1
    mask_on = (cavity_mask[0] == 1)[None, :]
    lower = lower_coupling[0]
    first = block_inverse[:, 0:1]
    first_edges = jnp.stack(
        [pressure[:, 0], pressure[:, col_count - 1], side_coupling[:, 0],
         side_coupling[:, col_count - 1]]
    )
    edge_coupling = first_edges[2:]
    last_row = lax.optimization_barrier(block_inverse[last])
    edge_weight = last_row[None, :] * edge_coupling
    edge_inverse = block_inverse[None, :, :] * edge_coupling[:, None, :]
    gain = last_row[0] * lower
    col = counting(col_count)[None, :]
    pressure_now = pressure
    for sweep_step in range(SWEEPS):
        padded = jnp.pad(pressure_now, ((0, 0), (1, 1)))
        right_side = source + side_coupling * (padded[:, :-2] + padded[:, 2:])
        outflow = mm("m,mc->c", last_row, right_side)
        if sweep_step == 0:
            edges = first_edges[:2].reshape(-1)
        else:
            edges = jnp.stack([pressure_now[:, 0], pressure_now[:, col_count - 1]]).reshape(-1)
        parts = [outflow, edges]
        if sweep_step == 0:
            parts += [edge_weight.reshape(-1), gain]
        sent = jnp.concatenate(
            [jnp.broadcast_to(piece[None], (devices, piece.shape[0])) for piece in parts], axis=1
        )
        got = lax.all_to_all(sent, ("roll", "side"), 0, 0, tiled=True)
        got = got.reshape(roll_count, side_count, sent.shape[1])
        if sweep_step == 0:
            tables = fft_tables(row_count, col_count)
            got, tables = lax.optimization_barrier((got, tables))
            tail = got[:, :, col_count + 2 * row_count:]
            weights = jnp.pad(tail[:, :, :2 * row_count], ((0, 0), (1, 1), (0, 0)))
            gains = jnp.pad(tail[:, :, 2 * row_count:], ((0, 0), (1, 1), (0, 0)))
            my_weights = lax.dynamic_index_in_dim(weights, side_place + 1, 1, False)
            my_weights = my_weights.reshape(roll_count, 2, row_count)
            my_gains = lax.dynamic_index_in_dim(gains, side_place + 1, 1, False)
        head = got[:, :, :col_count + 2 * row_count]
        mine = sum(jnp.where(side_place == n, head[:, n], 0.0) for n in range(side_count))
        from_left = sum(jnp.where(side_place - 1 == n, head[:, n], 0.0) for n in range(side_count))
        from_right = sum(jnp.where(side_place + 1 == n, head[:, n], 0.0) for n in range(side_count))
        near_left = from_left[:, col_count + row_count:]
        near_right = from_right[:, col_count:col_count + row_count]
        outflows = mine[:, :col_count]
        fixes = jnp.sum(my_weights * jnp.stack([near_left, near_right], axis=1), axis=2)
        outflows = jnp.where(col == 0, outflows + fixes[:, 0:1], outflows)
        outflows = jnp.where(col == col_count - 1, outflows + fixes[:, 1:2], outflows)
        carry = jnp.zeros((col_count,), jnp.float32)
        for m in range(roll_count):
            carry = jnp.where(m < roll_place, outflows[m] + my_gains[m] * carry, carry)
        line_local = mm("im,mc->ic", block_inverse, right_side)
        own_left = lax.dynamic_index_in_dim(near_left, roll_place, 0, False)
        own_right = lax.dynamic_index_in_dim(near_right, roll_place, 0, False)
        edge_fix = mm("eim,em->ie", edge_inverse, jnp.stack([own_left, own_right]))
        line_local = jnp.where(col == 0, line_local + edge_fix[:, 0:1], line_local)
        line_local = jnp.where(col == col_count - 1, line_local + edge_fix[:, 1:2], line_local)
        solved = line_local + first * (lower * carry)[None, :]
        pressure_now = jnp.where(mask_on, jnp.maximum(solved, 0.0), solved)
    return pressure_now, tables


def deflection_of(pressure_now, tables):
    row_count, col_count = pressure_now.shape
    roll_count = lax.axis_size("roll")
    side_count = lax.axis_size("side")
    devices = roll_count * side_count
    col_table = tables["col_table"]
    all_slots = col_table.shape[1]
    slots = all_slots // devices
    part = fm("rvj,ij->rvi", col_table, pressure_now)
    sent = jnp.transpose(part.reshape(2, devices, slots, row_count), (1, 0, 2, 3))
    got = lax.all_to_all(sent, ("roll", "side"), 0, 0, tiled=True)
    got = got.reshape(roll_count, side_count, 2, slots, row_count).sum(axis=1)
    spread = fm("uRra,arvb->vuRb", tables["g1"], got)
    tw_re, tw_im = tables["tw_re"], tables["tw_im"]
    a_re, a_im = spread[:, :, 0], spread[:, :, 1]
    spread = jnp.stack([a_re * tw_re - a_im * tw_im, a_re * tw_im + a_im * tw_re], axis=2)
    wave = fm("vuRb,RbSw->vuSw", spread, tables["g2"]) * tables["kernel"]
    spread = fm("vuSw,SwRb->vuRb", wave, tables["g2_back"])
    b_re, b_im = spread[:, :, 0], spread[:, :, 1]
    spread = jnp.stack([b_re * tw_re + b_im * tw_im, b_im * tw_re - b_re * tw_im], axis=2)
    back = fm("RaUS,vUSb->aRvb", tables["g1_back"], spread)
    back = jnp.broadcast_to(back[:, None], (roll_count, side_count, 2, slots, row_count))
    back = back.reshape(devices, 2, slots, row_count)
    home = lax.all_to_all(back, ("roll", "side"), 0, 0, tiled=True)
    home = jnp.transpose(home, (1, 0, 2, 3)).reshape(2, all_slots, row_count)
    return fm("rvi,rvj->ij", home, col_table)


def per_device(
    pressure,
    source,
    side_coupling,
    block_inverse,
    lower_coupling,
    cavity_mask,
    rough_code,
    film_offset,
):
    row_count, col_count = pressure.shape
    roll_count = lax.axis_size("roll")
    side_count = lax.axis_size("side")
    roll_place = lax.axis_index("roll")
    side_place = lax.axis_index("side")
    pressure_now, tables = relax(
        pressure, source, side_coupling, block_inverse, lower_coupling, cavity_mask
    )
    deflection = deflection_of(pressure_now, tables)
    row_pos = (roll_place * row_count + counting(row_count)).astype(jnp.float32)
    col_pos = (side_place * col_count + counting(col_count)).astype(jnp.float32)
    across = 4.0 * (row_pos + 0.5) / (row_count * roll_count) - 2.5
    transverse = 4.0 * (col_pos + 0.5) / (col_count * side_count) - 2.0
    film_height = (
        film_offset[0]
        + 0.5 * across[:, None] * across[:, None]
        + 0.5 * transverse[None, :] * transverse[None, :]
        + deflection
        - ROUGH_STEP * rough_code.astype(jnp.float32)
    )
    return (pressure_now, film_height)


def solution(mesh):
    return jax.shard_map(
        per_device,
        mesh=mesh,
        in_specs=(
            P("roll", "side"),
            P("roll", "side"),
            P("roll", "side"),
            P("roll", "side"),
            P("roll", "side"),
            P("roll", "side"),
            P("roll", "side"),
            P(),
        ),
        out_specs=(P("roll", "side"), P("roll", "side")),
        check_vma=False,
    )
```

```python
import math

import jax
import jax.numpy as jnp
from jax import lax
from jax.sharding import PartitionSpec as P

SWEEPS = 4


HIGHEST = lax.Precision.HIGHEST
TWO_PI = 2.0 * math.pi
ROUGH_STEP = 0.05


def counting(length):
    return jnp.arange(length, dtype=jnp.int32)


def phase_pair(first_ints, second_ints, length, sign_value):
    angles = (first_ints * second_ints % length).astype(jnp.float32) * (TWO_PI / length)
    return (jnp.cos(angles), sign_value * jnp.sin(angles))


def mm(formula, left, right, precision=HIGHEST):
    return jnp.einsum(formula, left, right, precision=precision, preferred_element_type=jnp.float32)


def fm(formula, left, right):
    return mm(formula, left, right, lax.Precision.HIGH)


def col_tables(col_count, side_place, fft_cols, all_slots):
    split = 16 if col_count % 16 == 0 else 1
    freq = counting(all_slots)
    high = side_place * col_count + split * counting(col_count // split)
    high_re, high_im = phase_pair(high[:, None], freq[None, :], fft_cols, -1.0)
    low_re, low_im = phase_pair(counting(split)[:, None], freq[None, :], fft_cols, -1.0)
    cos_t = high_re[:, None, :] * low_re[None] - high_im[:, None, :] * low_im[None]
    sin_t = high_re[:, None, :] * low_im[None] + high_im[:, None, :] * low_re[None]
    table = jnp.stack([cos_t.reshape(col_count, all_slots), sin_t.reshape(col_count, all_slots)])
    return jnp.transpose(table, (0, 2, 1))


def complex_block(f_re, f_im):
    return jnp.stack([jnp.stack([f_re, -f_im]), jnp.stack([f_im, f_re])])


def fft_tables(row_count, col_count):
    roll_count = lax.axis_size("roll")
    side_count = lax.axis_size("side")
    side_place = lax.axis_index("side")
    devices = roll_count * side_count
    fft_rows = 2 * row_count * roll_count
    fft_cols = 2 * col_count * side_count
    half_cols = fft_cols // 2
    slots = -(-(half_cols + 1) // devices)
    all_slots = devices * slots
    first_len = fft_rows // row_count
    place_index = counting(roll_count)
    first_index = counting(first_len)
    inner_index = counting(row_count)
    col_table = col_tables(col_count, side_place, fft_cols, all_slots)
    f1_re, f1_im = phase_pair(first_index[:, None], place_index[None, :], first_len, -1.0)
    g1 = jnp.transpose(complex_block(f1_re, f1_im), (2, 0, 1, 3))
    g1_back = jnp.transpose(complex_block(f1_re, -f1_im), (0, 3, 2, 1))
    tw_re, tw_im = phase_pair(first_index[:, None], inner_index[None, :], fft_rows, -1.0)
    f2_re, f2_im = phase_pair(inner_index[:, None], inner_index[None, :], row_count, -1.0)
    g2 = jnp.transpose(complex_block(f2_re, f2_im), (1, 2, 0, 3))
    g2_back = jnp.transpose(complex_block(f2_re, -f2_im), (1, 3, 0, 2))
    my_device = lax.axis_index("roll") * side_count + side_place
    my_freq = my_device * slots + counting(slots)
    row_freq = first_index[:, None] + first_len * inner_index[None, :]
    row_wave = jnp.minimum(row_freq, fft_rows - row_freq).astype(jnp.float32) / fft_rows
    col_wave = jnp.minimum(my_freq, fft_cols - my_freq).astype(jnp.float32) / fft_cols
    kernel_reach = min(fft_rows, fft_cols) / 16.0
    radius = jnp.sqrt(
        row_wave[None] * row_wave[None] + col_wave[:, None, None] * col_wave[:, None, None]
    )
    weight = jnp.where(
        my_freq > half_cols, 0.0, jnp.where((my_freq == 0) | (my_freq == half_cols), 1.0, 2.0)
    )
    kernel = (0.4 * kernel_reach / (1.0 + kernel_reach * radius)) * (
        weight[:, None, None] / (float(fft_rows) * float(fft_cols))
    )
    return dict(
        col_table=col_table, g1=g1, g1_back=g1_back, tw_re=tw_re, tw_im=tw_im,
        g2=g2, g2_back=g2_back, kernel=kernel[:, :, None, :],
    )


def relax(pressure, source, side_coupling, block_inverse, lower_coupling, cavity_mask):
    row_count, col_count = pressure.shape
    roll_count = lax.axis_size("roll")
    side_count = lax.axis_size("side")
    roll_place = lax.axis_index("roll")
    side_place = lax.axis_index("side")
    devices = roll_count * side_count
    last = row_count - 1
    mask_on = (cavity_mask[0] == 1)[None, :]
    lower = lower_coupling[0]
    first = block_inverse[:, 0:1]
    first_edges = jnp.stack(
        [pressure[:, 0], pressure[:, col_count - 1], side_coupling[:, 0],
         side_coupling[:, col_count - 1]]
    )
    edge_coupling = first_edges[2:]
    last_row = lax.optimization_barrier(block_inverse[last])
    edge_weight = last_row[None, :] * edge_coupling
    edge_inverse = block_inverse[None, :, :] * edge_coupling[:, None, :]
    gain = last_row[0] * lower
    col = counting(col_count)[None, :]
    pressure_now = pressure
    for sweep_step in range(SWEEPS):
        padded = jnp.pad(pressure_now, ((0, 0), (1, 1)))
        right_side = source + side_coupling * (padded[:, :-2] + padded[:, 2:])
        outflow = mm("m,mc->c", last_row, right_side)
        if sweep_step == 0:
            edges = first_edges[:2].reshape(-1)
        else:
            edges = jnp.stack([pressure_now[:, 0], pressure_now[:, col_count - 1]]).reshape(-1)
        parts = [outflow, edges]
        if sweep_step == 0:
            parts += [edge_weight.reshape(-1), gain]
        sent = jnp.concatenate(
            [jnp.broadcast_to(piece[None], (devices, piece.shape[0])) for piece in parts], axis=1
        )
        got = lax.all_to_all(sent, ("roll", "side"), 0, 0, tiled=True)
        got = got.reshape(roll_count, side_count, sent.shape[1])
        if sweep_step == 0:
            tables = fft_tables(row_count, col_count)
            got, tables = lax.optimization_barrier((got, tables))
            tail = got[:, :, col_count + 2 * row_count:]
            tail = sum(jnp.where(side_place == n, tail[:, n], 0.0) for n in range(side_count))
            my_weights = tail[:, :2 * row_count].reshape(roll_count, 2, row_count)
            my_gains = tail[:, 2 * row_count:]
        head = got[:, :, :col_count + 2 * row_count]
        mine = sum(jnp.where(side_place == n, head[:, n], 0.0) for n in range(side_count))
        from_left = sum(jnp.where(side_place - 1 == n, head[:, n], 0.0) for n in range(side_count))
        from_right = sum(jnp.where(side_place + 1 == n, head[:, n], 0.0) for n in range(side_count))
        near_left = from_left[:, col_count + row_count:]
        near_right = from_right[:, col_count:col_count + row_count]
        outflows = mine[:, :col_count]
        fixes = jnp.sum(my_weights * jnp.stack([near_left, near_right], axis=1), axis=2)
        outflows = jnp.where(col == 0, outflows + fixes[:, 0:1], outflows)
        outflows = jnp.where(col == col_count - 1, outflows + fixes[:, 1:2], outflows)
        carry = jnp.zeros((col_count,), jnp.float32)
        for m in range(roll_count):
            carry = jnp.where(m < roll_place, outflows[m] + my_gains[m] * carry, carry)
        line_local = mm("im,mc->ic", block_inverse, right_side)
        own_left = lax.dynamic_index_in_dim(near_left, roll_place, 0, False)
        own_right = lax.dynamic_index_in_dim(near_right, roll_place, 0, False)
        edge_fix = mm("eim,em->ie", edge_inverse, jnp.stack([own_left, own_right]))
        line_local = jnp.where(col == 0, line_local + edge_fix[:, 0:1], line_local)
        line_local = jnp.where(col == col_count - 1, line_local + edge_fix[:, 1:2], line_local)
        solved = line_local + first * (lower * carry)[None, :]
        pressure_now = jnp.where(mask_on, jnp.maximum(solved, 0.0), solved)
    return pressure_now, tables


def deflection_of(pressure_now, tables):
    row_count, col_count = pressure_now.shape
    roll_count = lax.axis_size("roll")
    side_count = lax.axis_size("side")
    devices = roll_count * side_count
    col_table = tables["col_table"]
    all_slots = col_table.shape[1]
    slots = all_slots // devices
    part = fm("rvj,ij->rvi", col_table, pressure_now)
    sent = jnp.transpose(part.reshape(2, devices, slots, row_count), (1, 0, 2, 3))
    got = lax.all_to_all(sent, ("roll", "side"), 0, 0, tiled=True)
    got = got.reshape(roll_count, side_count, 2, slots, row_count).sum(axis=1)
    spread = fm("uRra,arvb->vuRb", tables["g1"], got)
    tw_re, tw_im = tables["tw_re"], tables["tw_im"]
    a_re, a_im = spread[:, :, 0], spread[:, :, 1]
    spread = jnp.stack([a_re * tw_re - a_im * tw_im, a_re * tw_im + a_im * tw_re], axis=2)
    wave = fm("vuRb,RbSw->vuSw", spread, tables["g2"]) * tables["kernel"]
    spread = fm("vuSw,SwRb->vuRb", wave, tables["g2_back"])
    b_re, b_im = spread[:, :, 0], spread[:, :, 1]
    spread = jnp.stack([b_re * tw_re + b_im * tw_im, b_im * tw_re - b_re * tw_im], axis=2)
    back = fm("RaUS,vUSb->aRvb", tables["g1_back"], spread)
    back = jnp.broadcast_to(back[:, None], (roll_count, side_count, 2, slots, row_count))
    back = back.reshape(devices, 2, slots, row_count)
    home = lax.all_to_all(back, ("roll", "side"), 0, 0, tiled=True)
    home = jnp.transpose(home, (1, 0, 2, 3)).reshape(2, all_slots, row_count)
    return fm("rvi,rvj->ij", home, col_table)


def per_device(
    pressure,
    source,
    side_coupling,
    block_inverse,
    lower_coupling,
    cavity_mask,
    rough_code,
    film_offset,
):
    row_count, col_count = pressure.shape
    roll_count = lax.axis_size("roll")
    side_count = lax.axis_size("side")
    roll_place = lax.axis_index("roll")
    side_place = lax.axis_index("side")
    pressure_now, tables = relax(
        pressure, source, side_coupling, block_inverse, lower_coupling, cavity_mask
    )
    deflection = deflection_of(pressure_now, tables)
    row_pos = (roll_place * row_count + counting(row_count)).astype(jnp.float32)
    col_pos = (side_place * col_count + counting(col_count)).astype(jnp.float32)
    across = 4.0 * (row_pos + 0.5) / (row_count * roll_count) - 2.5
    transverse = 4.0 * (col_pos + 0.5) / (col_count * side_count) - 2.0
    film_height = (
        film_offset[0]
        + 0.5 * across[:, None] * across[:, None]
        + 0.5 * transverse[None, :] * transverse[None, :]
        + deflection
        - ROUGH_STEP * rough_code.astype(jnp.float32)
    )
    return (pressure_now, film_height)


def solution(mesh):
    return jax.shard_map(
        per_device,
        mesh=mesh,
        in_specs=(
            P("roll", "side"),
            P("roll", "side"),
            P("roll", "side"),
            P("roll", "side"),
            P("roll", "side"),
            P("roll", "side"),
            P("roll", "side"),
            P(),
        ),
        out_specs=(P("roll", "side"), P("roll", "side")),
        check_vma=False,
    )
```

```python
import math

import jax
import jax.numpy as jnp
from jax import lax
from jax.sharding import PartitionSpec as P

SWEEPS = 4


HIGHEST = lax.Precision.HIGHEST
TWO_PI = 2.0 * math.pi
ROUGH_STEP = 0.05


def counting(length):
    return jnp.arange(length, dtype=jnp.int32)


def phase_pair(first_ints, second_ints, length, sign_value):
    angles = (first_ints * second_ints % length).astype(jnp.float32) * (TWO_PI / length)
    return (jnp.cos(angles), sign_value * jnp.sin(angles))


def mm(formula, left, right, precision=HIGHEST):
    return jnp.einsum(formula, left, right, precision=precision, preferred_element_type=jnp.float32)


def fm(formula, left, right):
    return mm(formula, left, right, lax.Precision.HIGH)


def col_tables(col_count, side_place, fft_cols, all_slots):
    split = 16 if col_count % 16 == 0 else 1
    freq = counting(all_slots)
    high = side_place * col_count + split * counting(col_count // split)
    high_re, high_im = phase_pair(high[:, None], freq[None, :], fft_cols, -1.0)
    low_re, low_im = phase_pair(counting(split)[:, None], freq[None, :], fft_cols, -1.0)
    cos_t = high_re[:, None, :] * low_re[None] - high_im[:, None, :] * low_im[None]
    sin_t = high_re[:, None, :] * low_im[None] + high_im[:, None, :] * low_re[None]
    table = jnp.stack([cos_t.reshape(col_count, all_slots), sin_t.reshape(col_count, all_slots)])
    return jnp.transpose(table, (0, 2, 1))


def complex_block(f_re, f_im):
    return jnp.stack([jnp.stack([f_re, -f_im]), jnp.stack([f_im, f_re])])


def fft_tables(row_count, col_count):
    roll_count = lax.axis_size("roll")
    side_count = lax.axis_size("side")
    side_place = lax.axis_index("side")
    devices = roll_count * side_count
    fft_rows = 2 * row_count * roll_count
    fft_cols = 2 * col_count * side_count
    half_cols = fft_cols // 2
    slots = -(-(half_cols + 1) // devices)
    all_slots = devices * slots
    first_len = fft_rows // row_count
    place_index = counting(roll_count)
    first_index = counting(first_len)
    inner_index = counting(row_count)
    col_table = col_tables(col_count, side_place, fft_cols, all_slots)
    f1_re, f1_im = phase_pair(first_index[:, None], place_index[None, :], first_len, -1.0)
    g1 = jnp.transpose(complex_block(f1_re, f1_im), (2, 0, 1, 3))
    g1_back = jnp.transpose(complex_block(f1_re, -f1_im), (0, 3, 2, 1))
    tw_re, tw_im = phase_pair(first_index[:, None], inner_index[None, :], fft_rows, -1.0)
    f2_re, f2_im = phase_pair(inner_index[:, None], inner_index[None, :], row_count, -1.0)
    g2 = jnp.transpose(complex_block(f2_re, f2_im), (1, 2, 0, 3))
    g2_back = jnp.transpose(complex_block(f2_re, -f2_im), (1, 3, 0, 2))
    my_device = lax.axis_index("roll") * side_count + side_place
    my_freq = my_device * slots + counting(slots)
    row_freq = first_index[:, None] + first_len * inner_index[None, :]
    row_wave = jnp.minimum(row_freq, fft_rows - row_freq).astype(jnp.float32) / fft_rows
    col_wave = jnp.minimum(my_freq, fft_cols - my_freq).astype(jnp.float32) / fft_cols
    kernel_reach = min(fft_rows, fft_cols) / 16.0
    radius = jnp.sqrt(
        row_wave[None] * row_wave[None] + col_wave[:, None, None] * col_wave[:, None, None]
    )
    weight = jnp.where(
        my_freq > half_cols, 0.0, jnp.where((my_freq == 0) | (my_freq == half_cols), 1.0, 2.0)
    )
    kernel = (0.4 * kernel_reach / (1.0 + kernel_reach * radius)) * (
        weight[:, None, None] / (float(fft_rows) * float(fft_cols))
    )
    return dict(
        col_table=col_table, g1=g1, g1_back=g1_back, tw_re=tw_re, tw_im=tw_im,
        g2=g2, g2_back=g2_back, kernel=kernel[:, :, None, :],
    )


def relax(pressure, source, side_coupling, block_inverse, lower_coupling, cavity_mask):
    row_count, col_count = pressure.shape
    roll_count = lax.axis_size("roll")
    side_count = lax.axis_size("side")
    roll_place = lax.axis_index("roll")
    side_place = lax.axis_index("side")
    devices = roll_count * side_count
    last = row_count - 1
    mask_on = (cavity_mask[0] == 1)[None, :]
    lower = lower_coupling[0]
    first = block_inverse[:, 0:1]
    first_edges = jnp.stack(
        [pressure[:, 0], pressure[:, col_count - 1], side_coupling[:, 0],
         side_coupling[:, col_count - 1]]
    )
    edge_coupling = first_edges[2:]
    last_row = lax.optimization_barrier(block_inverse[last])
    edge_weight = last_row[None, :] * edge_coupling
    edge_inverse = block_inverse[None, :, :] * edge_coupling[:, None, :]
    gain = last_row[0] * lower
    col = counting(col_count)[None, :]
    pressure_now = pressure
    for sweep_step in range(SWEEPS):
        padded = jnp.pad(pressure_now, ((0, 0), (1, 1)))
        right_side = source + side_coupling * (padded[:, :-2] + padded[:, 2:])
        outflow = mm("m,mc->c", last_row, right_side)
        if sweep_step == 0:
            edges = first_edges[:2].reshape(-1)
        else:
            edges = jnp.stack([pressure_now[:, 0], pressure_now[:, col_count - 1]]).reshape(-1)
        parts = [outflow, edges]
        if sweep_step == 0:
            parts += [edge_weight.reshape(-1), gain]
        sent = jnp.concatenate(
            [jnp.broadcast_to(piece[None], (devices, piece.shape[0])) for piece in parts], axis=1
        )
        got = lax.all_to_all(sent, ("roll", "side"), 0, 0, tiled=True)
        got = got.reshape(roll_count, side_count, sent.shape[1])
        if sweep_step == 0:
            tables = fft_tables(row_count, col_count)
            got, tables = lax.optimization_barrier((got, tables))
            tail = got[:, :, col_count + 2 * row_count:]
            tail = sum(jnp.where(side_place == n, tail[:, n], 0.0) for n in range(side_count))
            my_weights = tail[:, :2 * row_count].reshape(roll_count, 2, row_count)
            my_gains = tail[:, 2 * row_count:]
        head = got[:, :, :col_count + 2 * row_count]
        mine = sum(jnp.where(side_place == n, head[:, n], 0.0) for n in range(side_count))
        from_left = sum(jnp.where(side_place - 1 == n, head[:, n], 0.0) for n in range(side_count))
        from_right = sum(jnp.where(side_place + 1 == n, head[:, n], 0.0) for n in range(side_count))
        near_left = from_left[:, col_count + row_count:]
        near_right = from_right[:, col_count:col_count + row_count]
        outflows = mine[:, :col_count]
        fixes = jnp.sum(my_weights * jnp.stack([near_left, near_right], axis=1), axis=2)
        outflows = jnp.where(col == 0, outflows + fixes[:, 0:1], outflows)
        outflows = jnp.where(col == col_count - 1, outflows + fixes[:, 1:2], outflows)
        carry = jnp.zeros((col_count,), jnp.float32)
        for m in range(roll_count):
            carry = jnp.where(m < roll_place, outflows[m] + my_gains[m] * carry, carry)
        line_local = mm("im,mc->ic", block_inverse, right_side)
        own_rows = (counting(roll_count) == roll_place)[:, None]
        own_left = jnp.sum(jnp.where(own_rows, near_left, 0.0), axis=0)
        own_right = jnp.sum(jnp.where(own_rows, near_right, 0.0), axis=0)
        edge_fix = mm("eim,em->ie", edge_inverse, jnp.stack([own_left, own_right]))
        line_local = jnp.where(col == 0, line_local + edge_fix[:, 0:1], line_local)
        line_local = jnp.where(col == col_count - 1, line_local + edge_fix[:, 1:2], line_local)
        solved = line_local + first * (lower * carry)[None, :]
        pressure_now = jnp.where(mask_on, jnp.maximum(solved, 0.0), solved)
    return pressure_now, tables


def deflection_of(pressure_now, tables):
    row_count, col_count = pressure_now.shape
    roll_count = lax.axis_size("roll")
    side_count = lax.axis_size("side")
    devices = roll_count * side_count
    col_table = tables["col_table"]
    all_slots = col_table.shape[1]
    slots = all_slots // devices
    part = fm("rvj,ij->rvi", col_table, pressure_now)
    sent = jnp.transpose(part.reshape(2, devices, slots, row_count), (1, 0, 2, 3))
    got = lax.all_to_all(sent, ("roll", "side"), 0, 0, tiled=True)
    got = got.reshape(roll_count, side_count, 2, slots, row_count).sum(axis=1)
    spread = fm("uRra,arvb->vuRb", tables["g1"], got)
    tw_re, tw_im = tables["tw_re"], tables["tw_im"]
    a_re, a_im = spread[:, :, 0], spread[:, :, 1]
    spread = jnp.stack([a_re * tw_re - a_im * tw_im, a_re * tw_im + a_im * tw_re], axis=2)
    wave = fm("vuRb,RbSw->vuSw", spread, tables["g2"]) * tables["kernel"]
    spread = fm("vuSw,SwRb->vuRb", wave, tables["g2_back"])
    b_re, b_im = spread[:, :, 0], spread[:, :, 1]
    spread = jnp.stack([b_re * tw_re + b_im * tw_im, b_im * tw_re - b_re * tw_im], axis=2)
    back = fm("RaUS,vUSb->aRvb", tables["g1_back"], spread)
    back = jnp.broadcast_to(back[:, None], (roll_count, side_count, 2, slots, row_count))
    back = back.reshape(devices, 2, slots, row_count)
    home = lax.all_to_all(back, ("roll", "side"), 0, 0, tiled=True)
    home = jnp.transpose(home, (1, 0, 2, 3)).reshape(2, all_slots, row_count)
    return fm("rvi,rvj->ij", home, col_table)


def per_device(
    pressure,
    source,
    side_coupling,
    block_inverse,
    lower_coupling,
    cavity_mask,
    rough_code,
    film_offset,
):
    row_count, col_count = pressure.shape
    roll_count = lax.axis_size("roll")
    side_count = lax.axis_size("side")
    roll_place = lax.axis_index("roll")
    side_place = lax.axis_index("side")
    pressure_now, tables = relax(
        pressure, source, side_coupling, block_inverse, lower_coupling, cavity_mask
    )
    deflection = deflection_of(pressure_now, tables)
    row_pos = (roll_place * row_count + counting(row_count)).astype(jnp.float32)
    col_pos = (side_place * col_count + counting(col_count)).astype(jnp.float32)
    across = 4.0 * (row_pos + 0.5) / (row_count * roll_count) - 2.5
    transverse = 4.0 * (col_pos + 0.5) / (col_count * side_count) - 2.0
    film_height = (
        film_offset[0]
        + 0.5 * across[:, None] * across[:, None]
        + 0.5 * transverse[None, :] * transverse[None, :]
        + deflection
        - ROUGH_STEP * rough_code.astype(jnp.float32)
    )
    return (pressure_now, film_height)


def solution(mesh):
    return jax.shard_map(
        per_device,
        mesh=mesh,
        in_specs=(
            P("roll", "side"),
            P("roll", "side"),
            P("roll", "side"),
            P("roll", "side"),
            P("roll", "side"),
            P("roll", "side"),
            P("roll", "side"),
            P(),
        ),
        out_specs=(P("roll", "side"), P("roll", "side")),
        check_vma=False,
    )
```

```python
import math

import jax
import jax.numpy as jnp
from jax import lax
from jax.sharding import PartitionSpec as P

SWEEPS = 4


HIGHEST = lax.Precision.HIGHEST
TWO_PI = 2.0 * math.pi
ROUGH_STEP = 0.05


def counting(length):
    return jnp.arange(length, dtype=jnp.int32)


def phase_pair(first_ints, second_ints, length, sign_value):
    angles = (first_ints * second_ints % length).astype(jnp.float32) * (TWO_PI / length)
    return (jnp.cos(angles), sign_value * jnp.sin(angles))


def mm(formula, left, right, precision=HIGHEST):
    return jnp.einsum(formula, left, right, precision=precision, preferred_element_type=jnp.float32)


def fm(formula, left, right):
    return mm(formula, left, right, lax.Precision.HIGH)


def col_tables(col_count, side_place, fft_cols, all_slots):
    split = 16 if col_count % 16 == 0 else 1
    freq = counting(all_slots)
    high = side_place * col_count + split * counting(col_count // split)
    high_re, high_im = phase_pair(high[:, None], freq[None, :], fft_cols, -1.0)
    low_re, low_im = phase_pair(counting(split)[:, None], freq[None, :], fft_cols, -1.0)
    cos_t = high_re[:, None, :] * low_re[None] - high_im[:, None, :] * low_im[None]
    sin_t = high_re[:, None, :] * low_im[None] + high_im[:, None, :] * low_re[None]
    table = jnp.stack([cos_t.reshape(col_count, all_slots), sin_t.reshape(col_count, all_slots)])
    return jnp.transpose(table, (0, 2, 1))


def complex_block(f_re, f_im):
    return jnp.stack([jnp.stack([f_re, -f_im]), jnp.stack([f_im, f_re])])


def fft_tables(row_count, col_count):
    roll_count = lax.axis_size("roll")
    side_count = lax.axis_size("side")
    side_place = lax.axis_index("side")
    devices = roll_count * side_count
    fft_rows = 2 * row_count * roll_count
    fft_cols = 2 * col_count * side_count
    half_cols = fft_cols // 2
    slots = -(-(half_cols + 1) // devices)
    all_slots = devices * slots
    first_len = fft_rows // row_count
    place_index = counting(roll_count)
    first_index = counting(first_len)
    inner_index = counting(row_count)
    col_table = col_tables(col_count, side_place, fft_cols, all_slots)
    f1_re, f1_im = phase_pair(first_index[:, None], place_index[None, :], first_len, -1.0)
    g1 = jnp.transpose(complex_block(f1_re, f1_im), (2, 0, 1, 3))
    g1_back = jnp.transpose(complex_block(f1_re, -f1_im), (0, 3, 2, 1))
    tw_re, tw_im = phase_pair(first_index[:, None], inner_index[None, :], fft_rows, -1.0)
    f2_re, f2_im = phase_pair(inner_index[:, None], inner_index[None, :], row_count, -1.0)
    g2 = jnp.transpose(complex_block(f2_re, f2_im), (1, 2, 0, 3))
    g2_back = jnp.transpose(complex_block(f2_re, -f2_im), (1, 3, 0, 2))
    my_device = lax.axis_index("roll") * side_count + side_place
    my_freq = my_device * slots + counting(slots)
    row_freq = first_index[:, None] + first_len * inner_index[None, :]
    row_wave = jnp.minimum(row_freq, fft_rows - row_freq).astype(jnp.float32) / fft_rows
    col_wave = jnp.minimum(my_freq, fft_cols - my_freq).astype(jnp.float32) / fft_cols
    kernel_reach = min(fft_rows, fft_cols) / 16.0
    radius = jnp.sqrt(
        row_wave[None] * row_wave[None] + col_wave[:, None, None] * col_wave[:, None, None]
    )
    weight = jnp.where(
        my_freq > half_cols, 0.0, jnp.where((my_freq == 0) | (my_freq == half_cols), 1.0, 2.0)
    )
    kernel = (0.4 * kernel_reach / (1.0 + kernel_reach * radius)) * (
        weight[:, None, None] / (float(fft_rows) * float(fft_cols))
    )
    return dict(
        col_table=col_table, g1=g1, g1_back=g1_back, tw_re=tw_re, tw_im=tw_im,
        g2=g2, g2_back=g2_back, kernel=kernel[:, :, None, :],
    )


def relax(pressure, source, side_coupling, block_inverse, lower_coupling, cavity_mask):
    row_count, col_count = pressure.shape
    roll_count = lax.axis_size("roll")
    side_count = lax.axis_size("side")
    roll_place = lax.axis_index("roll")
    side_place = lax.axis_index("side")
    devices = roll_count * side_count
    last = row_count - 1
    mask_on = (cavity_mask[0] == 1)[None, :]
    lower = lower_coupling[0]
    first = block_inverse[:, 0:1]
    first_edges = jnp.stack(
        [pressure[:, 0], pressure[:, col_count - 1], side_coupling[:, 0],
         side_coupling[:, col_count - 1]]
    )
    edge_coupling = first_edges[2:]
    last_row = lax.optimization_barrier(block_inverse[last])
    edge_weight = last_row[None, :] * edge_coupling
    edge_inverse = block_inverse[None, :, :] * edge_coupling[:, None, :]
    gain = last_row[0] * lower
    col = counting(col_count)[None, :]
    pressure_now = pressure
    for sweep_step in range(SWEEPS):
        padded = jnp.pad(pressure_now, ((0, 0), (1, 1)))
        right_side = source + side_coupling * (padded[:, :-2] + padded[:, 2:])
        outflow = mm("m,mc->c", last_row, right_side)
        if sweep_step == 0:
            edges = first_edges[:2].reshape(-1)
        else:
            edges = jnp.stack([pressure_now[:, 0], pressure_now[:, col_count - 1]]).reshape(-1)
        parts = [outflow, edges]
        if sweep_step == 0:
            parts += [edge_weight.reshape(-1), gain]
        sent = jnp.concatenate(
            [jnp.broadcast_to(piece[None], (devices, piece.shape[0])) for piece in parts], axis=1
        )
        got = lax.all_to_all(sent, ("roll", "side"), 0, 0, tiled=True)
        got = got.reshape(roll_count, side_count, sent.shape[1])
        if sweep_step == 0:
            tables = fft_tables(row_count, col_count)
            got, tables = lax.optimization_barrier((got, tables))
            tail = got[:, :, col_count + 2 * row_count:]
            tail = sum(jnp.where(side_place == n, tail[:, n], 0.0) for n in range(side_count))
            my_weights = tail[:, :2 * row_count].reshape(roll_count, 2, row_count)
            my_gains = tail[:, 2 * row_count:]
        head = got[:, :, :col_count + 2 * row_count]
        mine = sum(jnp.where(side_place == n, head[:, n], 0.0) for n in range(side_count))
        from_left = sum(jnp.where(side_place - 1 == n, head[:, n], 0.0) for n in range(side_count))
        from_right = sum(jnp.where(side_place + 1 == n, head[:, n], 0.0) for n in range(side_count))
        near_left = from_left[:, col_count + row_count:]
        near_right = from_right[:, col_count:col_count + row_count]
        outflows = mine[:, :col_count]
        fixes = jnp.sum(my_weights * jnp.stack([near_left, near_right], axis=1), axis=2)
        outflows = jnp.where(col == 0, outflows + fixes[:, 0:1], outflows)
        outflows = jnp.where(col == col_count - 1, outflows + fixes[:, 1:2], outflows)
        carry = jnp.zeros((col_count,), jnp.float32)
        for m in range(roll_count):
            carry = jnp.where(m < roll_place, outflows[m] + my_gains[m] * carry, carry)
        line_local = mm("im,mc->ic", block_inverse, right_side)
        own_left = lax.dynamic_index_in_dim(near_left, roll_place, 0, False)
        own_right = lax.dynamic_index_in_dim(near_right, roll_place, 0, False)
        edge_fix = mm("eim,em->ie", edge_inverse, jnp.stack([own_left, own_right]))
        line_local = jnp.where(col == 0, line_local + edge_fix[:, 0:1], line_local)
        line_local = jnp.where(col == col_count - 1, line_local + edge_fix[:, 1:2], line_local)
        solved = line_local + first * (lower * carry)[None, :]
        pressure_now = jnp.where(mask_on, jnp.maximum(solved, 0.0), solved)
    return pressure_now, tables


def deflection_of(pressure_now, tables, base):
    row_count, col_count = pressure_now.shape
    roll_count = lax.axis_size("roll")
    side_count = lax.axis_size("side")
    devices = roll_count * side_count
    col_table = tables["col_table"]
    all_slots = col_table.shape[1]
    slots = all_slots // devices
    part = fm("rvj,ij->rvi", col_table, pressure_now)
    sent = jnp.transpose(part.reshape(2, devices, slots, row_count), (1, 0, 2, 3))
    got = lax.all_to_all(sent, ("roll", "side"), 0, 0, tiled=True)
    got = got.reshape(roll_count, side_count, 2, slots, row_count).sum(axis=1)
    spread = fm("uRra,arvb->vuRb", tables["g1"], got)
    tw_re, tw_im = tables["tw_re"], tables["tw_im"]
    a_re, a_im = spread[:, :, 0], spread[:, :, 1]
    spread = jnp.stack([a_re * tw_re - a_im * tw_im, a_re * tw_im + a_im * tw_re], axis=2)
    wave = fm("vuRb,RbSw->vuSw", spread, tables["g2"]) * tables["kernel"]
    spread = fm("vuSw,SwRb->vuRb", wave, tables["g2_back"])
    b_re, b_im = spread[:, :, 0], spread[:, :, 1]
    spread = jnp.stack([b_re * tw_re + b_im * tw_im, b_im * tw_re - b_re * tw_im], axis=2)
    back = fm("RaUS,vUSb->aRvb", tables["g1_back"], spread)
    back = jnp.broadcast_to(back[:, None], (roll_count, side_count, 2, slots, row_count))
    back = back.reshape(devices, 2, slots, row_count)
    home = lax.all_to_all(back, ("roll", "side"), 0, 0, tiled=True)
    home, base = lax.optimization_barrier((home, base))
    home = jnp.transpose(home, (1, 0, 2, 3)).reshape(2, all_slots, row_count)
    return fm("rvi,rvj->ij", home, col_table) + base


def per_device(
    pressure,
    source,
    side_coupling,
    block_inverse,
    lower_coupling,
    cavity_mask,
    rough_code,
    film_offset,
):
    row_count, col_count = pressure.shape
    roll_count = lax.axis_size("roll")
    side_count = lax.axis_size("side")
    roll_place = lax.axis_index("roll")
    side_place = lax.axis_index("side")
    pressure_now, tables = relax(
        pressure, source, side_coupling, block_inverse, lower_coupling, cavity_mask
    )
    row_pos = (roll_place * row_count + counting(row_count)).astype(jnp.float32)
    col_pos = (side_place * col_count + counting(col_count)).astype(jnp.float32)
    across = 4.0 * (row_pos + 0.5) / (row_count * roll_count) - 2.5
    transverse = 4.0 * (col_pos + 0.5) / (col_count * side_count) - 2.0
    base = (
        film_offset[0]
        + 0.5 * across[:, None] * across[:, None]
        + 0.5 * transverse[None, :] * transverse[None, :]
        - ROUGH_STEP * rough_code.astype(jnp.float32)
    )
    film_height = deflection_of(pressure_now, tables, base)
    return (pressure_now, film_height)


def solution(mesh):
    return jax.shard_map(
        per_device,
        mesh=mesh,
        in_specs=(
            P("roll", "side"),
            P("roll", "side"),
            P("roll", "side"),
            P("roll", "side"),
            P("roll", "side"),
            P("roll", "side"),
            P("roll", "side"),
            P(),
        ),
        out_specs=(P("roll", "side"), P("roll", "side")),
        check_vma=False,
    )
```
